128 devices in a mesh: row: 16 (over z_lo, y, core), col: 8 (over x, z_hi).
Axes of the slice: x: 4, y: 4, z: 4 (z_hi: 2, z_lo: 2; z = z_hi * 2 + z_lo), core: 2. Of those that a mesh axis runs over, the one named last changes fastest.
Arguments:
- frames: bfloat16 [4, 4096, 512], P(None, 'row'), may hold values from -6 to 6
- orders: int32 [2, 2], replicated, may hold values from 1 to 16
- owners: int32 [16384, 1], P(('row', 'col')), may hold values from 0 to 127; in each aligned block of 128 rows (0 to 127, 128 to 255, ...) at most 2 rows name the same one
- templates: bfloat16 [128, 512, 128], P(('row', 'col')), may hold values from -0.25 to 0.25
Outputs:
- spectrum: bfloat16 [2, 4, 4, 2048, 4096], P(None, None, None, ('row', 'col'))
- detections: bfloat16 [128, 128, 2, 16, 128], P(('row', 'col'))
The draws below stay inside these ranges and needn't reach their ends.
Inputs may be any that keep to these rules, and one draw needn't show every extreme that they name: `owners`: rows 128 * i to 128 * (i + 1) - 1 hold the tiles of the device with index i along row+col. At most 2 tiles of one device name the same owner, and some device reaches that in every draw.
All inputs are finite; a program needn't handle non-finite values.
Results may differ from the reference program's by a relative error of at most 0.0078.
Values may be sent and summed in bfloat16 or wider, within the bound.
No kernel may reach another device: no remote copies, remote signals or barrier semaphores. Data moves between devices by JAX's collectives and lax.ppermute only.
A program may use at most 128 MiB of HBM per device.

```python
import math
import jax
import jax.numpy as jnp
import numpy as np
from jax import lax

SENSORS = 4
NCH = 2048
HOPS = 4096
RADIX = 8
WHEELS = 2
ORDERS = 2
FEAT = 128
FRAME = 512
SUB = 512
COMBOS = 4
CH_DEV = 16
TILES_DEV = 128
TILES = 16384
CAP = 2
N_ROW = 16
N_COL = 8
DEVICES = 128


def with_ends(result, key, smallest, top_value):
    place = [jax.random.randint(jax.random.fold_in(key, axis), (), 0, length) for axis, length in enumerate(result.shape)]
    main_axis = result.shape.index(max(result.shape))
    beside = place[:main_axis] + [(place[main_axis] + 1) % result.shape[main_axis]] + place[main_axis + 1:]
    return result.at[tuple(place)].set(smallest).at[tuple(beside)].set(top_value)


def level_of(rng, dims, split, low, top_value):
    def one(axis_at, parts):
        draws = jax.random.uniform(jax.random.fold_in(jax.random.fold_in(rng, 6), axis_at), (parts,), jnp.float32, low / len(split), top_value / len(split))
        return jnp.repeat(jnp.exp(draws), dims[axis_at] // parts).reshape((-1,) + (1,) * (len(dims) - axis_at - 1))

    gain = one(*split[0])
    for cut in split[1:]:
        gain = gain * one(*cut)
    return gain


def assign_block(rng, own, number, rows, number_of, top, limit, slope):
    ranking = jax.random.permutation(rng, number_of)
    heavy_load, common = load_shares(number_of, rows * top, limit, slope, True), load_shares(number_of, rows * top, limit, slope, False)
    places = jnp.arange(number_of)

    def named(lengths, rotation):
        used = int((lengths > 0).sum())
        fixed = max(1, used // 4)
        moved = fixed + (places - fixed + rotation * (used - fixed)) % max(1, number_of - fixed)
        return jnp.zeros((number_of,), jnp.int32).at[ranking[jnp.where(places < fixed, places, moved)]].set(jnp.asarray(lengths, jnp.int32))

    lengths = jnp.where(number % 4 == 0, named(heavy_load, number // 4), named(common, number - number // 4 - 1))
    mixed = jax.random.permutation(jax.random.fold_in(own, 3), number_of)
    giver, taker = mixed[0:number_of // 2 * 2:2], mixed[1:number_of // 2 * 2:2]
    room = jnp.minimum(lengths[giver] - 1, limit - lengths[taker]) // 2
    room = jnp.where((giver == ranking[0]) | (taker == ranking[0]) | (lengths[taker] == 0), 0, jnp.maximum(room, 0))
    moved = jax.random.randint(jax.random.fold_in(own, 4), (number_of // 2,), 0, 1 << 20) % (room + 1)
    lengths = lengths.at[giver].add(-moved).at[taker].add(moved)
    members = jnp.searchsorted(jnp.cumsum(lengths), jnp.arange(rows * top), side="right").astype(jnp.int32)
    listing = members.reshape(top, rows).T
    listing = listing[jax.random.permutation(jax.random.fold_in(own, 1), rows)]
    rotation = jax.random.randint(jax.random.fold_in(own, 2), (rows, 1), 0, top)
    return jnp.take_along_axis(listing, (jnp.arange(top)[None, :] + rotation) % top, axis=1)


def load_shares(amount, total, bound, lean, full):
    loads = [(1 << 20) // math.isqrt(grade ** lean) + 1 for grade in range(1, amount + 1)]
    largest = bound if full else min(bound, max(-(-total // amount), total * loads[0] // sum(loads)))
    least = 1 if total - largest >= amount - 1 else 0
    holding, surplus = [largest] + [least] * (amount - 1), total - largest - least * (amount - 1)
    while surplus > 0:
        candidates = [i for i in range(1, amount) if holding[i] < largest] or [i for i in range(1, amount) if holding[i] < bound]
        pool, remaining = sum([loads[i] for i in candidates]), surplus
        for i in candidates:
            more = min(bound - holding[i], max(1, remaining * loads[i] // pool), surplus)
            holding[i] = holding[i] + more
            surplus = surplus - more
    return np.array(holding)


def scatter_about(key, extent, width, limit, shards=(), kind=jnp.bfloat16):
    entries = width * jax.random.normal(key, extent, jnp.float32)
    if shards:
        entries = entries * level_of(key, extent, shards, -0.22, 0.18)
    return jnp.clip(entries, -limit, limit).astype(kind)


def setup_inputs(seed: int = 0) -> dict:
    keys = jax.random.split(jax.random.key(seed), 5)
    frames = scatter_about(keys[0], (SENSORS, HOPS, FRAME), 1.0, 6.0, ((1, 16),))
    orders = with_ends(jax.random.randint(keys[1], (WHEELS, ORDERS), 1, CH_DEV + 1), jax.random.fold_in(keys[1], 1), 1, CH_DEV).astype(jnp.int32)
    owners_keys = jax.random.split(jax.random.fold_in(keys[2], 1), TILES // TILES_DEV)
    owners_turns = jax.random.permutation(jax.random.fold_in(keys[2], 3), TILES // TILES_DEV)
    owners = jax.vmap(lambda own, number: assign_block(jax.random.fold_in(keys[2], 2), own, number, TILES_DEV, DEVICES, 1, CAP, 2))(owners_keys, owners_turns).reshape((TILES, 1))
    templates = scatter_about(keys[3], (DEVICES, SUB, FEAT), SUB ** -0.5, 0.25, ((0, 128),))
    return {"frames": frames, "orders": orders, "owners": owners, "templates": templates}


def channel_coefficients(n_total, channel_ids):
    position = jnp.arange(n_total, dtype=jnp.int32)
    turns = position[:, None] * channel_ids[None, :] % n_total
    phase_angle = 2.0 * math.pi / n_total * turns.astype(jnp.float32)
    window = 0.5 - 0.5 * jnp.cos(2.0 * math.pi / n_total * position.astype(jnp.float32))
    gain_factor = math.sqrt(8.0 / (3.0 * n_total))
    weighted = gain_factor * window[:, None]
    both = jnp.concatenate([weighted * jnp.cos(phase_angle), weighted * jnp.sin(phase_angle)], axis=1)
    return both.astype(jnp.bfloat16)

def sub_coefficients(sub_total):
    index_a = jnp.arange(sub_total, dtype=jnp.int32)
    turns = index_a[:, None] * index_a[None, :] % sub_total
    phase_angle = 2.0 * math.pi / sub_total * turns.astype(jnp.float32)
    return jnp.concatenate([jnp.cos(phase_angle), jnp.sin(phase_angle)], axis=1).astype(jnp.bfloat16)

def quarter_turn(a_cos, a_sin, channel_ids, hop_ids):
    phase_step = channel_ids[:, None] % 4 * (hop_ids[None, :] % 4) % 4
    cos_quarter = (phase_step == 0).astype(jnp.float32) - (phase_step == 2).astype(jnp.float32)
    sin_quarter = (phase_step == 1).astype(jnp.float32) - (phase_step == 3).astype(jnp.float32)
    real_part = a_cos * cos_quarter - a_sin * sin_quarter
    imag_part = -a_sin * cos_quarter - a_cos * sin_quarter
    return (real_part, imag_part)

def finish_transform(first_real, first_imag, hops_total):
    radix_count = first_real.shape[-2]
    sub_total = first_real.shape[-1]
    index_b = jnp.arange(radix_count, dtype=jnp.int32)[:, None]
    index_p = jnp.arange(sub_total, dtype=jnp.int32)[None, :]
    twist_angle = 2.0 * math.pi / hops_total * (index_b * index_p % hops_total).astype(jnp.float32)
    twist_cos = jnp.cos(twist_angle)
    twist_sin = jnp.sin(twist_angle)
    twist_real = first_real * twist_cos + first_imag * twist_sin
    twist_imag = first_imag * twist_cos - first_real * twist_sin
    index_d = jnp.arange(radix_count, dtype=jnp.int32)[None, :]
    section_angle = 2.0 * math.pi / radix_count * (index_b * index_d % radix_count).astype(jnp.float32)
    section_cos = jnp.cos(section_angle)
    section_sin = jnp.sin(section_angle)
    highest = lax.Precision.HIGHEST
    norm_factor = 1.0 / math.sqrt(hops_total)
    out_real = norm_factor * (jnp.einsum('...bq,bd->...dq', twist_real, section_cos, precision=highest) + jnp.einsum('...bq,bd->...dq', twist_imag, section_sin, precision=highest))
    out_imag = norm_factor * (jnp.einsum('...bq,bd->...dq', twist_imag, section_cos, precision=highest) - jnp.einsum('...bq,bd->...dq', twist_real, section_sin, precision=highest))
    return (out_real, out_imag)

def reference(frames, orders, owners, templates):
    devices_n = N_ROW * N_COL
    every_channel = jnp.arange(NCH, dtype=jnp.int32)
    coefficients = channel_coefficients(NCH, every_channel)
    table_sub = sub_coefficients(SUB)
    cos_sub = table_sub[:, :SUB].astype(jnp.float32)
    sin_sub = table_sub[:, SUB:].astype(jnp.float32)
    hop_ids = jnp.arange(HOPS, dtype=jnp.int32)
    spectra = []
    features = []
    for sensor in range(SENSORS):
        padded = jnp.concatenate([frames[sensor], jnp.zeros((3, FRAME), frames.dtype)], axis=0)
        summed = jnp.zeros((2 * NCH, HOPS), jnp.float32)
        for quarter in range(4):
            summed = summed + jnp.einsum('hf,fk->kh', padded[quarter:quarter + HOPS].astype(jnp.float32), coefficients[quarter * FRAME:(quarter + 1) * FRAME].astype(jnp.float32))
        real_part, imag_part = quarter_turn(summed[:NCH], summed[NCH:], every_channel, hop_ids)
        demod = jnp.stack([real_part, imag_part]).astype(jnp.bfloat16)
        own_real = demod[0].astype(jnp.float32)
        own_imag = demod[1].astype(jnp.float32)
        prod_real = []
        prod_imag = []
        for wheel in range(WHEELS):
            for order_at in range(ORDERS):
                partner = jnp.roll(demod, -orders[wheel, order_at], axis=1).astype(jnp.float32)
                prod_real.append(own_real * partner[0] + own_imag * partner[1])
                prod_imag.append(own_imag * partner[0] - own_real * partner[1])
        products = jnp.stack([jnp.stack(prod_real), jnp.stack(prod_imag)]).astype(jnp.bfloat16)
        grid = products.astype(jnp.float32).reshape(2, COMBOS, NCH, SUB, RADIX)
        first_real = jnp.einsum('ckab,aq->ckbq', grid[0], cos_sub) + jnp.einsum('ckab,aq->ckbq', grid[1], sin_sub)
        first_imag = jnp.einsum('ckab,aq->ckbq', grid[1], cos_sub) - jnp.einsum('ckab,aq->ckbq', grid[0], sin_sub)
        out_real, out_imag = finish_transform(first_real, first_imag, HOPS)
        spectra.append(jnp.stack([out_real, out_imag]).reshape(2, COMBOS, NCH, HOPS).astype(jnp.bfloat16))
        features.append(jnp.log1p(out_real * out_real + out_imag * out_imag).astype(jnp.bfloat16))
    spectrum = jnp.stack(spectra, axis=1)
    feature = jnp.stack(features)
    tiles = feature.reshape(SENSORS, COMBOS, devices_n, CH_DEV, RADIX, SUB)
    tiles = tiles.transpose(2, 0, 1, 4, 3, 5).reshape(devices_n, TILES_DEV, CH_DEV, SUB)
    owner_ids = owners[:, 0].reshape(devices_n, TILES_DEV)

    def score_block(block):
        block_tiles, block_owners = block
        return jnp.einsum('tkq,tqf->tkf', block_tiles.astype(jnp.float32), templates[block_owners].astype(jnp.float32)).astype(jnp.bfloat16)
    scores = lax.map(score_block, (tiles, owner_ids))
    targets = jnp.arange(devices_n, dtype=jnp.int32)
    one_hot = (owner_ids[:, :, None] == targets[None, None, :]).astype(jnp.int32)
    before = jnp.cumsum(one_hot, axis=1) - one_hot
    slot_ids = lax.optimization_barrier(jnp.sum(before * one_hot, axis=2)).astype(jnp.int32)
    sources = jnp.broadcast_to(targets[:, None], owner_ids.shape)
    detections = jnp.zeros((devices_n, devices_n, CAP, CH_DEV, FEAT), jnp.bfloat16)
    detections = detections.at[owner_ids, sources, slot_ids].set(scores)
    return (spectrum, detections)
```

```python
import math

import jax
import jax.numpy as jnp
from jax import lax
from jax.sharding import PartitionSpec as P

RADIX = 8


def from_behind(block, axis, distance):
    devices = range(lax.axis_size(axis))
    route = [(i - distance, i) for i in devices if i - distance in devices]
    return lax.ppermute(block, axis, route)


def from_behind_2(value, axis, steps):
    count = lax.axis_size(axis)
    pairs = [(source, (source + steps) % count) for source in range(count)]
    return lax.ppermute(value, axis, pairs)


def channel_coefficients(n_total, channel_ids):
    position = jnp.arange(n_total, dtype=jnp.int32)
    turns = position[:, None] * channel_ids[None, :] % n_total
    phase_angle = 2.0 * math.pi / n_total * turns.astype(jnp.float32)
    window = 0.5 - 0.5 * jnp.cos(2.0 * math.pi / n_total * position.astype(jnp.float32))
    gain_factor = math.sqrt(8.0 / (3.0 * n_total))
    weighted = gain_factor * window[:, None]
    both = jnp.concatenate(
        [weighted * jnp.cos(phase_angle), weighted * jnp.sin(phase_angle)], axis=1
    )
    return both.astype(jnp.bfloat16)


def sub_coefficients(sub_total):
    index_a = jnp.arange(sub_total, dtype=jnp.int32)
    turns = index_a[:, None] * index_a[None, :] % sub_total
    phase_angle = 2.0 * math.pi / sub_total * turns.astype(jnp.float32)
    return jnp.concatenate([jnp.cos(phase_angle), jnp.sin(phase_angle)], axis=1).astype(
        jnp.bfloat16
    )


def quarter_turn(a_cos, a_sin, channel_ids, hop_ids):
    phase_step = channel_ids[:, None] % 4 * (hop_ids[None, :] % 4) % 4
    cos_quarter = (phase_step == 0).astype(jnp.float32) - (phase_step == 2).astype(jnp.float32)
    sin_quarter = (phase_step == 1).astype(jnp.float32) - (phase_step == 3).astype(jnp.float32)
    real_part = a_cos * cos_quarter - a_sin * sin_quarter
    imag_part = -a_sin * cos_quarter - a_cos * sin_quarter
    return (real_part, imag_part)


def finish_transform(first_real, first_imag, hops_total):
    radix_count = first_real.shape[-2]
    sub_total = first_real.shape[-1]
    index_b = jnp.arange(radix_count, dtype=jnp.int32)[:, None]
    index_p = jnp.arange(sub_total, dtype=jnp.int32)[None, :]
    twist_angle = 2.0 * math.pi / hops_total * (index_b * index_p % hops_total).astype(jnp.float32)
    twist_cos = jnp.cos(twist_angle)
    twist_sin = jnp.sin(twist_angle)
    twist_real = first_real * twist_cos + first_imag * twist_sin
    twist_imag = first_imag * twist_cos - first_real * twist_sin
    index_d = jnp.arange(radix_count, dtype=jnp.int32)[None, :]
    section_angle = (
        2.0 * math.pi / radix_count * (index_b * index_d % radix_count).astype(jnp.float32)
    )
    section_cos = jnp.cos(section_angle)
    section_sin = jnp.sin(section_angle)
    highest = lax.Precision.HIGHEST
    norm_factor = 1.0 / math.sqrt(hops_total)
    out_real = norm_factor * (
        jnp.einsum("...bq,bd->...dq", twist_real, section_cos, precision=highest)
        + jnp.einsum("...bq,bd->...dq", twist_imag, section_sin, precision=highest)
    )
    out_imag = norm_factor * (
        jnp.einsum("...bq,bd->...dq", twist_imag, section_cos, precision=highest)
        - jnp.einsum("...bq,bd->...dq", twist_real, section_sin, precision=highest)
    )
    return (out_real, out_imag)


def shards(frames, orders, owners, templates):
    rows_count = lax.axis_size("row")
    cols_count = lax.axis_size("col")
    devices_n = rows_count * cols_count
    sensors = frames.shape[0]
    hop_dev = frames.shape[1]
    frame_len = frames.shape[2]
    channels_n = 4 * frame_len
    hops_n = hop_dev * rows_count
    sub_n = hops_n // RADIX
    per_device = channels_n // devices_n
    local_channels = channels_n // cols_count
    combos = orders.shape[0] * orders.shape[1]
    feat_n = templates.shape[2]
    row_at = lax.axis_index("row")
    col_at = lax.axis_index("col")
    tail_frames = from_behind(frames[:, :3], "row", -1)
    padded = jnp.concatenate([frames, tail_frames], axis=1)
    column = jnp.arange(local_channels, dtype=jnp.int32)
    channel_ids = (column // per_device * cols_count + col_at) * per_device + column % per_device
    coefficients = channel_coefficients(channels_n, channel_ids)
    summed = jnp.zeros((sensors, 2 * local_channels, hop_dev), jnp.float32)
    for quarter in range(4):
        summed = summed + jnp.einsum(
            "shf,fk->skh",
            padded[:, quarter : quarter + hop_dev],
            coefficients[quarter * frame_len : (quarter + 1) * frame_len],
            preferred_element_type=jnp.float32,
        )
    hop_ids = row_at * hop_dev + jnp.arange(hop_dev, dtype=jnp.int32)
    real_part, imag_part = quarter_turn(
        summed[:, :local_channels], summed[:, local_channels:], channel_ids, hop_ids
    )
    demod = jnp.stack([real_part, imag_part]).astype(jnp.bfloat16)
    swapped = lax.all_to_all(demod, "row", split_axis=2, concat_axis=3, tiled=True)
    ordered = swapped.reshape(2, sensors, per_device, sub_n, RADIX).transpose(0, 1, 2, 4, 3)
    above = from_behind_2(ordered, ("row", "col"), -1)
    extended = jnp.concatenate([ordered, above], axis=2)
    own_real = ordered[0].astype(jnp.float32)
    own_imag = ordered[1].astype(jnp.float32)
    prod_real = []
    prod_imag = []
    for wheel in range(orders.shape[0]):
        for order_at in range(orders.shape[1]):
            partner = lax.dynamic_slice_in_dim(
                extended, orders[wheel, order_at], per_device, axis=2
            )
            partner = partner.astype(jnp.float32)
            prod_real.append(own_real * partner[0] + own_imag * partner[1])
            prod_imag.append(own_imag * partner[0] - own_real * partner[1])
    products = jnp.stack([jnp.stack(prod_real, axis=1), jnp.stack(prod_imag, axis=1)]).astype(
        jnp.bfloat16
    )
    flat_products = products.reshape(2, -1, sub_n)
    table_sub = sub_coefficients(sub_n)
    section_out = jnp.einsum(
        "prs,sq->prq", flat_products, table_sub, preferred_element_type=jnp.float32
    )
    grid_shape = (sensors, combos, per_device, RADIX, sub_n)
    first_real = (section_out[0, :, :sub_n] + section_out[1, :, sub_n:]).reshape(grid_shape)
    first_imag = (section_out[1, :, :sub_n] - section_out[0, :, sub_n:]).reshape(grid_shape)
    out_real, out_imag = finish_transform(first_real, first_imag, hops_n)
    spectrum = (
        jnp.stack([out_real, out_imag])
        .reshape(2, sensors, combos, per_device, hops_n)
        .astype(jnp.bfloat16)
    )
    feature = jnp.log1p(out_real * out_real + out_imag * out_imag).astype(jnp.bfloat16)
    tiles_dev = sensors * combos * RADIX
    tiles = feature.transpose(0, 1, 3, 2, 4).reshape(tiles_dev, per_device, sub_n)
    capacity = max(2, 2 * tiles_dev // devices_n)
    owner_ids = owners[:, 0]
    targets = jnp.arange(devices_n, dtype=jnp.int32)
    one_hot = (owner_ids[:, None] == targets[None, :]).astype(jnp.int32)
    before = jnp.cumsum(one_hot, axis=0) - one_hot
    slot_ids = jnp.sum(before * one_hot, axis=1)
    places = owner_ids * capacity + slot_ids
    slot_range = jnp.arange(devices_n * capacity, dtype=jnp.int32)
    placing = (places[None, :] == slot_range[:, None]).astype(jnp.bfloat16)
    outgoing = jnp.dot(
        placing, tiles.reshape(tiles_dev, per_device * sub_n), preferred_element_type=jnp.float32
    )
    outgoing = outgoing.astype(jnp.bfloat16).reshape(devices_n, capacity * per_device, sub_n)
    arrived = lax.all_to_all(outgoing, ("row", "col"), split_axis=0, concat_axis=0, tiled=True)
    found = jnp.einsum(
        "tkq,qf->tkf", arrived, templates[0], preferred_element_type=jnp.float32
    ).astype(jnp.bfloat16)
    found = found.reshape(devices_n, capacity, per_device, feat_n)
    return (spectrum, found[None])


def solution(mesh):
    in_specs = (P(None, "row", None), P(), P(("row", "col"), None), P(("row", "col"), None, None))
    out_specs = (
        P(None, None, None, ("row", "col"), None),
        P(("row", "col"), None, None, None, None),
    )
    return jax.shard_map(shards, mesh=mesh, in_specs=in_specs, out_specs=out_specs, check_vma=False)
```

```python
import math

import jax
import jax.numpy as jnp
from jax import lax
from jax.experimental import pallas as pl
from jax.experimental.pallas import tpu as pltpu
from jax.sharding import PartitionSpec as P
import numpy as np

RADIX = 8


def from_behind(block, axis, distance):
    devices = range(lax.axis_size(axis))
    route = [(i - distance, i) for i in devices if i - distance in devices]
    return lax.ppermute(block, axis, route)


def from_behind_2(value, axis, steps):
    count = lax.axis_size(axis)
    pairs = [(source, (source + steps) % count) for source in range(count)]
    return lax.ppermute(value, axis, pairs)


def channel_coefficients(n_total, channel_ids):
    position = jnp.arange(n_total, dtype=jnp.int32)
    turns = position[:, None] * channel_ids[None, :] % n_total
    phase_angle = 2.0 * math.pi / n_total * turns.astype(jnp.float32)
    window = 0.5 - 0.5 * jnp.cos(2.0 * math.pi / n_total * position.astype(jnp.float32))
    gain_factor = math.sqrt(8.0 / (3.0 * n_total))
    weighted = gain_factor * window[:, None]
    both = jnp.concatenate(
        [weighted * jnp.cos(phase_angle), weighted * jnp.sin(phase_angle)], axis=1
    )
    return both.astype(jnp.bfloat16)


def sub_coefficients(sub_total):
    index_a = jnp.arange(sub_total, dtype=jnp.int32)
    turns = index_a[:, None] * index_a[None, :] % sub_total
    phase_angle = 2.0 * math.pi / sub_total * turns.astype(jnp.float32)
    return jnp.concatenate([jnp.cos(phase_angle), jnp.sin(phase_angle)], axis=1).astype(
        jnp.bfloat16
    )


def quarter_turn(a_cos, a_sin, channel_ids, hop_ids):
    phase_step = channel_ids[:, None] % 4 * (hop_ids[None, :] % 4) % 4
    cos_quarter = (phase_step == 0).astype(jnp.float32) - (phase_step == 2).astype(jnp.float32)
    sin_quarter = (phase_step == 1).astype(jnp.float32) - (phase_step == 3).astype(jnp.float32)
    real_part = a_cos * cos_quarter - a_sin * sin_quarter
    imag_part = -a_sin * cos_quarter - a_cos * sin_quarter
    return (real_part, imag_part)


def finish_transform(first_real, first_imag, hops_total):
    radix_count = first_real.shape[-2]
    sub_total = first_real.shape[-1]
    index_b = jnp.arange(radix_count, dtype=jnp.int32)[:, None]
    index_p = jnp.arange(sub_total, dtype=jnp.int32)[None, :]
    twist_angle = 2.0 * math.pi / hops_total * (index_b * index_p % hops_total).astype(jnp.float32)
    twist_cos = jnp.cos(twist_angle)
    twist_sin = jnp.sin(twist_angle)
    twist_real = first_real * twist_cos + first_imag * twist_sin
    twist_imag = first_imag * twist_cos - first_real * twist_sin
    index_d = jnp.arange(radix_count, dtype=jnp.int32)[None, :]
    section_angle = (
        2.0 * math.pi / radix_count * (index_b * index_d % radix_count).astype(jnp.float32)
    )
    section_cos = jnp.cos(section_angle)
    section_sin = jnp.sin(section_angle)
    highest = lax.Precision.HIGHEST
    norm_factor = 1.0 / math.sqrt(hops_total)
    out_real = norm_factor * (
        jnp.einsum("...bq,bd->...dq", twist_real, section_cos, precision=highest)
        + jnp.einsum("...bq,bd->...dq", twist_imag, section_sin, precision=highest)
    )
    out_imag = norm_factor * (
        jnp.einsum("...bq,bd->...dq", twist_imag, section_cos, precision=highest)
        - jnp.einsum("...bq,bd->...dq", twist_real, section_sin, precision=highest)
    )
    return (out_real, out_imag)


def section_mixers(radix_count, rows_per):
    index_b = np.arange(radix_count)
    angle = 2.0 * np.pi / radix_count * ((index_b[:, None] * index_b[None, :]) % radix_count)
    mixers = []
    for table in (np.cos(angle).astype(np.float32), np.sin(angle).astype(np.float32)):
        full = np.zeros((radix_count * rows_per, rows_per * radix_count), np.float32)
        for d in range(radix_count):
            for b in range(radix_count):
                for k in range(rows_per):
                    full[d * rows_per + k, k * radix_count + b] = table[b, d]
        high = jnp.asarray(full).astype(jnp.bfloat16)
        low = (jnp.asarray(full) - high.astype(jnp.float32)).astype(jnp.bfloat16)
        mixers += [high, low]
    return jnp.stack(mixers)


def spectrum_kernel(prod_ref, cos_ref, sin_ref, twc_ref, tws_ref, mix_ref, spec_ref, tile_ref):
    f32 = jnp.float32
    prod_real = prod_ref[0, 0]
    prod_imag = prod_ref[1, 0]
    sub_cos = cos_ref[...]
    sub_sin = sin_ref[...]
    first_real = jnp.dot(prod_real, sub_cos, preferred_element_type=f32) + jnp.dot(
        prod_imag, sub_sin, preferred_element_type=f32
    )
    first_imag = jnp.dot(prod_imag, sub_cos, preferred_element_type=f32) - jnp.dot(
        prod_real, sub_sin, preferred_element_type=f32
    )
    twist_cos = twc_ref[...]
    twist_sin = tws_ref[...]
    twist_real = first_real * twist_cos + first_imag * twist_sin
    twist_imag = first_imag * twist_cos - first_real * twist_sin

    def split(value):
        high = value.astype(jnp.bfloat16)
        return high, (value - high.astype(f32)).astype(jnp.bfloat16)

    real_high, real_low = split(twist_real)
    imag_high, imag_low = split(twist_imag)

    def mix(table, high, low):
        return (
            jnp.dot(mix_ref[table], high, preferred_element_type=f32)
            + jnp.dot(mix_ref[table], low, preferred_element_type=f32)
            + jnp.dot(mix_ref[table + 1], high, preferred_element_type=f32)
        )

    out_real = mix(0, real_high, real_low) + mix(2, imag_high, imag_low)
    out_imag = mix(0, imag_high, imag_low) - mix(2, real_high, real_low)
    feature = jnp.log1p(out_real * out_real + out_imag * out_imag)
    rows_per = tile_ref.shape[1]
    sub_n = tile_ref.shape[2]
    for d in range(tile_ref.shape[0]):
        rows = slice(d * rows_per, (d + 1) * rows_per)
        lanes = slice(d * sub_n, (d + 1) * sub_n)
        spec_ref[0, 0, 0, :, lanes] = out_real[rows].astype(spec_ref.dtype)
        spec_ref[1, 0, 0, :, lanes] = out_imag[rows].astype(spec_ref.dtype)
        tile_ref[d] = feature[rows].astype(tile_ref.dtype)


def spectrum_call(products, table_sub, hops_total):
    _, sensors, combos, rows, sub_n = products.shape
    per_device = rows // RADIX
    blocks = sensors * combos
    flat = products.reshape(2, blocks, rows, sub_n)
    index_b = jnp.arange(RADIX, dtype=jnp.int32)[:, None]
    index_p = jnp.arange(sub_n, dtype=jnp.int32)[None, :]
    twist_angle = 2.0 * math.pi / hops_total * (index_b * index_p % hops_total).astype(jnp.float32)
    norm_factor = 1.0 / math.sqrt(hops_total)
    twist_cos = jnp.tile(norm_factor * jnp.cos(twist_angle), (per_device, 1))
    twist_sin = jnp.tile(norm_factor * jnp.sin(twist_angle), (per_device, 1))
    mixers = section_mixers(RADIX, per_device)
    spectrum, tiles = pl.pallas_call(
        spectrum_kernel,
        grid=(blocks,),
        in_specs=[
            pl.BlockSpec((2, 1, rows, sub_n), lambda i: (0, i, 0, 0)),
            pl.BlockSpec((sub_n, sub_n), lambda i: (0, 0)),
            pl.BlockSpec((sub_n, sub_n), lambda i: (0, 1)),
            pl.BlockSpec((rows, sub_n), lambda i: (0, 0)),
            pl.BlockSpec((rows, sub_n), lambda i: (0, 0)),
            pl.BlockSpec((4, rows, rows), lambda i: (0, 0, 0)),
        ],
        out_specs=[
            pl.BlockSpec(
                (2, 1, 1, per_device, RADIX * sub_n),
                lambda i: (0, i // combos, i % combos, 0, 0),
            ),
            pl.BlockSpec((RADIX, per_device, sub_n), lambda i: (i, 0, 0)),
        ],
        out_shape=[
            jax.ShapeDtypeStruct((2, sensors, combos, per_device, RADIX * sub_n), jnp.bfloat16),
            jax.ShapeDtypeStruct((blocks * RADIX, per_device, sub_n), jnp.bfloat16),
        ],
        compiler_params=pltpu.CompilerParams(vmem_limit_bytes=48 * 1024 * 1024),
        cost_estimate=pl.CostEstimate(
            flops=blocks * (8 * rows * sub_n * sub_n + 24 * rows * rows * sub_n),
            transcendentals=blocks * rows * sub_n,
            bytes_accessed=blocks * rows * sub_n * 2 * 5 + 4 * sub_n * sub_n,
        ),
    )(flat, table_sub, table_sub, twist_cos, twist_sin, mixers)
    return spectrum, tiles


def shards(frames, orders, owners, templates):
    rows_count = lax.axis_size("row")
    cols_count = lax.axis_size("col")
    devices_n = rows_count * cols_count
    sensors = frames.shape[0]
    hop_dev = frames.shape[1]
    frame_len = frames.shape[2]
    channels_n = 4 * frame_len
    hops_n = hop_dev * rows_count
    sub_n = hops_n // RADIX
    per_device = channels_n // devices_n
    local_channels = channels_n // cols_count
    combos = orders.shape[0] * orders.shape[1]
    feat_n = templates.shape[2]
    row_at = lax.axis_index("row")
    col_at = lax.axis_index("col")
    tail_frames = from_behind(frames[:, :3], "row", -1)
    padded = jnp.concatenate([frames, tail_frames], axis=1)
    column = jnp.arange(local_channels, dtype=jnp.int32)
    channel_ids = (column // per_device * cols_count + col_at) * per_device + column % per_device
    coefficients = channel_coefficients(channels_n, channel_ids)
    summed = jnp.zeros((sensors, 2 * local_channels, hop_dev), jnp.float32)
    for quarter in range(4):
        summed = summed + jnp.einsum(
            "shf,fk->skh",
            padded[:, quarter : quarter + hop_dev],
            coefficients[quarter * frame_len : (quarter + 1) * frame_len],
            preferred_element_type=jnp.float32,
        )
    hop_ids = row_at * hop_dev + jnp.arange(hop_dev, dtype=jnp.int32)
    real_part, imag_part = quarter_turn(
        summed[:, :local_channels], summed[:, local_channels:], channel_ids, hop_ids
    )
    demod = jnp.stack([real_part, imag_part]).astype(jnp.bfloat16)
    swapped = lax.all_to_all(demod, "row", split_axis=2, concat_axis=3, tiled=True)
    ordered = swapped.reshape(2, sensors, per_device, sub_n, RADIX).transpose(0, 1, 2, 4, 3)
    above = from_behind_2(ordered, ("row", "col"), -1)
    extended = jnp.concatenate([ordered, above], axis=2)
    own_real = ordered[0].astype(jnp.float32)
    own_imag = ordered[1].astype(jnp.float32)
    prod_real = []
    prod_imag = []
    for wheel in range(orders.shape[0]):
        for order_at in range(orders.shape[1]):
            partner = lax.dynamic_slice_in_dim(
                extended, orders[wheel, order_at], per_device, axis=2
            )
            partner = partner.astype(jnp.float32)
            prod_real.append(own_real * partner[0] + own_imag * partner[1])
            prod_imag.append(own_imag * partner[0] - own_real * partner[1])
    products = jnp.stack([jnp.stack(prod_real, axis=1), jnp.stack(prod_imag, axis=1)]).astype(
        jnp.bfloat16
    )
    table_sub = sub_coefficients(sub_n)
    spectrum, tiles = spectrum_call(
        products.reshape(2, sensors, combos, per_device * RADIX, sub_n), table_sub, hops_n
    )
    tiles_dev = sensors * combos * RADIX
    capacity = max(2, 2 * tiles_dev // devices_n)
    owner_ids = owners[:, 0]
    targets = jnp.arange(devices_n, dtype=jnp.int32)
    one_hot = (owner_ids[:, None] == targets[None, :]).astype(jnp.int32)
    before = jnp.cumsum(one_hot, axis=0) - one_hot
    slot_ids = jnp.sum(before * one_hot, axis=1)
    places = owner_ids * capacity + slot_ids
    slot_range = jnp.arange(devices_n * capacity, dtype=jnp.int32)
    placing = (places[None, :] == slot_range[:, None]).astype(jnp.bfloat16)
    outgoing = jnp.einsum("ot,tkq->okq", placing, tiles, preferred_element_type=jnp.float32)
    outgoing = outgoing.astype(jnp.bfloat16).reshape(devices_n, capacity * per_device, sub_n)
    arrived = lax.all_to_all(outgoing, ("row", "col"), split_axis=0, concat_axis=0, tiled=True)
    found = jnp.einsum(
        "tkq,qf->tkf", arrived, templates[0], preferred_element_type=jnp.float32
    ).astype(jnp.bfloat16)
    found = found.reshape(devices_n, capacity, per_device, feat_n)
    return (spectrum, found[None])


def solution(mesh):
    in_specs = (P(None, "row", None), P(), P(("row", "col"), None), P(("row", "col"), None, None))
    out_specs = (
        P(None, None, None, ("row", "col"), None),
        P(("row", "col"), None, None, None, None),
    )
    return jax.shard_map(shards, mesh=mesh, in_specs=in_specs, out_specs=out_specs, check_vma=False)
```

```python
import math

import jax
import jax.numpy as jnp
from jax import lax
from jax.experimental import pallas as pl
from jax.experimental.pallas import tpu as pltpu
from jax.sharding import PartitionSpec as P
import numpy as np

RADIX = 8


def from_behind(block, axis, distance):
    devices = range(lax.axis_size(axis))
    route = [(i - distance, i) for i in devices if i - distance in devices]
    return lax.ppermute(block, axis, route)


def from_behind_2(value, axis, steps):
    count = lax.axis_size(axis)
    pairs = [(source, (source + steps) % count) for source in range(count)]
    return lax.ppermute(value, axis, pairs)


def channel_coefficients(n_total, channel_ids):
    position = jnp.arange(n_total, dtype=jnp.int32)
    turns = position[:, None] * channel_ids[None, :] % n_total
    phase_angle = 2.0 * math.pi / n_total * turns.astype(jnp.float32)
    window = 0.5 - 0.5 * jnp.cos(2.0 * math.pi / n_total * position.astype(jnp.float32))
    gain_factor = math.sqrt(8.0 / (3.0 * n_total))
    weighted = gain_factor * window[:, None]
    both = jnp.concatenate(
        [weighted * jnp.cos(phase_angle), weighted * jnp.sin(phase_angle)], axis=1
    )
    return both.astype(jnp.bfloat16)


def sub_coefficients(sub_total):
    index_a = jnp.arange(sub_total, dtype=jnp.int32)
    turns = index_a[:, None] * index_a[None, :] % sub_total
    phase_angle = 2.0 * math.pi / sub_total * turns.astype(jnp.float32)
    return jnp.concatenate([jnp.cos(phase_angle), jnp.sin(phase_angle)], axis=1).astype(
        jnp.bfloat16
    )


def quarter_turn(a_cos, a_sin, channel_ids, hop_ids):
    phase_step = channel_ids[:, None] % 4 * (hop_ids[None, :] % 4) % 4
    cos_quarter = (phase_step == 0).astype(jnp.float32) - (phase_step == 2).astype(jnp.float32)
    sin_quarter = (phase_step == 1).astype(jnp.float32) - (phase_step == 3).astype(jnp.float32)
    real_part = a_cos * cos_quarter - a_sin * sin_quarter
    imag_part = -a_sin * cos_quarter - a_cos * sin_quarter
    return (real_part, imag_part)


def finish_transform(first_real, first_imag, hops_total):
    radix_count = first_real.shape[-2]
    sub_total = first_real.shape[-1]
    index_b = jnp.arange(radix_count, dtype=jnp.int32)[:, None]
    index_p = jnp.arange(sub_total, dtype=jnp.int32)[None, :]
    twist_angle = 2.0 * math.pi / hops_total * (index_b * index_p % hops_total).astype(jnp.float32)
    twist_cos = jnp.cos(twist_angle)
    twist_sin = jnp.sin(twist_angle)
    twist_real = first_real * twist_cos + first_imag * twist_sin
    twist_imag = first_imag * twist_cos - first_real * twist_sin
    index_d = jnp.arange(radix_count, dtype=jnp.int32)[None, :]
    section_angle = (
        2.0 * math.pi / radix_count * (index_b * index_d % radix_count).astype(jnp.float32)
    )
    section_cos = jnp.cos(section_angle)
    section_sin = jnp.sin(section_angle)
    highest = lax.Precision.HIGHEST
    norm_factor = 1.0 / math.sqrt(hops_total)
    out_real = norm_factor * (
        jnp.einsum("...bq,bd->...dq", twist_real, section_cos, precision=highest)
        + jnp.einsum("...bq,bd->...dq", twist_imag, section_sin, precision=highest)
    )
    out_imag = norm_factor * (
        jnp.einsum("...bq,bd->...dq", twist_imag, section_cos, precision=highest)
        - jnp.einsum("...bq,bd->...dq", twist_real, section_sin, precision=highest)
    )
    return (out_real, out_imag)


def section_mixers(radix_count, rows_per):
    index_b = np.arange(radix_count)
    angle = 2.0 * np.pi / radix_count * ((index_b[:, None] * index_b[None, :]) % radix_count)
    mixers = []
    for table in (np.cos(angle).astype(np.float32), np.sin(angle).astype(np.float32)):
        full = np.zeros((radix_count * rows_per, rows_per * radix_count), np.float32)
        for d in range(radix_count):
            for b in range(radix_count):
                for k in range(rows_per):
                    full[d * rows_per + k, k * radix_count + b] = table[b, d]
        high = jnp.asarray(full).astype(jnp.bfloat16)
        low = (jnp.asarray(full) - high.astype(jnp.float32)).astype(jnp.bfloat16)
        mixers += [high, low]
    return jnp.stack(mixers)


def spectrum_kernel(prod_ref, cos_ref, sin_ref, twc_ref, tws_ref, mix_ref, spec_ref, tile_ref):
    f32 = jnp.float32
    prod_real = prod_ref[0, 0]
    prod_imag = prod_ref[1, 0]
    sub_cos = cos_ref[...]
    sub_sin = sin_ref[...]
    first_real = jnp.dot(prod_real, sub_cos, preferred_element_type=f32) + jnp.dot(
        prod_imag, sub_sin, preferred_element_type=f32
    )
    first_imag = jnp.dot(prod_imag, sub_cos, preferred_element_type=f32) - jnp.dot(
        prod_real, sub_sin, preferred_element_type=f32
    )
    twist_cos = twc_ref[...]
    twist_sin = tws_ref[...]
    twist_real = first_real * twist_cos + first_imag * twist_sin
    twist_imag = first_imag * twist_cos - first_real * twist_sin

    def split(value):
        high = value.astype(jnp.bfloat16)
        return high, (value - high.astype(f32)).astype(jnp.bfloat16)

    real_high, real_low = split(twist_real)
    imag_high, imag_low = split(twist_imag)

    def mix(table, high, low):
        return (
            jnp.dot(mix_ref[table], high, preferred_element_type=f32)
            + jnp.dot(mix_ref[table], low, preferred_element_type=f32)
            + jnp.dot(mix_ref[table + 1], high, preferred_element_type=f32)
        )

    out_real = mix(0, real_high, real_low) + mix(2, imag_high, imag_low)
    out_imag = mix(0, imag_high, imag_low) - mix(2, real_high, real_low)
    feature = jnp.log1p(out_real * out_real + out_imag * out_imag)
    rows_per = tile_ref.shape[1]
    sub_n = tile_ref.shape[2]
    for d in range(tile_ref.shape[0]):
        rows = slice(d * rows_per, (d + 1) * rows_per)
        lanes = slice(d * sub_n, (d + 1) * sub_n)
        spec_ref[0, 0, 0, :, lanes] = out_real[rows].astype(spec_ref.dtype)
        spec_ref[1, 0, 0, :, lanes] = out_imag[rows].astype(spec_ref.dtype)
        tile_ref[d] = feature[rows].astype(tile_ref.dtype)


def spectrum_call(products, table_sub, hops_total):
    _, sensors, combos, rows, sub_n = products.shape
    per_device = rows // RADIX
    blocks = sensors * combos
    flat = products.reshape(2, blocks, rows, sub_n)
    index_b = jnp.arange(RADIX, dtype=jnp.int32)[:, None]
    index_p = jnp.arange(sub_n, dtype=jnp.int32)[None, :]
    twist_angle = 2.0 * math.pi / hops_total * (index_b * index_p % hops_total).astype(jnp.float32)
    norm_factor = 1.0 / math.sqrt(hops_total)
    twist_cos = jnp.tile(norm_factor * jnp.cos(twist_angle), (per_device, 1))
    twist_sin = jnp.tile(norm_factor * jnp.sin(twist_angle), (per_device, 1))
    mixers = section_mixers(RADIX, per_device)
    spectrum, tiles = pl.pallas_call(
        spectrum_kernel,
        grid=(blocks,),
        in_specs=[
            pl.BlockSpec((2, 1, rows, sub_n), lambda i: (0, i, 0, 0)),
            pl.BlockSpec((sub_n, sub_n), lambda i: (0, 0)),
            pl.BlockSpec((sub_n, sub_n), lambda i: (0, 1)),
            pl.BlockSpec((rows, sub_n), lambda i: (0, 0)),
            pl.BlockSpec((rows, sub_n), lambda i: (0, 0)),
            pl.BlockSpec((4, rows, rows), lambda i: (0, 0, 0)),
        ],
        out_specs=[
            pl.BlockSpec(
                (2, 1, 1, per_device, RADIX * sub_n),
                lambda i: (0, i // combos, i % combos, 0, 0),
            ),
            pl.BlockSpec((RADIX, per_device, sub_n), lambda i: (i, 0, 0)),
        ],
        out_shape=[
            jax.ShapeDtypeStruct((2, sensors, combos, per_device, RADIX * sub_n), jnp.bfloat16),
            jax.ShapeDtypeStruct((blocks * RADIX, per_device, sub_n), jnp.bfloat16),
        ],
        compiler_params=pltpu.CompilerParams(vmem_limit_bytes=48 * 1024 * 1024),
        cost_estimate=pl.CostEstimate(
            flops=blocks * (8 * rows * sub_n * sub_n + 24 * rows * rows * sub_n),
            transcendentals=blocks * rows * sub_n,
            bytes_accessed=blocks * rows * sub_n * 2 * 5 + 4 * sub_n * sub_n,
        ),
    )(flat, table_sub, table_sub, twist_cos, twist_sin, mixers)
    return spectrum, tiles


def shards(frames, orders, owners, templates):
    rows_count = lax.axis_size("row")
    cols_count = lax.axis_size("col")
    devices_n = rows_count * cols_count
    sensors = frames.shape[0]
    hop_dev = frames.shape[1]
    frame_len = frames.shape[2]
    channels_n = 4 * frame_len
    hops_n = hop_dev * rows_count
    sub_n = hops_n // RADIX
    per_device = channels_n // devices_n
    local_channels = channels_n // cols_count
    combos = orders.shape[0] * orders.shape[1]
    feat_n = templates.shape[2]
    row_at = lax.axis_index("row")
    col_at = lax.axis_index("col")
    tail_frames = from_behind(frames[:, :3], "row", -1)
    padded = jnp.concatenate([frames, tail_frames], axis=1)
    column = jnp.arange(local_channels, dtype=jnp.int32)
    channel_ids = (column // per_device * cols_count + col_at) * per_device + column % per_device
    coefficients = channel_coefficients(channels_n, channel_ids)
    summed = jnp.zeros((sensors, 2 * local_channels, hop_dev), jnp.float32)
    for quarter in range(4):
        summed = summed + jnp.einsum(
            "shf,fk->skh",
            padded[:, quarter : quarter + hop_dev],
            coefficients[quarter * frame_len : (quarter + 1) * frame_len],
            preferred_element_type=jnp.float32,
        )
    hop_ids = row_at * hop_dev + jnp.arange(hop_dev, dtype=jnp.int32)
    real_part, imag_part = quarter_turn(
        summed[:, :local_channels], summed[:, local_channels:], channel_ids, hop_ids
    )
    demod = jnp.stack([real_part, imag_part]).astype(jnp.bfloat16)
    swapped = lax.all_to_all(demod, "row", split_axis=2, concat_axis=3, tiled=True)
    ordered = swapped.reshape(2, sensors, per_device, sub_n, RADIX).transpose(0, 1, 2, 4, 3)
    above = from_behind_2(ordered, ("row", "col"), -1)
    extended = jnp.concatenate([ordered, above], axis=2)
    own_real = ordered[0].astype(jnp.float32)
    own_imag = ordered[1].astype(jnp.float32)
    prod_real = []
    prod_imag = []
    for wheel in range(orders.shape[0]):
        for order_at in range(orders.shape[1]):
            partner = lax.dynamic_slice_in_dim(
                extended, orders[wheel, order_at], per_device, axis=2
            )
            partner = partner.astype(jnp.float32)
            prod_real.append(own_real * partner[0] + own_imag * partner[1])
            prod_imag.append(own_imag * partner[0] - own_real * partner[1])
    products = jnp.stack([jnp.stack(prod_real, axis=1), jnp.stack(prod_imag, axis=1)]).astype(
        jnp.bfloat16
    )
    table_sub = sub_coefficients(sub_n)
    spectrum, tiles = spectrum_call(
        products.reshape(2, sensors, combos, per_device * RADIX, sub_n), table_sub, hops_n
    )
    tiles_dev = sensors * combos * RADIX
    capacity = max(2, 2 * tiles_dev // devices_n)
    owner_ids = owners[:, 0]
    targets = jnp.arange(devices_n, dtype=jnp.int32)
    one_hot = (owner_ids[:, None] == targets[None, :]).astype(jnp.int32)
    before = jnp.cumsum(one_hot, axis=0) - one_hot
    slot_ids = jnp.sum(before * one_hot, axis=1)
    places = owner_ids * capacity + slot_ids
    slot_range = jnp.arange(devices_n * capacity, dtype=jnp.int32)
    placing = (places[None, :] == slot_range[:, None]).astype(jnp.bfloat16)
    outgoing = jnp.einsum("ot,tkq->okq", placing, tiles, preferred_element_type=jnp.float32)
    outgoing = outgoing.astype(jnp.bfloat16).reshape(devices_n, capacity * per_device, sub_n)
    rows_count_ = lax.axis_size("row")
    staged = outgoing.reshape(rows_count_, cols_count, capacity * per_device, sub_n)
    staged = lax.all_to_all(staged, "col", split_axis=1, concat_axis=1, tiled=True)
    staged = lax.all_to_all(staged, "row", split_axis=0, concat_axis=0, tiled=True)
    arrived = staged.reshape(devices_n, capacity * per_device, sub_n)
    found = jnp.einsum(
        "tkq,qf->tkf", arrived, templates[0], preferred_element_type=jnp.float32
    ).astype(jnp.bfloat16)
    found = found.reshape(devices_n, capacity, per_device, feat_n)
    return (spectrum, found[None])


def solution(mesh):
    in_specs = (P(None, "row", None), P(), P(("row", "col"), None), P(("row", "col"), None, None))
    out_specs = (
        P(None, None, None, ("row", "col"), None),
        P(("row", "col"), None, None, None, None),
    )
    return jax.shard_map(shards, mesh=mesh, in_specs=in_specs, out_specs=out_specs, check_vma=False)
```

```python
import math

import jax
import jax.numpy as jnp
from jax import lax
from jax.experimental import pallas as pl
from jax.experimental.pallas import tpu as pltpu
from jax.sharding import PartitionSpec as P
import numpy as np

RADIX = 8


def from_behind(block, axis, distance):
    devices = range(lax.axis_size(axis))
    route = [(i - distance, i) for i in devices if i - distance in devices]
    return lax.ppermute(block, axis, route)


def from_behind_2(value, axis, steps):
    count = lax.axis_size(axis)
    pairs = [(source, (source + steps) % count) for source in range(count)]
    return lax.ppermute(value, axis, pairs)


def channel_coefficients(n_total, channel_ids):
    coarse_n = 64
    position = jnp.arange(n_total, dtype=jnp.int32)
    high = jnp.arange(n_total // coarse_n, dtype=jnp.int32) * coarse_n
    low = jnp.arange(coarse_n, dtype=jnp.int32)
    step = 2.0 * math.pi / n_total
    high_angle = step * (high[:, None] * channel_ids[None, :] % n_total).astype(jnp.float32)
    low_angle = step * (low[:, None] * channel_ids[None, :] % n_total).astype(jnp.float32)
    high_cos, high_sin = jnp.cos(high_angle)[:, None], jnp.sin(high_angle)[:, None]
    low_cos, low_sin = jnp.cos(low_angle)[None], jnp.sin(low_angle)[None]
    cos_part = (high_cos * low_cos - high_sin * low_sin).reshape(n_total, -1)
    sin_part = (high_sin * low_cos + high_cos * low_sin).reshape(n_total, -1)
    window = 0.5 - 0.5 * jnp.cos(step * position.astype(jnp.float32))
    gain_factor = math.sqrt(8.0 / (3.0 * n_total))
    weighted = gain_factor * window[:, None]
    both = jnp.concatenate([weighted * cos_part, weighted * sin_part], axis=1)
    return both.astype(jnp.bfloat16)


def sub_coefficients(sub_total):
    index_a = jnp.arange(sub_total, dtype=jnp.int32)
    turns = index_a[:, None] * index_a[None, :] % sub_total
    phase_angle = 2.0 * math.pi / sub_total * turns.astype(jnp.float32)
    return jnp.concatenate([jnp.cos(phase_angle), jnp.sin(phase_angle)], axis=1).astype(
        jnp.bfloat16
    )


def quarter_turn(a_cos, a_sin, channel_ids, hop_ids):
    phase_step = channel_ids[:, None] % 4 * (hop_ids[None, :] % 4) % 4
    cos_quarter = (phase_step == 0).astype(jnp.float32) - (phase_step == 2).astype(jnp.float32)
    sin_quarter = (phase_step == 1).astype(jnp.float32) - (phase_step == 3).astype(jnp.float32)
    real_part = a_cos * cos_quarter - a_sin * sin_quarter
    imag_part = -a_sin * cos_quarter - a_cos * sin_quarter
    return (real_part, imag_part)


def finish_transform(first_real, first_imag, hops_total):
    radix_count = first_real.shape[-2]
    sub_total = first_real.shape[-1]
    index_b = jnp.arange(radix_count, dtype=jnp.int32)[:, None]
    index_p = jnp.arange(sub_total, dtype=jnp.int32)[None, :]
    twist_angle = 2.0 * math.pi / hops_total * (index_b * index_p % hops_total).astype(jnp.float32)
    twist_cos = jnp.cos(twist_angle)
    twist_sin = jnp.sin(twist_angle)
    twist_real = first_real * twist_cos + first_imag * twist_sin
    twist_imag = first_imag * twist_cos - first_real * twist_sin
    index_d = jnp.arange(radix_count, dtype=jnp.int32)[None, :]
    section_angle = (
        2.0 * math.pi / radix_count * (index_b * index_d % radix_count).astype(jnp.float32)
    )
    section_cos = jnp.cos(section_angle)
    section_sin = jnp.sin(section_angle)
    highest = lax.Precision.HIGHEST
    norm_factor = 1.0 / math.sqrt(hops_total)
    out_real = norm_factor * (
        jnp.einsum("...bq,bd->...dq", twist_real, section_cos, precision=highest)
        + jnp.einsum("...bq,bd->...dq", twist_imag, section_sin, precision=highest)
    )
    out_imag = norm_factor * (
        jnp.einsum("...bq,bd->...dq", twist_imag, section_cos, precision=highest)
        - jnp.einsum("...bq,bd->...dq", twist_real, section_sin, precision=highest)
    )
    return (out_real, out_imag)


def section_mixers(radix_count, rows_per):
    index_b = np.arange(radix_count)
    angle = 2.0 * np.pi / radix_count * ((index_b[:, None] * index_b[None, :]) % radix_count)
    mixers = []
    for table in (np.cos(angle).astype(np.float32), np.sin(angle).astype(np.float32)):
        full = np.zeros((radix_count * rows_per, rows_per * radix_count), np.float32)
        for d in range(radix_count):
            for b in range(radix_count):
                for k in range(rows_per):
                    full[d * rows_per + k, k * radix_count + b] = table[b, d]
        high = jnp.asarray(full).astype(jnp.bfloat16)
        low = (jnp.asarray(full) - high.astype(jnp.float32)).astype(jnp.bfloat16)
        mixers += [high, low]
    return jnp.stack(mixers)


def spectrum_kernel(prod_ref, cos_ref, sin_ref, twc_ref, tws_ref, mix_ref, spec_ref, tile_ref):
    f32 = jnp.float32
    prod_real = prod_ref[0, 0]
    prod_imag = prod_ref[1, 0]
    sub_cos = cos_ref[...]
    sub_sin = sin_ref[...]
    first_real = jnp.dot(prod_real, sub_cos, preferred_element_type=f32) + jnp.dot(
        prod_imag, sub_sin, preferred_element_type=f32
    )
    first_imag = jnp.dot(prod_imag, sub_cos, preferred_element_type=f32) - jnp.dot(
        prod_real, sub_sin, preferred_element_type=f32
    )
    twist_cos = twc_ref[...]
    twist_sin = tws_ref[...]
    twist_real = first_real * twist_cos + first_imag * twist_sin
    twist_imag = first_imag * twist_cos - first_real * twist_sin

    def split(value):
        high = value.astype(jnp.bfloat16)
        return high, (value - high.astype(f32)).astype(jnp.bfloat16)

    real_high, real_low = split(twist_real)
    imag_high, imag_low = split(twist_imag)

    def mix(table, high, low):
        return jnp.dot(mix_ref[table], high, preferred_element_type=f32) + jnp.dot(
            mix_ref[table], low, preferred_element_type=f32
        )

    out_real = mix(0, real_high, real_low) + mix(2, imag_high, imag_low)
    out_imag = mix(0, imag_high, imag_low) - mix(2, real_high, real_low)
    feature = jnp.log1p(out_real * out_real + out_imag * out_imag)
    rows_per = tile_ref.shape[1]
    sub_n = tile_ref.shape[2]
    for d in range(tile_ref.shape[0]):
        rows = slice(d * rows_per, (d + 1) * rows_per)
        lanes = slice(d * sub_n, (d + 1) * sub_n)
        spec_ref[0, 0, 0, :, lanes] = out_real[rows].astype(spec_ref.dtype)
        spec_ref[1, 0, 0, :, lanes] = out_imag[rows].astype(spec_ref.dtype)
        tile_ref[d] = feature[rows].astype(tile_ref.dtype)


def spectrum_call(products, table_sub, hops_total):
    _, sensors, combos, rows, sub_n = products.shape
    per_device = rows // RADIX
    blocks = sensors * combos
    flat = products.reshape(2, blocks, rows, sub_n)
    index_b = jnp.arange(RADIX, dtype=jnp.int32)[:, None]
    index_p = jnp.arange(sub_n, dtype=jnp.int32)[None, :]
    twist_angle = 2.0 * math.pi / hops_total * (index_b * index_p % hops_total).astype(jnp.float32)
    norm_factor = 1.0 / math.sqrt(hops_total)
    twist_cos = jnp.tile(norm_factor * jnp.cos(twist_angle), (per_device, 1))
    twist_sin = jnp.tile(norm_factor * jnp.sin(twist_angle), (per_device, 1))
    mixers = section_mixers(RADIX, per_device)
    spectrum, tiles = pl.pallas_call(
        spectrum_kernel,
        grid=(blocks,),
        in_specs=[
            pl.BlockSpec((2, 1, rows, sub_n), lambda i: (0, i, 0, 0)),
            pl.BlockSpec((sub_n, sub_n), lambda i: (0, 0)),
            pl.BlockSpec((sub_n, sub_n), lambda i: (0, 1)),
            pl.BlockSpec((rows, sub_n), lambda i: (0, 0)),
            pl.BlockSpec((rows, sub_n), lambda i: (0, 0)),
            pl.BlockSpec((4, rows, rows), lambda i: (0, 0, 0)),
        ],
        out_specs=[
            pl.BlockSpec(
                (2, 1, 1, per_device, RADIX * sub_n),
                lambda i: (0, i // combos, i % combos, 0, 0),
            ),
            pl.BlockSpec((RADIX, per_device, sub_n), lambda i: (i, 0, 0)),
        ],
        out_shape=[
            jax.ShapeDtypeStruct((2, sensors, combos, per_device, RADIX * sub_n), jnp.bfloat16),
            jax.ShapeDtypeStruct((blocks * RADIX, per_device, sub_n), jnp.bfloat16),
        ],
        compiler_params=pltpu.CompilerParams(vmem_limit_bytes=48 * 1024 * 1024),
        cost_estimate=pl.CostEstimate(
            flops=blocks * (8 * rows * sub_n * sub_n + 16 * rows * rows * sub_n),
            transcendentals=blocks * rows * sub_n,
            bytes_accessed=blocks * rows * sub_n * 2 * 5 + 4 * sub_n * sub_n,
        ),
    )(flat, table_sub, table_sub, twist_cos, twist_sin, mixers)
    return spectrum, tiles


def shards(frames, orders, owners, templates):
    rows_count = lax.axis_size("row")
    cols_count = lax.axis_size("col")
    devices_n = rows_count * cols_count
    sensors = frames.shape[0]
    hop_dev = frames.shape[1]
    frame_len = frames.shape[2]
    channels_n = 4 * frame_len
    hops_n = hop_dev * rows_count
    sub_n = hops_n // RADIX
    per_device = channels_n // devices_n
    local_channels = channels_n // cols_count
    combos = orders.shape[0] * orders.shape[1]
    feat_n = templates.shape[2]
    row_at = lax.axis_index("row")
    col_at = lax.axis_index("col")
    tail_frames = from_behind(frames[:, :3], "row", -1)
    padded = jnp.concatenate([frames, tail_frames], axis=1)
    column = jnp.arange(local_channels, dtype=jnp.int32)
    channel_ids = (column // per_device * cols_count + col_at) * per_device + column % per_device
    coefficients = channel_coefficients(channels_n, channel_ids)
    summed = jnp.zeros((sensors, 2 * local_channels, hop_dev), jnp.float32)
    for quarter in range(4):
        summed = summed + jnp.einsum(
            "shf,fk->skh",
            padded[:, quarter : quarter + hop_dev],
            coefficients[quarter * frame_len : (quarter + 1) * frame_len],
            preferred_element_type=jnp.float32,
        )
    hop_ids = row_at * hop_dev + jnp.arange(hop_dev, dtype=jnp.int32)
    real_part, imag_part = quarter_turn(
        summed[:, :local_channels], summed[:, local_channels:], channel_ids, hop_ids
    )
    demod = jnp.stack([real_part, imag_part]).astype(jnp.bfloat16)
    swapped = lax.all_to_all(demod, "row", split_axis=2, concat_axis=3, tiled=True)
    ordered = swapped.reshape(2, sensors, per_device, sub_n, RADIX).transpose(0, 1, 2, 4, 3)
    above = from_behind_2(ordered, ("row", "col"), -1)
    extended = jnp.concatenate([ordered, above], axis=2)
    own_real = ordered[0].astype(jnp.float32)
    own_imag = ordered[1].astype(jnp.float32)
    prod_real = []
    prod_imag = []
    for wheel in range(orders.shape[0]):
        for order_at in range(orders.shape[1]):
            partner = lax.dynamic_slice_in_dim(
                extended, orders[wheel, order_at], per_device, axis=2
            )
            partner = partner.astype(jnp.float32)
            prod_real.append(own_real * partner[0] + own_imag * partner[1])
            prod_imag.append(own_imag * partner[0] - own_real * partner[1])
    products = jnp.stack([jnp.stack(prod_real, axis=1), jnp.stack(prod_imag, axis=1)]).astype(
        jnp.bfloat16
    )
    table_sub = sub_coefficients(sub_n)
    spectrum, tiles = spectrum_call(
        products.reshape(2, sensors, combos, per_device * RADIX, sub_n), table_sub, hops_n
    )
    tiles_dev = sensors * combos * RADIX
    capacity = max(2, 2 * tiles_dev // devices_n)
    owner_ids = owners[:, 0]
    targets = jnp.arange(devices_n, dtype=jnp.int32)
    one_hot = (owner_ids[:, None] == targets[None, :]).astype(jnp.int32)
    before = jnp.cumsum(one_hot, axis=0) - one_hot
    slot_ids = jnp.sum(before * one_hot, axis=1)
    places = owner_ids * capacity + slot_ids
    slot_range = jnp.arange(devices_n * capacity, dtype=jnp.int32)
    placing = (places[None, :] == slot_range[:, None]).astype(jnp.bfloat16)
    outgoing = jnp.einsum("ot,tkq->okq", placing, tiles, preferred_element_type=jnp.float32)
    outgoing = outgoing.astype(jnp.bfloat16).reshape(devices_n, capacity * per_device, sub_n)
    arrived = lax.all_to_all(outgoing, ("row", "col"), split_axis=0, concat_axis=0, tiled=True)
    found = jnp.einsum(
        "tkq,qf->tkf", arrived, templates[0], preferred_element_type=jnp.float32
    ).astype(jnp.bfloat16)
    found = found.reshape(devices_n, capacity, per_device, feat_n)
    return (spectrum, found[None])


def solution(mesh):
    in_specs = (P(None, "row", None), P(), P(("row", "col"), None), P(("row", "col"), None, None))
    out_specs = (
        P(None, None, None, ("row", "col"), None),
        P(("row", "col"), None, None, None, None),
    )
    return jax.shard_map(shards, mesh=mesh, in_specs=in_specs, out_specs=out_specs, check_vma=False)
```

```python
import math

import jax
import jax.numpy as jnp
from jax import lax
from jax.experimental import pallas as pl
from jax.experimental.pallas import tpu as pltpu
from jax.sharding import PartitionSpec as P
import numpy as np

RADIX = 8


def from_behind(block, axis, distance):
    devices = range(lax.axis_size(axis))
    route = [(i - distance, i) for i in devices if i - distance in devices]
    return lax.ppermute(block, axis, route)


def from_behind_2(value, axis, steps):
    count = lax.axis_size(axis)
    pairs = [(source, (source + steps) % count) for source in range(count)]
    return lax.ppermute(value, axis, pairs)


def channel_coefficients(n_total, channel_ids):
    lanes = 128
    position = jnp.arange(n_total, dtype=jnp.int32)
    high = jnp.arange(n_total // lanes, dtype=jnp.int32) * lanes
    low = jnp.arange(lanes, dtype=jnp.int32)
    step = 2.0 * math.pi / n_total
    high_angle = step * (channel_ids[:, None] * high[None, :] % n_total).astype(jnp.float32)
    low_angle = step * (channel_ids[:, None] * low[None, :] % n_total).astype(jnp.float32)
    high_cos, high_sin = jnp.cos(high_angle)[:, :, None], jnp.sin(high_angle)[:, :, None]
    low_cos, low_sin = jnp.cos(low_angle)[:, None], jnp.sin(low_angle)[:, None]
    cos_part = (high_cos * low_cos - high_sin * low_sin).reshape(-1, n_total)
    sin_part = (high_sin * low_cos + high_cos * low_sin).reshape(-1, n_total)
    window = 0.5 - 0.5 * jnp.cos(step * position.astype(jnp.float32))
    gain_factor = math.sqrt(8.0 / (3.0 * n_total))
    weighted = gain_factor * window[None, :]
    both = jnp.concatenate([weighted * cos_part, weighted * sin_part], axis=0)
    return both.astype(jnp.bfloat16)


def sub_coefficients(sub_total):
    index_a = jnp.arange(sub_total, dtype=jnp.int32)
    turns = index_a[:, None] * index_a[None, :] % sub_total
    phase_angle = 2.0 * math.pi / sub_total * turns.astype(jnp.float32)
    return jnp.concatenate([jnp.cos(phase_angle), jnp.sin(phase_angle)], axis=1).astype(
        jnp.bfloat16
    )


def quarter_turn(a_cos, a_sin, channel_ids, hop_ids):
    phase_step = channel_ids[:, None] % 4 * (hop_ids[None, :] % 4) % 4
    cos_quarter = (phase_step == 0).astype(jnp.float32) - (phase_step == 2).astype(jnp.float32)
    sin_quarter = (phase_step == 1).astype(jnp.float32) - (phase_step == 3).astype(jnp.float32)
    real_part = a_cos * cos_quarter - a_sin * sin_quarter
    imag_part = -a_sin * cos_quarter - a_cos * sin_quarter
    return (real_part, imag_part)


def finish_transform(first_real, first_imag, hops_total):
    radix_count = first_real.shape[-2]
    sub_total = first_real.shape[-1]
    index_b = jnp.arange(radix_count, dtype=jnp.int32)[:, None]
    index_p = jnp.arange(sub_total, dtype=jnp.int32)[None, :]
    twist_angle = 2.0 * math.pi / hops_total * (index_b * index_p % hops_total).astype(jnp.float32)
    twist_cos = jnp.cos(twist_angle)
    twist_sin = jnp.sin(twist_angle)
    twist_real = first_real * twist_cos + first_imag * twist_sin
    twist_imag = first_imag * twist_cos - first_real * twist_sin
    index_d = jnp.arange(radix_count, dtype=jnp.int32)[None, :]
    section_angle = (
        2.0 * math.pi / radix_count * (index_b * index_d % radix_count).astype(jnp.float32)
    )
    section_cos = jnp.cos(section_angle)
    section_sin = jnp.sin(section_angle)
    highest = lax.Precision.HIGHEST
    norm_factor = 1.0 / math.sqrt(hops_total)
    out_real = norm_factor * (
        jnp.einsum("...bq,bd->...dq", twist_real, section_cos, precision=highest)
        + jnp.einsum("...bq,bd->...dq", twist_imag, section_sin, precision=highest)
    )
    out_imag = norm_factor * (
        jnp.einsum("...bq,bd->...dq", twist_imag, section_cos, precision=highest)
        - jnp.einsum("...bq,bd->...dq", twist_real, section_sin, precision=highest)
    )
    return (out_real, out_imag)


def section_mixers(radix_count, rows_per):
    index_b = np.arange(radix_count)
    angle = 2.0 * np.pi / radix_count * ((index_b[:, None] * index_b[None, :]) % radix_count)
    mixers = []
    for table in (np.cos(angle).astype(np.float32), np.sin(angle).astype(np.float32)):
        full = np.zeros((radix_count * rows_per, rows_per * radix_count), np.float32)
        for d in range(radix_count):
            for b in range(radix_count):
                for k in range(rows_per):
                    full[d * rows_per + k, k * radix_count + b] = table[b, d]
        high = jnp.asarray(full).astype(jnp.bfloat16)
        low = (jnp.asarray(full) - high.astype(jnp.float32)).astype(jnp.bfloat16)
        mixers += [high, low]
    return jnp.stack(mixers)


def spectrum_kernel(
    dest_ref, prod_ref, cos_ref, sin_ref, twc_ref, tws_ref, mix_ref, zero_ref, spec_ref, out_ref,
    feat_scratch,
):
    del dest_ref, zero_ref
    rows_per = out_ref.shape[1]
    sub_n = out_ref.shape[2]

    @pl.when(pl.program_id(1) == 0)
    def _():
        f32 = jnp.float32
        prod_real = prod_ref[0, 0]
        prod_imag = prod_ref[1, 0]
        sub_cos = cos_ref[...]
        sub_sin = sin_ref[...]
        first_real = jnp.dot(prod_real, sub_cos, preferred_element_type=f32) + jnp.dot(
            prod_imag, sub_sin, preferred_element_type=f32
        )
        first_imag = jnp.dot(prod_imag, sub_cos, preferred_element_type=f32) - jnp.dot(
            prod_real, sub_sin, preferred_element_type=f32
        )
        twist_cos = twc_ref[...]
        twist_sin = tws_ref[...]
        twist_real = first_real * twist_cos + first_imag * twist_sin
        twist_imag = first_imag * twist_cos - first_real * twist_sin

        def split(value):
            high = value.astype(jnp.bfloat16)
            return high, (value - high.astype(f32)).astype(jnp.bfloat16)

        real_high, real_low = split(twist_real)
        imag_high, imag_low = split(twist_imag)

        def mix(table, high, low):
            return jnp.dot(mix_ref[table], high, preferred_element_type=f32) + jnp.dot(
                mix_ref[table], low, preferred_element_type=f32
            )

        out_real = mix(0, real_high, real_low) + mix(2, imag_high, imag_low)
        out_imag = mix(0, imag_high, imag_low) - mix(2, real_high, real_low)
        feat_scratch[...] = jnp.log1p(out_real * out_real + out_imag * out_imag).astype(
            feat_scratch.dtype
        )
        for d in range(RADIX):
            rows = slice(d * rows_per, (d + 1) * rows_per)
            lanes = slice(d * sub_n, (d + 1) * sub_n)
            spec_ref[0, 0, 0, :, lanes] = out_real[rows].astype(spec_ref.dtype)
            spec_ref[1, 0, 0, :, lanes] = out_imag[rows].astype(spec_ref.dtype)

    start = pl.multiple_of(pl.program_id(1) * rows_per, rows_per)
    out_ref[0] = feat_scratch[pl.ds(start, rows_per), :]


def spectrum_call(products, table_sub, hops_total, dest, slots):
    _, sensors, combos, rows, sub_n = products.shape
    per_device = rows // RADIX
    blocks = sensors * combos
    flat = products.reshape(2, blocks, rows, sub_n)
    index_b = jnp.arange(RADIX, dtype=jnp.int32)[:, None]
    index_p = jnp.arange(sub_n, dtype=jnp.int32)[None, :]
    twist_angle = 2.0 * math.pi / hops_total * (index_b * index_p % hops_total).astype(jnp.float32)
    norm_factor = 1.0 / math.sqrt(hops_total)
    twist_cos = jnp.tile(norm_factor * jnp.cos(twist_angle), (per_device, 1))
    twist_sin = jnp.tile(norm_factor * jnp.sin(twist_angle), (per_device, 1))
    mixers = section_mixers(RADIX, per_device)
    zeros = jnp.zeros((slots, per_device, sub_n), jnp.bfloat16)
    grid_spec = pltpu.PrefetchScalarGridSpec(
        num_scalar_prefetch=1,
        grid=(blocks, RADIX),
        in_specs=[
            pl.BlockSpec((2, 1, rows, sub_n), lambda i, d, dest: (0, i, 0, 0)),
            pl.BlockSpec((sub_n, sub_n), lambda i, d, dest: (0, 0)),
            pl.BlockSpec((sub_n, sub_n), lambda i, d, dest: (0, 1)),
            pl.BlockSpec((rows, sub_n), lambda i, d, dest: (0, 0)),
            pl.BlockSpec((rows, sub_n), lambda i, d, dest: (0, 0)),
            pl.BlockSpec((4, rows, rows), lambda i, d, dest: (0, 0, 0)),
            pl.BlockSpec(memory_space=pl.ANY),
        ],
        out_specs=[
            pl.BlockSpec(
                (2, 1, 1, per_device, RADIX * sub_n),
                lambda i, d, dest: (0, i // combos, i % combos, 0, 0),
            ),
            pl.BlockSpec((1, per_device, sub_n), lambda i, d, dest: (dest[i * RADIX + d], 0, 0)),
        ],
        scratch_shapes=[pltpu.VMEM((rows, sub_n), jnp.bfloat16)],
    )
    spectrum, outgoing = pl.pallas_call(
        spectrum_kernel,
        grid_spec=grid_spec,
        out_shape=[
            jax.ShapeDtypeStruct((2, sensors, combos, per_device, RADIX * sub_n), jnp.bfloat16),
            jax.ShapeDtypeStruct((slots, per_device, sub_n), jnp.bfloat16),
        ],
        input_output_aliases={7: 1},
        compiler_params=pltpu.CompilerParams(
            vmem_limit_bytes=48 * 1024 * 1024,
            dimension_semantics=("arbitrary", "arbitrary"),
        ),
        cost_estimate=pl.CostEstimate(
            flops=blocks * (8 * rows * sub_n * sub_n + 16 * rows * rows * sub_n),
            transcendentals=blocks * rows * sub_n,
            bytes_accessed=blocks * rows * sub_n * 2 * 5 + 4 * sub_n * sub_n,
        ),
    )(dest, flat, table_sub, table_sub, twist_cos, twist_sin, mixers, zeros)
    return spectrum, outgoing


def shards(frames, orders, owners, templates):
    rows_count = lax.axis_size("row")
    cols_count = lax.axis_size("col")
    devices_n = rows_count * cols_count
    sensors = frames.shape[0]
    hop_dev = frames.shape[1]
    frame_len = frames.shape[2]
    channels_n = 4 * frame_len
    hops_n = hop_dev * rows_count
    sub_n = hops_n // RADIX
    per_device = channels_n // devices_n
    local_channels = channels_n // cols_count
    combos = orders.shape[0] * orders.shape[1]
    feat_n = templates.shape[2]
    row_at = lax.axis_index("row")
    col_at = lax.axis_index("col")
    tail_frames = from_behind(frames[:, :3], "row", -1)
    padded = jnp.concatenate([frames, tail_frames], axis=1)
    column = jnp.arange(local_channels, dtype=jnp.int32)
    channel_ids = (column // per_device * cols_count + col_at) * per_device + column % per_device
    coefficients = channel_coefficients(channels_n, channel_ids)
    summed = jnp.zeros((sensors, 2 * local_channels, hop_dev), jnp.float32)
    for quarter in range(4):
        summed = summed + jnp.einsum(
            "shf,kf->skh",
            padded[:, quarter : quarter + hop_dev],
            coefficients[:, quarter * frame_len : (quarter + 1) * frame_len],
            preferred_element_type=jnp.float32,
        )
    hop_ids = row_at * hop_dev + jnp.arange(hop_dev, dtype=jnp.int32)
    real_part, imag_part = quarter_turn(
        summed[:, :local_channels], summed[:, local_channels:], channel_ids, hop_ids
    )
    demod = jnp.stack([real_part, imag_part]).astype(jnp.bfloat16)
    demod = demod.reshape(2, sensors, rows_count, per_device, hop_dev).transpose(2, 0, 1, 3, 4)
    swapped = lax.all_to_all(demod, "row", split_axis=0, concat_axis=0, tiled=True)
    ordered = swapped.reshape(
        rows_count, 2, sensors, per_device, hop_dev // RADIX, RADIX
    ).transpose(1, 2, 3, 5, 0, 4)
    ordered = ordered.reshape(2, sensors, per_device, RADIX, sub_n)
    above = from_behind_2(ordered, ("row", "col"), -1)
    extended = jnp.concatenate([ordered, above], axis=2)
    own_real = ordered[0].astype(jnp.float32)
    own_imag = ordered[1].astype(jnp.float32)
    prod_real = []
    prod_imag = []
    for wheel in range(orders.shape[0]):
        for order_at in range(orders.shape[1]):
            partner = lax.dynamic_slice_in_dim(
                extended, orders[wheel, order_at], per_device, axis=2
            )
            partner = partner.astype(jnp.float32)
            prod_real.append(own_real * partner[0] + own_imag * partner[1])
            prod_imag.append(own_imag * partner[0] - own_real * partner[1])
    products = jnp.stack([jnp.stack(prod_real, axis=1), jnp.stack(prod_imag, axis=1)]).astype(
        jnp.bfloat16
    )
    tiles_dev = sensors * combos * RADIX
    capacity = max(2, 2 * tiles_dev // devices_n)
    owner_ids = owners[:, 0]
    targets = jnp.arange(devices_n, dtype=jnp.int32)
    one_hot = (owner_ids[:, None] == targets[None, :]).astype(jnp.int32)
    before = jnp.cumsum(one_hot, axis=0) - one_hot
    slot_ids = jnp.sum(before * one_hot, axis=1)
    places = owner_ids * capacity + slot_ids
    table_sub = sub_coefficients(sub_n)
    spectrum, outgoing = spectrum_call(
        products.reshape(2, sensors, combos, per_device * RADIX, sub_n),
        table_sub,
        hops_n,
        places,
        devices_n * capacity,
    )
    outgoing = outgoing.reshape(devices_n, capacity * per_device, sub_n)
    arrived = lax.all_to_all(outgoing, ("row", "col"), split_axis=0, concat_axis=0, tiled=True)
    found = jnp.dot(
        arrived.reshape(-1, sub_n), templates[0], preferred_element_type=jnp.float32
    ).astype(jnp.bfloat16)
    found = found.reshape(devices_n, capacity, per_device, feat_n)
    return (spectrum, found[None])


def solution(mesh):
    in_specs = (P(None, "row", None), P(), P(("row", "col"), None), P(("row", "col"), None, None))
    out_specs = (
        P(None, None, None, ("row", "col"), None),
        P(("row", "col"), None, None, None, None),
    )
    return jax.shard_map(shards, mesh=mesh, in_specs=in_specs, out_specs=out_specs, check_vma=False)
```

```python
import math

import jax
import jax.numpy as jnp
from jax import lax
from jax.experimental import pallas as pl
from jax.experimental.pallas import tpu as pltpu
from jax.sharding import PartitionSpec as P
import numpy as np

RADIX = 8


def from_behind(block, axis, distance):
    devices = range(lax.axis_size(axis))
    route = [(i - distance, i) for i in devices if i - distance in devices]
    return lax.ppermute(block, axis, route)


def from_behind_2(value, axis, steps):
    count = lax.axis_size(axis)
    pairs = [(source, (source + steps) % count) for source in range(count)]
    return lax.ppermute(value, axis, pairs)


def channel_coefficients(n_total, channel_ids):
    lanes = 128
    position = jnp.arange(n_total, dtype=jnp.int32)
    high = jnp.arange(n_total // lanes, dtype=jnp.int32) * lanes
    low = jnp.arange(lanes, dtype=jnp.int32)
    step = 2.0 * math.pi / n_total
    high_angle = step * (channel_ids[:, None] * high[None, :] % n_total).astype(jnp.float32)
    low_angle = step * (channel_ids[:, None] * low[None, :] % n_total).astype(jnp.float32)
    high_cos, high_sin = jnp.cos(high_angle)[:, :, None], jnp.sin(high_angle)[:, :, None]
    low_cos, low_sin = jnp.cos(low_angle)[:, None], jnp.sin(low_angle)[:, None]
    cos_part = (high_cos * low_cos - high_sin * low_sin).reshape(-1, n_total)
    sin_part = (high_sin * low_cos + high_cos * low_sin).reshape(-1, n_total)
    window = 0.5 - 0.5 * jnp.cos(step * position.astype(jnp.float32))
    gain_factor = math.sqrt(8.0 / (3.0 * n_total))
    weighted = gain_factor * window[None, :]
    both = jnp.concatenate([weighted * cos_part, weighted * sin_part], axis=0)
    return both.astype(jnp.bfloat16)


def sub_coefficients(sub_total):
    index_a = jnp.arange(sub_total, dtype=jnp.int32)
    turns = index_a[:, None] * index_a[None, :] % sub_total
    phase_angle = 2.0 * math.pi / sub_total * turns.astype(jnp.float32)
    return jnp.concatenate([jnp.cos(phase_angle), jnp.sin(phase_angle)], axis=1).astype(
        jnp.bfloat16
    )


def quarter_turn(a_cos, a_sin, channel_ids, hop_ids):
    phase_step = channel_ids[:, None] % 4 * (hop_ids[None, :] % 4) % 4
    cos_quarter = (phase_step == 0).astype(jnp.float32) - (phase_step == 2).astype(jnp.float32)
    sin_quarter = (phase_step == 1).astype(jnp.float32) - (phase_step == 3).astype(jnp.float32)
    real_part = a_cos * cos_quarter - a_sin * sin_quarter
    imag_part = -a_sin * cos_quarter - a_cos * sin_quarter
    return (real_part, imag_part)


def finish_transform(first_real, first_imag, hops_total):
    radix_count = first_real.shape[-2]
    sub_total = first_real.shape[-1]
    index_b = jnp.arange(radix_count, dtype=jnp.int32)[:, None]
    index_p = jnp.arange(sub_total, dtype=jnp.int32)[None, :]
    twist_angle = 2.0 * math.pi / hops_total * (index_b * index_p % hops_total).astype(jnp.float32)
    twist_cos = jnp.cos(twist_angle)
    twist_sin = jnp.sin(twist_angle)
    twist_real = first_real * twist_cos + first_imag * twist_sin
    twist_imag = first_imag * twist_cos - first_real * twist_sin
    index_d = jnp.arange(radix_count, dtype=jnp.int32)[None, :]
    section_angle = (
        2.0 * math.pi / radix_count * (index_b * index_d % radix_count).astype(jnp.float32)
    )
    section_cos = jnp.cos(section_angle)
    section_sin = jnp.sin(section_angle)
    highest = lax.Precision.HIGHEST
    norm_factor = 1.0 / math.sqrt(hops_total)
    out_real = norm_factor * (
        jnp.einsum("...bq,bd->...dq", twist_real, section_cos, precision=highest)
        + jnp.einsum("...bq,bd->...dq", twist_imag, section_sin, precision=highest)
    )
    out_imag = norm_factor * (
        jnp.einsum("...bq,bd->...dq", twist_imag, section_cos, precision=highest)
        - jnp.einsum("...bq,bd->...dq", twist_real, section_sin, precision=highest)
    )
    return (out_real, out_imag)


def section_mixers(radix_count, rows_per):
    index_b = np.arange(radix_count)
    angle = 2.0 * np.pi / radix_count * ((index_b[:, None] * index_b[None, :]) % radix_count)
    mixers = []
    for table in (np.cos(angle).astype(np.float32), np.sin(angle).astype(np.float32)):
        full = np.zeros((radix_count * rows_per, rows_per * radix_count), np.float32)
        for d in range(radix_count):
            for b in range(radix_count):
                for k in range(rows_per):
                    full[d * rows_per + k, k * radix_count + b] = table[b, d]
        high = jnp.asarray(full).astype(jnp.bfloat16)
        low = (jnp.asarray(full) - high.astype(jnp.float32)).astype(jnp.bfloat16)
        mixers += [high, low]
    return jnp.stack(mixers)


def spectrum_kernel(
    dest_ref, prod_ref, cos_ref, sin_ref, twc_ref, tws_ref, mix_ref, zero_ref, spec_ref, out_ref,
    feat_scratch, sems,
):
    del zero_ref
    f32 = jnp.float32
    block = pl.program_id(0)
    rows_per = feat_scratch.shape[1]
    sub_n = feat_scratch.shape[2]
    prod_real = prod_ref[0, 0]
    prod_imag = prod_ref[1, 0]
    sub_cos = cos_ref[...]
    sub_sin = sin_ref[...]
    first_real = jnp.dot(prod_real, sub_cos, preferred_element_type=f32) + jnp.dot(
        prod_imag, sub_sin, preferred_element_type=f32
    )
    first_imag = jnp.dot(prod_imag, sub_cos, preferred_element_type=f32) - jnp.dot(
        prod_real, sub_sin, preferred_element_type=f32
    )
    twist_cos = twc_ref[...]
    twist_sin = tws_ref[...]
    twist_real = first_real * twist_cos + first_imag * twist_sin
    twist_imag = first_imag * twist_cos - first_real * twist_sin

    def split(value):
        high = value.astype(jnp.bfloat16)
        return high, (value - high.astype(f32)).astype(jnp.bfloat16)

    real_high, real_low = split(twist_real)
    imag_high, imag_low = split(twist_imag)

    def mix(table, high, low):
        return jnp.dot(mix_ref[table], high, preferred_element_type=f32) + jnp.dot(
            mix_ref[table], low, preferred_element_type=f32
        )

    out_real = mix(0, real_high, real_low) + mix(2, imag_high, imag_low)
    out_imag = mix(0, imag_high, imag_low) - mix(2, real_high, real_low)
    feature = jnp.log1p(out_real * out_real + out_imag * out_imag).astype(feat_scratch.dtype)
    for d in range(RADIX):
        rows = slice(d * rows_per, (d + 1) * rows_per)
        lanes = slice(d * sub_n, (d + 1) * sub_n)
        spec_ref[0, 0, 0, :, lanes] = out_real[rows].astype(spec_ref.dtype)
        spec_ref[1, 0, 0, :, lanes] = out_imag[rows].astype(spec_ref.dtype)

    def tile_copy(step, d):
        return pltpu.make_async_copy(
            feat_scratch.at[d], out_ref.at[dest_ref[step * RADIX + d]], sems.at[d]
        )

    @pl.when(block > 0)
    def _():
        for d in range(RADIX):
            tile_copy(block - 1, d).wait()

    for d in range(RADIX):
        feat_scratch[d] = feature[d * rows_per : (d + 1) * rows_per]
    for d in range(RADIX):
        tile_copy(block, d).start()

    @pl.when(block == pl.num_programs(0) - 1)
    def _():
        for d in range(RADIX):
            tile_copy(block, d).wait()


def spectrum_call(products, table_sub, hops_total, dest, slots):
    _, sensors, combos, rows, sub_n = products.shape
    per_device = rows // RADIX
    blocks = sensors * combos
    flat = products.reshape(2, blocks, rows, sub_n)
    index_b = jnp.arange(RADIX, dtype=jnp.int32)[:, None]
    index_p = jnp.arange(sub_n, dtype=jnp.int32)[None, :]
    twist_angle = 2.0 * math.pi / hops_total * (index_b * index_p % hops_total).astype(jnp.float32)
    norm_factor = 1.0 / math.sqrt(hops_total)
    twist_cos = jnp.tile(norm_factor * jnp.cos(twist_angle), (per_device, 1))
    twist_sin = jnp.tile(norm_factor * jnp.sin(twist_angle), (per_device, 1))
    mixers = section_mixers(RADIX, per_device)
    zeros = jnp.zeros((slots, per_device, sub_n), jnp.bfloat16)
    grid_spec = pltpu.PrefetchScalarGridSpec(
        num_scalar_prefetch=1,
        grid=(blocks,),
        in_specs=[
            pl.BlockSpec((2, 1, rows, sub_n), lambda i, dest: (0, i, 0, 0)),
            pl.BlockSpec((sub_n, sub_n), lambda i, dest: (0, 0)),
            pl.BlockSpec((sub_n, sub_n), lambda i, dest: (0, 1)),
            pl.BlockSpec((rows, sub_n), lambda i, dest: (0, 0)),
            pl.BlockSpec((rows, sub_n), lambda i, dest: (0, 0)),
            pl.BlockSpec((4, rows, rows), lambda i, dest: (0, 0, 0)),
            pl.BlockSpec(memory_space=pl.ANY),
        ],
        out_specs=[
            pl.BlockSpec(
                (2, 1, 1, per_device, RADIX * sub_n),
                lambda i, dest: (0, i // combos, i % combos, 0, 0),
            ),
            pl.BlockSpec(memory_space=pl.ANY),
        ],
        scratch_shapes=[
            pltpu.VMEM((RADIX, per_device, sub_n), jnp.bfloat16),
            pltpu.SemaphoreType.DMA((RADIX,)),
        ],
    )
    spectrum, outgoing = pl.pallas_call(
        spectrum_kernel,
        grid_spec=grid_spec,
        out_shape=[
            jax.ShapeDtypeStruct((2, sensors, combos, per_device, RADIX * sub_n), jnp.bfloat16),
            jax.ShapeDtypeStruct((slots, per_device, sub_n), jnp.bfloat16),
        ],
        input_output_aliases={7: 1},
        compiler_params=pltpu.CompilerParams(
            vmem_limit_bytes=48 * 1024 * 1024,
            dimension_semantics=("arbitrary",),
        ),
        cost_estimate=pl.CostEstimate(
            flops=blocks * (8 * rows * sub_n * sub_n + 16 * rows * rows * sub_n),
            transcendentals=blocks * rows * sub_n,
            bytes_accessed=blocks * rows * sub_n * 2 * 5 + 4 * sub_n * sub_n,
        ),
    )(dest, flat, table_sub, table_sub, twist_cos, twist_sin, mixers, zeros)
    return spectrum, outgoing


def shards(frames, orders, owners, templates):
    rows_count = lax.axis_size("row")
    cols_count = lax.axis_size("col")
    devices_n = rows_count * cols_count
    sensors = frames.shape[0]
    hop_dev = frames.shape[1]
    frame_len = frames.shape[2]
    channels_n = 4 * frame_len
    hops_n = hop_dev * rows_count
    sub_n = hops_n // RADIX
    per_device = channels_n // devices_n
    local_channels = channels_n // cols_count
    combos = orders.shape[0] * orders.shape[1]
    feat_n = templates.shape[2]
    row_at = lax.axis_index("row")
    col_at = lax.axis_index("col")
    tail_frames = from_behind(frames[:, :3], "row", -1)
    padded = jnp.concatenate([frames, tail_frames], axis=1)
    column = jnp.arange(local_channels, dtype=jnp.int32)
    channel_ids = (column // per_device * cols_count + col_at) * per_device + column % per_device
    coefficients = channel_coefficients(channels_n, channel_ids)
    summed = jnp.zeros((sensors, 2 * local_channels, hop_dev), jnp.float32)
    for quarter in range(4):
        summed = summed + jnp.einsum(
            "shf,kf->skh",
            padded[:, quarter : quarter + hop_dev],
            coefficients[:, quarter * frame_len : (quarter + 1) * frame_len],
            preferred_element_type=jnp.float32,
        )
    hop_ids = row_at * hop_dev + jnp.arange(hop_dev, dtype=jnp.int32)
    real_part, imag_part = quarter_turn(
        summed[:, :local_channels], summed[:, local_channels:], channel_ids, hop_ids
    )
    demod = jnp.stack([real_part, imag_part]).astype(jnp.bfloat16)
    swapped = lax.all_to_all(demod, "row", split_axis=2, concat_axis=3, tiled=True)
    ordered = swapped.reshape(2, sensors, per_device, sub_n, RADIX).transpose(0, 1, 2, 4, 3)
    above = from_behind_2(ordered, ("row", "col"), -1)
    extended = jnp.concatenate([ordered, above], axis=2)
    own_real = ordered[0].astype(jnp.float32)
    own_imag = ordered[1].astype(jnp.float32)
    prod_real = []
    prod_imag = []
    for wheel in range(orders.shape[0]):
        for order_at in range(orders.shape[1]):
            partner = lax.dynamic_slice_in_dim(
                extended, orders[wheel, order_at], per_device, axis=2
            )
            partner = partner.astype(jnp.float32)
            prod_real.append(own_real * partner[0] + own_imag * partner[1])
            prod_imag.append(own_imag * partner[0] - own_real * partner[1])
    products = jnp.stack([jnp.stack(prod_real, axis=1), jnp.stack(prod_imag, axis=1)]).astype(
        jnp.bfloat16
    )
    tiles_dev = sensors * combos * RADIX
    capacity = max(2, 2 * tiles_dev // devices_n)
    owner_ids = owners[:, 0]
    targets = jnp.arange(devices_n, dtype=jnp.int32)
    one_hot = (owner_ids[:, None] == targets[None, :]).astype(jnp.int32)
    before = jnp.cumsum(one_hot, axis=0) - one_hot
    slot_ids = jnp.sum(before * one_hot, axis=1)
    places = owner_ids * capacity + slot_ids
    table_sub = sub_coefficients(sub_n)
    spectrum, outgoing = spectrum_call(
        products.reshape(2, sensors, combos, per_device * RADIX, sub_n),
        table_sub,
        hops_n,
        places,
        devices_n * capacity,
    )
    outgoing = outgoing.reshape(devices_n, capacity * per_device, sub_n)
    arrived = lax.all_to_all(outgoing, ("row", "col"), split_axis=0, concat_axis=0, tiled=True)
    found = jnp.dot(
        arrived.reshape(-1, sub_n), templates[0], preferred_element_type=jnp.float32
    ).astype(jnp.bfloat16)
    found = found.reshape(devices_n, capacity, per_device, feat_n)
    return (spectrum, found[None])


def solution(mesh):
    in_specs = (P(None, "row", None), P(), P(("row", "col"), None), P(("row", "col"), None, None))
    out_specs = (
        P(None, None, None, ("row", "col"), None),
        P(("row", "col"), None, None, None, None),
    )
    return jax.shard_map(shards, mesh=mesh, in_specs=in_specs, out_specs=out_specs, check_vma=False)
```

```python
import math

import jax
import jax.numpy as jnp
from jax import lax
from jax.experimental import pallas as pl
from jax.experimental.pallas import tpu as pltpu
from jax.sharding import PartitionSpec as P
import numpy as np

RADIX = 8


def from_behind(block, axis, distance):
    devices = range(lax.axis_size(axis))
    route = [(i - distance, i) for i in devices if i - distance in devices]
    return lax.ppermute(block, axis, route)


def from_behind_2(value, axis, steps):
    count = lax.axis_size(axis)
    pairs = [(source, (source + steps) % count) for source in range(count)]
    return lax.ppermute(value, axis, pairs)


def channel_coefficients(n_total, channel_ids):
    lanes = 128
    position = jnp.arange(n_total, dtype=jnp.int32)
    high = jnp.arange(n_total // lanes, dtype=jnp.int32) * lanes
    low = jnp.arange(lanes, dtype=jnp.int32)
    step = 2.0 * math.pi / n_total
    high_angle = step * (channel_ids[:, None] * high[None, :] % n_total).astype(jnp.float32)
    low_angle = step * (channel_ids[:, None] * low[None, :] % n_total).astype(jnp.float32)
    high_cos, high_sin = jnp.cos(high_angle)[:, :, None], jnp.sin(high_angle)[:, :, None]
    low_cos, low_sin = jnp.cos(low_angle)[:, None], jnp.sin(low_angle)[:, None]
    cos_part = (high_cos * low_cos - high_sin * low_sin).reshape(-1, n_total)
    sin_part = (high_sin * low_cos + high_cos * low_sin).reshape(-1, n_total)
    window = 0.5 - 0.5 * jnp.cos(step * position.astype(jnp.float32))
    gain_factor = math.sqrt(8.0 / (3.0 * n_total))
    weighted = gain_factor * window[None, :]
    both = jnp.concatenate([weighted * cos_part, weighted * sin_part], axis=0)
    return both.astype(jnp.bfloat16)


def sub_coefficients(sub_total):
    index_a = jnp.arange(sub_total, dtype=jnp.int32)
    turns = index_a[:, None] * index_a[None, :] % sub_total
    phase_angle = 2.0 * math.pi / sub_total * turns.astype(jnp.float32)
    return jnp.concatenate([jnp.cos(phase_angle), jnp.sin(phase_angle)], axis=1).astype(
        jnp.bfloat16
    )


def quarter_turn(a_cos, a_sin, channel_ids, hop_ids):
    phase_step = channel_ids[:, None] % 4 * (hop_ids[None, :] % 4) % 4
    cos_quarter = (phase_step == 0).astype(jnp.float32) - (phase_step == 2).astype(jnp.float32)
    sin_quarter = (phase_step == 1).astype(jnp.float32) - (phase_step == 3).astype(jnp.float32)
    real_part = a_cos * cos_quarter - a_sin * sin_quarter
    imag_part = -a_sin * cos_quarter - a_cos * sin_quarter
    return (real_part, imag_part)


def finish_transform(first_real, first_imag, hops_total):
    radix_count = first_real.shape[-2]
    sub_total = first_real.shape[-1]
    index_b = jnp.arange(radix_count, dtype=jnp.int32)[:, None]
    index_p = jnp.arange(sub_total, dtype=jnp.int32)[None, :]
    twist_angle = 2.0 * math.pi / hops_total * (index_b * index_p % hops_total).astype(jnp.float32)
    twist_cos = jnp.cos(twist_angle)
    twist_sin = jnp.sin(twist_angle)
    twist_real = first_real * twist_cos + first_imag * twist_sin
    twist_imag = first_imag * twist_cos - first_real * twist_sin
    index_d = jnp.arange(radix_count, dtype=jnp.int32)[None, :]
    section_angle = (
        2.0 * math.pi / radix_count * (index_b * index_d % radix_count).astype(jnp.float32)
    )
    section_cos = jnp.cos(section_angle)
    section_sin = jnp.sin(section_angle)
    highest = lax.Precision.HIGHEST
    norm_factor = 1.0 / math.sqrt(hops_total)
    out_real = norm_factor * (
        jnp.einsum("...bq,bd->...dq", twist_real, section_cos, precision=highest)
        + jnp.einsum("...bq,bd->...dq", twist_imag, section_sin, precision=highest)
    )
    out_imag = norm_factor * (
        jnp.einsum("...bq,bd->...dq", twist_imag, section_cos, precision=highest)
        - jnp.einsum("...bq,bd->...dq", twist_real, section_sin, precision=highest)
    )
    return (out_real, out_imag)


def section_mixers(radix_count, rows_per):
    index_b = np.arange(radix_count)
    angle = 2.0 * np.pi / radix_count * ((index_b[:, None] * index_b[None, :]) % radix_count)
    mixers = []
    for table in (np.cos(angle).astype(np.float32), np.sin(angle).astype(np.float32)):
        full = np.zeros((radix_count * rows_per, rows_per * radix_count), np.float32)
        for d in range(radix_count):
            for b in range(radix_count):
                for k in range(rows_per):
                    full[d * rows_per + k, k * radix_count + b] = table[b, d]
        high = jnp.asarray(full).astype(jnp.bfloat16)
        low = (jnp.asarray(full) - high.astype(jnp.float32)).astype(jnp.bfloat16)
        mixers += [high, low]
    return jnp.stack(mixers)


def spectrum_kernel(dest_ref, prod_ref, cos_ref, sin_ref, twc_ref, tws_ref, mix_ref, *refs):
    spec_ref, out_ref, feat_scratch, sems = refs[-4:]
    f32 = jnp.float32
    block = pl.program_id(0)
    rows_per = feat_scratch.shape[1]
    sub_n = feat_scratch.shape[2]
    prod_real = prod_ref[0, 0]
    prod_imag = prod_ref[1, 0]
    sub_cos = cos_ref[...]
    sub_sin = sin_ref[...]
    first_real = jnp.dot(prod_real, sub_cos, preferred_element_type=f32) + jnp.dot(
        prod_imag, sub_sin, preferred_element_type=f32
    )
    first_imag = jnp.dot(prod_imag, sub_cos, preferred_element_type=f32) - jnp.dot(
        prod_real, sub_sin, preferred_element_type=f32
    )
    twist_cos = twc_ref[...]
    twist_sin = tws_ref[...]
    twist_real = first_real * twist_cos + first_imag * twist_sin
    twist_imag = first_imag * twist_cos - first_real * twist_sin

    def split(value):
        high = value.astype(jnp.bfloat16)
        return high, (value - high.astype(f32)).astype(jnp.bfloat16)

    real_high, real_low = split(twist_real)
    imag_high, imag_low = split(twist_imag)

    def mix(table, high, low):
        return jnp.dot(mix_ref[table], high, preferred_element_type=f32) + jnp.dot(
            mix_ref[table], low, preferred_element_type=f32
        )

    out_real = mix(0, real_high, real_low) + mix(2, imag_high, imag_low)
    out_imag = mix(0, imag_high, imag_low) - mix(2, real_high, real_low)
    feature = jnp.log1p(out_real * out_real + out_imag * out_imag).astype(feat_scratch.dtype)
    for d in range(RADIX):
        rows = slice(d * rows_per, (d + 1) * rows_per)
        lanes = slice(d * sub_n, (d + 1) * sub_n)
        spec_ref[0, 0, 0, :, lanes] = out_real[rows].astype(spec_ref.dtype)
        spec_ref[1, 0, 0, :, lanes] = out_imag[rows].astype(spec_ref.dtype)

    def tile_copy(step, d):
        return pltpu.make_async_copy(
            feat_scratch.at[d], out_ref.at[dest_ref[step * RADIX + d]], sems.at[d]
        )

    @pl.when(block > 0)
    def _():
        for d in range(RADIX):
            tile_copy(block - 1, d).wait()

    for d in range(RADIX):
        feat_scratch[d] = feature[d * rows_per : (d + 1) * rows_per]
    for d in range(RADIX):
        tile_copy(block, d).start()

    @pl.when(block == pl.num_programs(0) - 1)
    def _():
        for d in range(RADIX):
            tile_copy(block, d).wait()


def spectrum_call(products, table_sub, hops_total, dest, outgoing, spectrum, first_block, sensors):
    _, _, combos, rows, sub_n = products.shape
    per_device = rows // RADIX
    blocks = products.shape[1] * combos
    flat = products.reshape(2, blocks, rows, sub_n)
    index_b = jnp.arange(RADIX, dtype=jnp.int32)[:, None]
    index_p = jnp.arange(sub_n, dtype=jnp.int32)[None, :]
    twist_angle = 2.0 * math.pi / hops_total * (index_b * index_p % hops_total).astype(jnp.float32)
    norm_factor = 1.0 / math.sqrt(hops_total)
    twist_cos = jnp.tile(norm_factor * jnp.cos(twist_angle), (per_device, 1))
    twist_sin = jnp.tile(norm_factor * jnp.sin(twist_angle), (per_device, 1))
    mixers = section_mixers(RADIX, per_device)
    operands = [dest, flat, table_sub, table_sub, twist_cos, twist_sin, mixers, outgoing]
    in_specs = [
        pl.BlockSpec((2, 1, rows, sub_n), lambda i, dest: (0, i, 0, 0)),
        pl.BlockSpec((sub_n, sub_n), lambda i, dest: (0, 0)),
        pl.BlockSpec((sub_n, sub_n), lambda i, dest: (0, 1)),
        pl.BlockSpec((rows, sub_n), lambda i, dest: (0, 0)),
        pl.BlockSpec((rows, sub_n), lambda i, dest: (0, 0)),
        pl.BlockSpec((4, rows, rows), lambda i, dest: (0, 0, 0)),
        pl.BlockSpec(memory_space=pl.ANY),
    ]
    aliases = {7: 1}
    if spectrum is not None:
        operands.append(spectrum)
        in_specs.append(pl.BlockSpec(memory_space=pl.ANY))
        aliases[8] = 0
    spec_shape = (2, sensors, combos, per_device, RADIX * sub_n)
    grid_spec = pltpu.PrefetchScalarGridSpec(
        num_scalar_prefetch=1,
        grid=(blocks,),
        in_specs=in_specs,
        out_specs=[
            pl.BlockSpec(
                (2, 1, 1, per_device, RADIX * sub_n),
                lambda i, dest: (0, (i + first_block) // combos, (i + first_block) % combos, 0, 0),
            ),
            pl.BlockSpec(memory_space=pl.ANY),
        ],
        scratch_shapes=[
            pltpu.VMEM((RADIX, per_device, sub_n), jnp.bfloat16),
            pltpu.SemaphoreType.DMA((RADIX,)),
        ],
    )
    return pl.pallas_call(
        spectrum_kernel,
        grid_spec=grid_spec,
        out_shape=[
            jax.ShapeDtypeStruct(spec_shape, jnp.bfloat16),
            jax.ShapeDtypeStruct(outgoing.shape, jnp.bfloat16),
        ],
        input_output_aliases=aliases,
        compiler_params=pltpu.CompilerParams(
            vmem_limit_bytes=48 * 1024 * 1024,
            dimension_semantics=("arbitrary",),
        ),
        cost_estimate=pl.CostEstimate(
            flops=blocks * (8 * rows * sub_n * sub_n + 16 * rows * rows * sub_n),
            transcendentals=blocks * rows * sub_n,
            bytes_accessed=blocks * rows * sub_n * 2 * 5 + 4 * sub_n * sub_n,
        ),
    )(*operands)


def shards(frames, orders, owners, templates):
    rows_count = lax.axis_size("row")
    cols_count = lax.axis_size("col")
    devices_n = rows_count * cols_count
    sensors = frames.shape[0]
    hop_dev = frames.shape[1]
    frame_len = frames.shape[2]
    channels_n = 4 * frame_len
    hops_n = hop_dev * rows_count
    sub_n = hops_n // RADIX
    per_device = channels_n // devices_n
    local_channels = channels_n // cols_count
    combos = orders.shape[0] * orders.shape[1]
    feat_n = templates.shape[2]
    row_at = lax.axis_index("row")
    col_at = lax.axis_index("col")
    tail_frames = from_behind(frames[:, :3], "row", -1)
    padded_all = jnp.concatenate([frames, tail_frames], axis=1)
    column = jnp.arange(local_channels, dtype=jnp.int32)
    channel_ids = (column // per_device * cols_count + col_at) * per_device + column % per_device
    coefficients = channel_coefficients(channels_n, channel_ids)

    def front(padded):
        sensors = padded.shape[0]
        summed = jnp.zeros((sensors, 2 * local_channels, hop_dev), jnp.float32)
        for quarter in range(4):
            summed = summed + jnp.einsum(
                "shf,kf->skh",
                padded[:, quarter : quarter + hop_dev],
                coefficients[:, quarter * frame_len : (quarter + 1) * frame_len],
                preferred_element_type=jnp.float32,
            )
        hop_ids = row_at * hop_dev + jnp.arange(hop_dev, dtype=jnp.int32)
        real_part, imag_part = quarter_turn(
            summed[:, :local_channels], summed[:, local_channels:], channel_ids, hop_ids
        )
        demod = jnp.stack([real_part, imag_part]).astype(jnp.bfloat16)
        swapped = lax.all_to_all(demod, "row", split_axis=2, concat_axis=3, tiled=True)
        ordered = swapped.reshape(2, sensors, per_device, sub_n, RADIX).transpose(0, 1, 2, 4, 3)
        above = from_behind_2(ordered, ("row", "col"), -1)
        extended = jnp.concatenate([ordered, above], axis=2)
        own_real = ordered[0].astype(jnp.float32)
        own_imag = ordered[1].astype(jnp.float32)
        prod_real = []
        prod_imag = []
        for wheel in range(orders.shape[0]):
            for order_at in range(orders.shape[1]):
                partner = lax.dynamic_slice_in_dim(
                    extended, orders[wheel, order_at], per_device, axis=2
                )
                partner = partner.astype(jnp.float32)
                prod_real.append(own_real * partner[0] + own_imag * partner[1])
                prod_imag.append(own_imag * partner[0] - own_real * partner[1])
        products = jnp.stack([jnp.stack(prod_real, axis=1), jnp.stack(prod_imag, axis=1)]).astype(
            jnp.bfloat16
        )

        return products.reshape(2, sensors, combos, per_device * RADIX, sub_n)

    tiles_dev = sensors * combos * RADIX
    capacity = max(2, 2 * tiles_dev // devices_n)
    owner_ids = owners[:, 0]
    targets = jnp.arange(devices_n, dtype=jnp.int32)
    one_hot = (owner_ids[:, None] == targets[None, :]).astype(jnp.int32)
    before = jnp.cumsum(one_hot, axis=0) - one_hot
    slot_ids = jnp.sum(before * one_hot, axis=1)
    places = owner_ids * capacity + slot_ids
    table_sub = sub_coefficients(sub_n)
    halves = 2
    part = sensors // halves
    tiles_part = tiles_dev // halves
    outgoing = jnp.zeros((devices_n * capacity, per_device, sub_n), jnp.bfloat16)
    spectrum = None
    for half in range(halves):
        products = front(padded_all[half * part : (half + 1) * part])
        spectrum, outgoing = spectrum_call(
            products,
            table_sub,
            hops_n,
            places[half * tiles_part : (half + 1) * tiles_part],
            outgoing,
            spectrum,
            half * part * combos,
            sensors,
        )
    outgoing = outgoing.reshape(devices_n, capacity * per_device, sub_n)
    arrived = lax.all_to_all(outgoing, ("row", "col"), split_axis=0, concat_axis=0, tiled=True)
    found = jnp.dot(
        arrived.reshape(-1, sub_n), templates[0], preferred_element_type=jnp.float32
    ).astype(jnp.bfloat16)
    found = found.reshape(devices_n, capacity, per_device, feat_n)
    return (spectrum, found[None])


def solution(mesh):
    in_specs = (P(None, "row", None), P(), P(("row", "col"), None), P(("row", "col"), None, None))
    out_specs = (
        P(None, None, None, ("row", "col"), None),
        P(("row", "col"), None, None, None, None),
    )
    return jax.shard_map(shards, mesh=mesh, in_specs=in_specs, out_specs=out_specs, check_vma=False)
```

```python
import math

import jax
import jax.numpy as jnp
from jax import lax
from jax.experimental import pallas as pl
from jax.experimental.pallas import tpu as pltpu
from jax.sharding import PartitionSpec as P
import numpy as np

RADIX = 8


def from_behind(block, axis, distance):
    devices = range(lax.axis_size(axis))
    route = [(i - distance, i) for i in devices if i - distance in devices]
    return lax.ppermute(block, axis, route)


def from_behind_2(value, axis, steps):
    count = lax.axis_size(axis)
    pairs = [(source, (source + steps) % count) for source in range(count)]
    return lax.ppermute(value, axis, pairs)


def channel_coefficients(n_total, channel_ids):
    lanes = 128
    position = jnp.arange(n_total, dtype=jnp.int32)
    high = jnp.arange(n_total // lanes, dtype=jnp.int32) * lanes
    low = jnp.arange(lanes, dtype=jnp.int32)
    step = 2.0 * math.pi / n_total
    high_angle = step * (channel_ids[:, None] * high[None, :] % n_total).astype(jnp.float32)
    low_angle = step * (channel_ids[:, None] * low[None, :] % n_total).astype(jnp.float32)
    high_cos, high_sin = jnp.cos(high_angle)[:, :, None], jnp.sin(high_angle)[:, :, None]
    low_cos, low_sin = jnp.cos(low_angle)[:, None], jnp.sin(low_angle)[:, None]
    cos_part = (high_cos * low_cos - high_sin * low_sin).reshape(-1, n_total)
    sin_part = (high_sin * low_cos + high_cos * low_sin).reshape(-1, n_total)
    window = 0.5 - 0.5 * jnp.cos(step * position.astype(jnp.float32))
    gain_factor = math.sqrt(8.0 / (3.0 * n_total))
    weighted = gain_factor * window[None, :]
    both = jnp.concatenate([weighted * cos_part, weighted * sin_part], axis=0)
    return both.astype(jnp.bfloat16)


def sub_coefficients(sub_total):
    index_a = jnp.arange(sub_total, dtype=jnp.int32)
    turns = index_a[:, None] * index_a[None, :] % sub_total
    phase_angle = 2.0 * math.pi / sub_total * turns.astype(jnp.float32)
    return jnp.concatenate([jnp.cos(phase_angle), jnp.sin(phase_angle)], axis=1).astype(
        jnp.bfloat16
    )


def quarter_turn(a_cos, a_sin, channel_ids, hop_ids):
    phase_step = channel_ids[:, None] % 4 * (hop_ids[None, :] % 4) % 4
    cos_quarter = (phase_step == 0).astype(jnp.float32) - (phase_step == 2).astype(jnp.float32)
    sin_quarter = (phase_step == 1).astype(jnp.float32) - (phase_step == 3).astype(jnp.float32)
    real_part = a_cos * cos_quarter - a_sin * sin_quarter
    imag_part = -a_sin * cos_quarter - a_cos * sin_quarter
    return (real_part, imag_part)


def finish_transform(first_real, first_imag, hops_total):
    radix_count = first_real.shape[-2]
    sub_total = first_real.shape[-1]
    index_b = jnp.arange(radix_count, dtype=jnp.int32)[:, None]
    index_p = jnp.arange(sub_total, dtype=jnp.int32)[None, :]
    twist_angle = 2.0 * math.pi / hops_total * (index_b * index_p % hops_total).astype(jnp.float32)
    twist_cos = jnp.cos(twist_angle)
    twist_sin = jnp.sin(twist_angle)
    twist_real = first_real * twist_cos + first_imag * twist_sin
    twist_imag = first_imag * twist_cos - first_real * twist_sin
    index_d = jnp.arange(radix_count, dtype=jnp.int32)[None, :]
    section_angle = (
        2.0 * math.pi / radix_count * (index_b * index_d % radix_count).astype(jnp.float32)
    )
    section_cos = jnp.cos(section_angle)
    section_sin = jnp.sin(section_angle)
    highest = lax.Precision.HIGHEST
    norm_factor = 1.0 / math.sqrt(hops_total)
    out_real = norm_factor * (
        jnp.einsum("...bq,bd->...dq", twist_real, section_cos, precision=highest)
        + jnp.einsum("...bq,bd->...dq", twist_imag, section_sin, precision=highest)
    )
    out_imag = norm_factor * (
        jnp.einsum("...bq,bd->...dq", twist_imag, section_cos, precision=highest)
        - jnp.einsum("...bq,bd->...dq", twist_real, section_sin, precision=highest)
    )
    return (out_real, out_imag)


def section_mixers(radix_count, rows_per):
    index_b = np.arange(radix_count)
    angle = 2.0 * np.pi / radix_count * ((index_b[:, None] * index_b[None, :]) % radix_count)
    size = radix_count * rows_per
    tables = []
    for table in (np.cos(angle).astype(np.float32), np.sin(angle).astype(np.float32)):
        full = np.zeros((size, size), np.float32)
        for d in range(radix_count):
            for b in range(radix_count):
                for k in range(rows_per):
                    full[d * rows_per + k, k * radix_count + b] = table[b, d]
        tables.append(full)
    cos_full, sin_full = tables
    both = np.block([[cos_full, sin_full], [-sin_full, cos_full]])
    return jnp.asarray(both).astype(jnp.bfloat16)[None]


def spectrum_kernel(
    dest_ref, prod_ref, cos_ref, sin_ref, twc_ref, tws_ref, mix_ref, zero_ref, spec_ref, out_ref,
    feat_scratch, sems,
):
    del zero_ref
    f32 = jnp.float32
    block = pl.program_id(0)
    rows_per = feat_scratch.shape[1]
    sub_n = feat_scratch.shape[2]
    rows_all = prod_ref.shape[2]
    both = jnp.concatenate([prod_ref[0, 0], prod_ref[1, 0]], axis=0)
    by_cos = jnp.dot(both, cos_ref[...], preferred_element_type=f32)
    by_sin = jnp.dot(both, sin_ref[...], preferred_element_type=f32)
    first_real = by_cos[:rows_all] + by_sin[rows_all:]
    first_imag = by_cos[rows_all:] - by_sin[:rows_all]
    twist_cos = twc_ref[...]
    twist_sin = tws_ref[...]
    twist_real = first_real * twist_cos + first_imag * twist_sin
    twist_imag = first_imag * twist_cos - first_real * twist_sin

    twist = jnp.concatenate([twist_real, twist_imag], axis=0)
    high = twist.astype(jnp.bfloat16)
    low = (twist - high.astype(f32)).astype(jnp.bfloat16)
    mixed = jnp.dot(mix_ref[0], high, preferred_element_type=f32) + jnp.dot(
        mix_ref[0], low, preferred_element_type=f32
    )
    out_real = mixed[:rows_all]
    out_imag = mixed[rows_all:]
    feature = jnp.log1p(out_real * out_real + out_imag * out_imag).astype(feat_scratch.dtype)
    for d in range(RADIX):
        rows = slice(d * rows_per, (d + 1) * rows_per)
        lanes = slice(d * sub_n, (d + 1) * sub_n)
        spec_ref[0, 0, 0, :, lanes] = out_real[rows].astype(spec_ref.dtype)
        spec_ref[1, 0, 0, :, lanes] = out_imag[rows].astype(spec_ref.dtype)

    def tile_copy(step, d):
        return pltpu.make_async_copy(
            feat_scratch.at[d], out_ref.at[dest_ref[step * RADIX + d]], sems.at[d]
        )

    @pl.when(block > 0)
    def _():
        for d in range(RADIX):
            tile_copy(block - 1, d).wait()

    for d in range(RADIX):
        feat_scratch[d] = feature[d * rows_per : (d + 1) * rows_per]
    for d in range(RADIX):
        tile_copy(block, d).start()

    @pl.when(block == pl.num_programs(0) - 1)
    def _():
        for d in range(RADIX):
            tile_copy(block, d).wait()


def spectrum_call(products, table_sub, hops_total, dest, slots):
    _, sensors, combos, rows, sub_n = products.shape
    per_device = rows // RADIX
    blocks = sensors * combos
    flat = products.reshape(2, blocks, rows, sub_n)
    index_b = jnp.arange(RADIX, dtype=jnp.int32)[:, None]
    index_p = jnp.arange(sub_n, dtype=jnp.int32)[None, :]
    twist_angle = 2.0 * math.pi / hops_total * (index_b * index_p % hops_total).astype(jnp.float32)
    norm_factor = 1.0 / math.sqrt(hops_total)
    twist_cos = jnp.tile(norm_factor * jnp.cos(twist_angle), (per_device, 1))
    twist_sin = jnp.tile(norm_factor * jnp.sin(twist_angle), (per_device, 1))
    mixers = section_mixers(RADIX, per_device)
    zeros = jnp.zeros((slots, per_device, sub_n), jnp.bfloat16)
    grid_spec = pltpu.PrefetchScalarGridSpec(
        num_scalar_prefetch=1,
        grid=(blocks,),
        in_specs=[
            pl.BlockSpec((2, 1, rows, sub_n), lambda i, dest: (0, i, 0, 0)),
            pl.BlockSpec((sub_n, sub_n), lambda i, dest: (0, 0)),
            pl.BlockSpec((sub_n, sub_n), lambda i, dest: (0, 1)),
            pl.BlockSpec((rows, sub_n), lambda i, dest: (0, 0)),
            pl.BlockSpec((rows, sub_n), lambda i, dest: (0, 0)),
            pl.BlockSpec((1, 2 * rows, 2 * rows), lambda i, dest: (0, 0, 0)),
            pl.BlockSpec(memory_space=pl.ANY),
        ],
        out_specs=[
            pl.BlockSpec(
                (2, 1, 1, per_device, RADIX * sub_n),
                lambda i, dest: (0, i // combos, i % combos, 0, 0),
            ),
            pl.BlockSpec(memory_space=pl.ANY),
        ],
        scratch_shapes=[
            pltpu.VMEM((RADIX, per_device, sub_n), jnp.bfloat16),
            pltpu.SemaphoreType.DMA((RADIX,)),
        ],
    )
    spectrum, outgoing = pl.pallas_call(
        spectrum_kernel,
        grid_spec=grid_spec,
        out_shape=[
            jax.ShapeDtypeStruct((2, sensors, combos, per_device, RADIX * sub_n), jnp.bfloat16),
            jax.ShapeDtypeStruct((slots, per_device, sub_n), jnp.bfloat16),
        ],
        input_output_aliases={7: 1},
        compiler_params=pltpu.CompilerParams(
            vmem_limit_bytes=48 * 1024 * 1024,
            dimension_semantics=("arbitrary",),
        ),
        cost_estimate=pl.CostEstimate(
            flops=blocks * (8 * rows * sub_n * sub_n + 16 * rows * rows * sub_n),
            transcendentals=blocks * rows * sub_n,
            bytes_accessed=blocks * rows * sub_n * 2 * 5 + 4 * sub_n * sub_n,
        ),
    )(dest, flat, table_sub, table_sub, twist_cos, twist_sin, mixers, zeros)
    return spectrum, outgoing


def shards(frames, orders, owners, templates):
    rows_count = lax.axis_size("row")
    cols_count = lax.axis_size("col")
    devices_n = rows_count * cols_count
    sensors = frames.shape[0]
    hop_dev = frames.shape[1]
    frame_len = frames.shape[2]
    channels_n = 4 * frame_len
    hops_n = hop_dev * rows_count
    sub_n = hops_n // RADIX
    per_device = channels_n // devices_n
    local_channels = channels_n // cols_count
    combos = orders.shape[0] * orders.shape[1]
    feat_n = templates.shape[2]
    row_at = lax.axis_index("row")
    col_at = lax.axis_index("col")
    tail_frames = from_behind(frames[:, :3], "row", -1)
    padded = jnp.concatenate([frames, tail_frames], axis=1)
    column = jnp.arange(local_channels, dtype=jnp.int32)
    channel_ids = (column // per_device * cols_count + col_at) * per_device + column % per_device
    coefficients = channel_coefficients(channels_n, channel_ids)
    summed = jnp.zeros((sensors, 2 * local_channels, hop_dev), jnp.float32)
    for quarter in range(4):
        summed = summed + jnp.einsum(
            "shf,kf->skh",
            padded[:, quarter : quarter + hop_dev],
            coefficients[:, quarter * frame_len : (quarter + 1) * frame_len],
            preferred_element_type=jnp.float32,
        )
    hop_ids = row_at * hop_dev + jnp.arange(hop_dev, dtype=jnp.int32)
    real_part, imag_part = quarter_turn(
        summed[:, :local_channels], summed[:, local_channels:], channel_ids, hop_ids
    )
    demod = jnp.stack([real_part, imag_part]).astype(jnp.bfloat16)
    swapped = lax.all_to_all(demod, "row", split_axis=2, concat_axis=3, tiled=True)
    ordered = swapped.reshape(2, sensors, per_device, sub_n, RADIX).transpose(0, 1, 2, 4, 3)
    above = from_behind_2(ordered, ("row", "col"), -1)
    extended = jnp.concatenate([ordered, above], axis=2)
    own_real = ordered[0].astype(jnp.float32)
    own_imag = ordered[1].astype(jnp.float32)
    prod_real = []
    prod_imag = []
    for wheel in range(orders.shape[0]):
        for order_at in range(orders.shape[1]):
            partner = lax.dynamic_slice_in_dim(
                extended, orders[wheel, order_at], per_device, axis=2
            )
            partner = partner.astype(jnp.float32)
            prod_real.append(own_real * partner[0] + own_imag * partner[1])
            prod_imag.append(own_imag * partner[0] - own_real * partner[1])
    products = jnp.stack([jnp.stack(prod_real, axis=1), jnp.stack(prod_imag, axis=1)]).astype(
        jnp.bfloat16
    )
    tiles_dev = sensors * combos * RADIX
    capacity = max(2, 2 * tiles_dev // devices_n)
    owner_ids = owners[:, 0]
    targets = jnp.arange(devices_n, dtype=jnp.int32)
    one_hot = (owner_ids[:, None] == targets[None, :]).astype(jnp.int32)
    before = jnp.cumsum(one_hot, axis=0) - one_hot
    slot_ids = jnp.sum(before * one_hot, axis=1)
    places = owner_ids * capacity + slot_ids
    table_sub = sub_coefficients(sub_n)
    spectrum, outgoing = spectrum_call(
        products.reshape(2, sensors, combos, per_device * RADIX, sub_n),
        table_sub,
        hops_n,
        places,
        devices_n * capacity,
    )
    outgoing = outgoing.reshape(devices_n, capacity * per_device, sub_n)
    arrived = lax.all_to_all(outgoing, ("row", "col"), split_axis=0, concat_axis=0, tiled=True)
    found = jnp.dot(
        arrived.reshape(-1, sub_n), templates[0], preferred_element_type=jnp.float32
    ).astype(jnp.bfloat16)
    found = found.reshape(devices_n, capacity, per_device, feat_n)
    return (spectrum, found[None])


def solution(mesh):
    in_specs = (P(None, "row", None), P(), P(("row", "col"), None), P(("row", "col"), None, None))
    out_specs = (
        P(None, None, None, ("row", "col"), None),
        P(("row", "col"), None, None, None, None),
    )
    return jax.shard_map(shards, mesh=mesh, in_specs=in_specs, out_specs=out_specs, check_vma=False)
```

```python
import math

import jax
import jax.numpy as jnp
from jax import lax
from jax.experimental import pallas as pl
from jax.experimental.pallas import tpu as pltpu
from jax.sharding import PartitionSpec as P
import numpy as np

RADIX = 8


def from_behind(block, axis, distance):
    devices = range(lax.axis_size(axis))
    route = [(i - distance, i) for i in devices if i - distance in devices]
    return lax.ppermute(block, axis, route)


def from_behind_2(value, axis, steps):
    count = lax.axis_size(axis)
    pairs = [(source, (source + steps) % count) for source in range(count)]
    return lax.ppermute(value, axis, pairs)


def channel_coefficients(n_total, channel_ids):
    lanes = 128
    position = jnp.arange(n_total, dtype=jnp.int32)
    high = jnp.arange(n_total // lanes, dtype=jnp.int32) * lanes
    low = jnp.arange(lanes, dtype=jnp.int32)
    step = 2.0 * math.pi / n_total
    high_angle = step * (channel_ids[:, None] * high[None, :] % n_total).astype(jnp.float32)
    low_angle = step * (channel_ids[:, None] * low[None, :] % n_total).astype(jnp.float32)
    high_cos, high_sin = jnp.cos(high_angle)[:, :, None], jnp.sin(high_angle)[:, :, None]
    low_cos, low_sin = jnp.cos(low_angle)[:, None], jnp.sin(low_angle)[:, None]
    cos_part = (high_cos * low_cos - high_sin * low_sin).reshape(-1, n_total)
    sin_part = (high_sin * low_cos + high_cos * low_sin).reshape(-1, n_total)
    window = 0.5 - 0.5 * jnp.cos(step * position.astype(jnp.float32))
    gain_factor = math.sqrt(8.0 / (3.0 * n_total))
    weighted = gain_factor * window[None, :]
    both = jnp.concatenate([weighted * cos_part, weighted * sin_part], axis=0)
    return both.astype(jnp.bfloat16)


def sub_coefficients(sub_total):
    index_a = jnp.arange(sub_total, dtype=jnp.int32)
    turns = index_a[:, None] * index_a[None, :] % sub_total
    phase_angle = 2.0 * math.pi / sub_total * turns.astype(jnp.float32)
    return jnp.concatenate([jnp.cos(phase_angle), jnp.sin(phase_angle)], axis=1).astype(
        jnp.bfloat16
    )


def quarter_turn(a_cos, a_sin, channel_ids, hop_ids):
    phase_step = channel_ids[:, None] % 4 * (hop_ids[None, :] % 4) % 4
    cos_quarter = (phase_step == 0).astype(jnp.float32) - (phase_step == 2).astype(jnp.float32)
    sin_quarter = (phase_step == 1).astype(jnp.float32) - (phase_step == 3).astype(jnp.float32)
    real_part = a_cos * cos_quarter - a_sin * sin_quarter
    imag_part = -a_sin * cos_quarter - a_cos * sin_quarter
    return (real_part, imag_part)


def finish_transform(first_real, first_imag, hops_total):
    radix_count = first_real.shape[-2]
    sub_total = first_real.shape[-1]
    index_b = jnp.arange(radix_count, dtype=jnp.int32)[:, None]
    index_p = jnp.arange(sub_total, dtype=jnp.int32)[None, :]
    twist_angle = 2.0 * math.pi / hops_total * (index_b * index_p % hops_total).astype(jnp.float32)
    twist_cos = jnp.cos(twist_angle)
    twist_sin = jnp.sin(twist_angle)
    twist_real = first_real * twist_cos + first_imag * twist_sin
    twist_imag = first_imag * twist_cos - first_real * twist_sin
    index_d = jnp.arange(radix_count, dtype=jnp.int32)[None, :]
    section_angle = (
        2.0 * math.pi / radix_count * (index_b * index_d % radix_count).astype(jnp.float32)
    )
    section_cos = jnp.cos(section_angle)
    section_sin = jnp.sin(section_angle)
    highest = lax.Precision.HIGHEST
    norm_factor = 1.0 / math.sqrt(hops_total)
    out_real = norm_factor * (
        jnp.einsum("...bq,bd->...dq", twist_real, section_cos, precision=highest)
        + jnp.einsum("...bq,bd->...dq", twist_imag, section_sin, precision=highest)
    )
    out_imag = norm_factor * (
        jnp.einsum("...bq,bd->...dq", twist_imag, section_cos, precision=highest)
        - jnp.einsum("...bq,bd->...dq", twist_real, section_sin, precision=highest)
    )
    return (out_real, out_imag)


def section_mixers(radix_count, rows_per):
    index_b = np.arange(radix_count)
    angle = 2.0 * np.pi / radix_count * ((index_b[:, None] * index_b[None, :]) % radix_count)
    size = radix_count * rows_per
    tables = []
    for table in (np.cos(angle).astype(np.float32), np.sin(angle).astype(np.float32)):
        full = np.zeros((size, size), np.float32)
        for d in range(radix_count):
            for b in range(radix_count):
                for k in range(rows_per):
                    full[d * rows_per + k, k * radix_count + b] = table[b, d]
        tables.append(full)
    cos_full, sin_full = tables
    both = np.block([[cos_full, sin_full], [-sin_full, cos_full]])
    return jnp.asarray(both).astype(jnp.bfloat16)[None]


def spectrum_kernel(
    dest_ref, prod_ref, cos_ref, sin_ref, twc_ref, tws_ref, mix_ref, zero_ref, spec_ref, out_ref,
    feat_scratch, sems,
):
    del zero_ref
    f32 = jnp.float32
    block = pl.program_id(0)
    rows_per = feat_scratch.shape[1]
    sub_n = feat_scratch.shape[2]
    rows_all = prod_ref.shape[2]
    both = jnp.concatenate([prod_ref[0, 0], prod_ref[1, 0]], axis=0)
    by_cos = jnp.dot(both, cos_ref[...], preferred_element_type=f32)
    by_sin = jnp.dot(both, sin_ref[...], preferred_element_type=f32)
    first_real = by_cos[:rows_all] + by_sin[rows_all:]
    first_imag = by_cos[rows_all:] - by_sin[:rows_all]
    twist_cos = twc_ref[...]
    twist_sin = tws_ref[...]
    twist_real = first_real * twist_cos + first_imag * twist_sin
    twist_imag = first_imag * twist_cos - first_real * twist_sin

    twist = jnp.concatenate([twist_real, twist_imag], axis=0)
    high = twist.astype(jnp.bfloat16)
    low = (twist - high.astype(f32)).astype(jnp.bfloat16)
    mixed = jnp.dot(mix_ref[0], high, preferred_element_type=f32) + jnp.dot(
        mix_ref[0], low, preferred_element_type=f32
    )
    out_real = mixed[:rows_all]
    out_imag = mixed[rows_all:]
    feature = jnp.log1p(out_real * out_real + out_imag * out_imag).astype(feat_scratch.dtype)
    for d in range(RADIX):
        rows = slice(d * rows_per, (d + 1) * rows_per)
        lanes = slice(d * sub_n, (d + 1) * sub_n)
        spec_ref[0, 0, 0, :, lanes] = out_real[rows].astype(spec_ref.dtype)
        spec_ref[1, 0, 0, :, lanes] = out_imag[rows].astype(spec_ref.dtype)

    def tile_copy(step, d):
        return pltpu.make_async_copy(
            feat_scratch.at[d], out_ref.at[dest_ref[step * RADIX + d]], sems.at[d]
        )

    @pl.when(block > 0)
    def _():
        for d in range(RADIX):
            tile_copy(block - 1, d).wait()

    for d in range(RADIX):
        feat_scratch[d] = feature[d * rows_per : (d + 1) * rows_per]
    for d in range(RADIX):
        tile_copy(block, d).start()

    @pl.when(block == pl.num_programs(0) - 1)
    def _():
        for d in range(RADIX):
            tile_copy(block, d).wait()


def spectrum_call(products, table_sub, hops_total, dest, slots):
    _, sensors, combos, rows, sub_n = products.shape
    per_device = rows // RADIX
    blocks = sensors * combos
    flat = products.reshape(2, blocks, rows, sub_n)
    index_b = jnp.arange(RADIX, dtype=jnp.int32)[:, None]
    index_p = jnp.arange(sub_n, dtype=jnp.int32)[None, :]
    twist_angle = 2.0 * math.pi / hops_total * (index_b * index_p % hops_total).astype(jnp.float32)
    norm_factor = 1.0 / math.sqrt(hops_total)
    twist_cos = jnp.tile(norm_factor * jnp.cos(twist_angle), (per_device, 1))
    twist_sin = jnp.tile(norm_factor * jnp.sin(twist_angle), (per_device, 1))
    mixers = section_mixers(RADIX, per_device)
    zeros = jnp.zeros((slots, per_device, sub_n), jnp.bfloat16)
    grid_spec = pltpu.PrefetchScalarGridSpec(
        num_scalar_prefetch=1,
        grid=(blocks,),
        in_specs=[
            pl.BlockSpec((2, 1, rows, sub_n), lambda i, dest: (0, i, 0, 0)),
            pl.BlockSpec((sub_n, sub_n), lambda i, dest: (0, 0)),
            pl.BlockSpec((sub_n, sub_n), lambda i, dest: (0, 1)),
            pl.BlockSpec((rows, sub_n), lambda i, dest: (0, 0)),
            pl.BlockSpec((rows, sub_n), lambda i, dest: (0, 0)),
            pl.BlockSpec((1, 2 * rows, 2 * rows), lambda i, dest: (0, 0, 0)),
            pl.BlockSpec(memory_space=pl.ANY),
        ],
        out_specs=[
            pl.BlockSpec(
                (2, 1, 1, per_device, RADIX * sub_n),
                lambda i, dest: (0, i // combos, i % combos, 0, 0),
            ),
            pl.BlockSpec(memory_space=pl.ANY),
        ],
        scratch_shapes=[
            pltpu.VMEM((RADIX, per_device, sub_n), jnp.bfloat16),
            pltpu.SemaphoreType.DMA((RADIX,)),
        ],
    )
    spectrum, outgoing = pl.pallas_call(
        spectrum_kernel,
        grid_spec=grid_spec,
        out_shape=[
            jax.ShapeDtypeStruct((2, sensors, combos, per_device, RADIX * sub_n), jnp.bfloat16),
            jax.ShapeDtypeStruct((slots, per_device, sub_n), jnp.bfloat16),
        ],
        input_output_aliases={7: 1},
        compiler_params=pltpu.CompilerParams(
            vmem_limit_bytes=48 * 1024 * 1024,
            dimension_semantics=("arbitrary",),
        ),
        cost_estimate=pl.CostEstimate(
            flops=blocks * (8 * rows * sub_n * sub_n + 16 * rows * rows * sub_n),
            transcendentals=blocks * rows * sub_n,
            bytes_accessed=blocks * rows * sub_n * 2 * 5 + 4 * sub_n * sub_n,
        ),
    )(dest, flat, table_sub, table_sub, twist_cos, twist_sin, mixers, zeros)
    return spectrum, outgoing


def shards(frames, orders, owners, templates):
    rows_count = lax.axis_size("row")
    cols_count = lax.axis_size("col")
    devices_n = rows_count * cols_count
    sensors = frames.shape[0]
    hop_dev = frames.shape[1]
    frame_len = frames.shape[2]
    channels_n = 4 * frame_len
    hops_n = hop_dev * rows_count
    sub_n = hops_n // RADIX
    per_device = channels_n // devices_n
    local_channels = channels_n // cols_count
    combos = orders.shape[0] * orders.shape[1]
    feat_n = templates.shape[2]
    row_at = lax.axis_index("row")
    col_at = lax.axis_index("col")
    tail_frames = from_behind(frames[:, :3], "row", -1)
    padded = jnp.concatenate([frames, tail_frames], axis=1)
    column = jnp.arange(local_channels, dtype=jnp.int32)
    channel_ids = (column // per_device * cols_count + col_at) * per_device + column % per_device
    coefficients = channel_coefficients(channels_n, channel_ids)
    summed = jnp.zeros((sensors, 2 * local_channels, hop_dev), jnp.float32)
    for quarter in range(4):
        summed = summed + jnp.einsum(
            "shf,kf->skh",
            padded[:, quarter : quarter + hop_dev],
            coefficients[:, quarter * frame_len : (quarter + 1) * frame_len],
            preferred_element_type=jnp.float32,
        )
    hop_ids = row_at * hop_dev + jnp.arange(hop_dev, dtype=jnp.int32)
    real_part, imag_part = quarter_turn(
        summed[:, :local_channels], summed[:, local_channels:], channel_ids, hop_ids
    )
    demod = jnp.stack([real_part, imag_part]).astype(jnp.bfloat16)
    swapped = lax.all_to_all(demod, "row", split_axis=2, concat_axis=3, tiled=True)
    halves = 2
    part = sensors // halves
    pieces = []
    for half in range(halves):
        ordered = swapped[:, half * part : (half + 1) * part]
        ordered = ordered.reshape(2, part, per_device, sub_n, RADIX).transpose(0, 1, 2, 4, 3)
        above = from_behind_2(ordered, ("row", "col"), -1)
        extended = jnp.concatenate([ordered, above], axis=2)
        own_real = ordered[0].astype(jnp.float32)
        own_imag = ordered[1].astype(jnp.float32)
        prod_real = []
        prod_imag = []
        for wheel in range(orders.shape[0]):
            for order_at in range(orders.shape[1]):
                partner = lax.dynamic_slice_in_dim(
                    extended, orders[wheel, order_at], per_device, axis=2
                )
                partner = partner.astype(jnp.float32)
                prod_real.append(own_real * partner[0] + own_imag * partner[1])
                prod_imag.append(own_imag * partner[0] - own_real * partner[1])
        pieces.append(
            jnp.stack([jnp.stack(prod_real, axis=1), jnp.stack(prod_imag, axis=1)]).astype(
                jnp.bfloat16
            )
        )
    products = jnp.concatenate(pieces, axis=1)
    tiles_dev = sensors * combos * RADIX
    capacity = max(2, 2 * tiles_dev // devices_n)
    owner_ids = owners[:, 0]
    targets = jnp.arange(devices_n, dtype=jnp.int32)
    one_hot = (owner_ids[:, None] == targets[None, :]).astype(jnp.int32)
    before = jnp.cumsum(one_hot, axis=0) - one_hot
    slot_ids = jnp.sum(before * one_hot, axis=1)
    places = owner_ids * capacity + slot_ids
    table_sub = sub_coefficients(sub_n)
    spectrum, outgoing = spectrum_call(
        products.reshape(2, sensors, combos, per_device * RADIX, sub_n),
        table_sub,
        hops_n,
        places,
        devices_n * capacity,
    )
    outgoing = outgoing.reshape(devices_n, capacity * per_device, sub_n)
    arrived = lax.all_to_all(outgoing, ("row", "col"), split_axis=0, concat_axis=0, tiled=True)
    found = jnp.dot(
        arrived.reshape(-1, sub_n), templates[0], preferred_element_type=jnp.float32
    ).astype(jnp.bfloat16)
    found = found.reshape(devices_n, capacity, per_device, feat_n)
    return (spectrum, found[None])


def solution(mesh):
    in_specs = (P(None, "row", None), P(), P(("row", "col"), None), P(("row", "col"), None, None))
    out_specs = (
        P(None, None, None, ("row", "col"), None),
        P(("row", "col"), None, None, None, None),
    )
    return jax.shard_map(shards, mesh=mesh, in_specs=in_specs, out_specs=out_specs, check_vma=False)
```

```python
import math

import jax
import jax.numpy as jnp
from jax import lax
from jax.experimental import pallas as pl
from jax.experimental.pallas import tpu as pltpu
from jax.sharding import PartitionSpec as P
import numpy as np

RADIX = 8


def from_behind(block, axis, distance):
    devices = range(lax.axis_size(axis))
    route = [(i - distance, i) for i in devices if i - distance in devices]
    return lax.ppermute(block, axis, route)


def from_behind_2(value, axis, steps):
    count = lax.axis_size(axis)
    pairs = [(source, (source + steps) % count) for source in range(count)]
    return lax.ppermute(value, axis, pairs)


def channel_coefficients(n_total, channel_ids):
    lanes = 128
    position = jnp.arange(n_total, dtype=jnp.int32)
    high = jnp.arange(n_total // lanes, dtype=jnp.int32) * lanes
    low = jnp.arange(lanes, dtype=jnp.int32)
    step = 2.0 * math.pi / n_total
    high_angle = step * (channel_ids[:, None] * high[None, :] % n_total).astype(jnp.float32)
    low_angle = step * (channel_ids[:, None] * low[None, :] % n_total).astype(jnp.float32)
    high_cos, high_sin = jnp.cos(high_angle)[:, :, None], jnp.sin(high_angle)[:, :, None]
    low_cos, low_sin = jnp.cos(low_angle)[:, None], jnp.sin(low_angle)[:, None]
    cos_part = (high_cos * low_cos - high_sin * low_sin).reshape(-1, n_total)
    sin_part = (high_sin * low_cos + high_cos * low_sin).reshape(-1, n_total)
    window = 0.5 - 0.5 * jnp.cos(step * position.astype(jnp.float32))
    gain_factor = math.sqrt(8.0 / (3.0 * n_total))
    weighted = gain_factor * window[None, :]
    both = jnp.concatenate([weighted * cos_part, weighted * sin_part], axis=0)
    return both.astype(jnp.bfloat16)


def sub_coefficients(sub_total):
    index_a = jnp.arange(sub_total, dtype=jnp.int32)
    turns = index_a[:, None] * index_a[None, :] % sub_total
    phase_angle = 2.0 * math.pi / sub_total * turns.astype(jnp.float32)
    return jnp.concatenate([jnp.cos(phase_angle), jnp.sin(phase_angle)], axis=1).astype(
        jnp.bfloat16
    )


def quarter_turn(a_cos, a_sin, channel_ids, hop_ids):
    phase_step = channel_ids[:, None] % 4 * (hop_ids[None, :] % 4) % 4
    cos_quarter = (phase_step == 0).astype(jnp.float32) - (phase_step == 2).astype(jnp.float32)
    sin_quarter = (phase_step == 1).astype(jnp.float32) - (phase_step == 3).astype(jnp.float32)
    real_part = a_cos * cos_quarter - a_sin * sin_quarter
    imag_part = -a_sin * cos_quarter - a_cos * sin_quarter
    return (real_part, imag_part)


def finish_transform(first_real, first_imag, hops_total):
    radix_count = first_real.shape[-2]
    sub_total = first_real.shape[-1]
    index_b = jnp.arange(radix_count, dtype=jnp.int32)[:, None]
    index_p = jnp.arange(sub_total, dtype=jnp.int32)[None, :]
    twist_angle = 2.0 * math.pi / hops_total * (index_b * index_p % hops_total).astype(jnp.float32)
    twist_cos = jnp.cos(twist_angle)
    twist_sin = jnp.sin(twist_angle)
    twist_real = first_real * twist_cos + first_imag * twist_sin
    twist_imag = first_imag * twist_cos - first_real * twist_sin
    index_d = jnp.arange(radix_count, dtype=jnp.int32)[None, :]
    section_angle = (
        2.0 * math.pi / radix_count * (index_b * index_d % radix_count).astype(jnp.float32)
    )
    section_cos = jnp.cos(section_angle)
    section_sin = jnp.sin(section_angle)
    highest = lax.Precision.HIGHEST
    norm_factor = 1.0 / math.sqrt(hops_total)
    out_real = norm_factor * (
        jnp.einsum("...bq,bd->...dq", twist_real, section_cos, precision=highest)
        + jnp.einsum("...bq,bd->...dq", twist_imag, section_sin, precision=highest)
    )
    out_imag = norm_factor * (
        jnp.einsum("...bq,bd->...dq", twist_imag, section_cos, precision=highest)
        - jnp.einsum("...bq,bd->...dq", twist_real, section_sin, precision=highest)
    )
    return (out_real, out_imag)


def section_mixers(radix_count, rows_per):
    index_b = np.arange(radix_count)
    angle = 2.0 * np.pi / radix_count * ((index_b[:, None] * index_b[None, :]) % radix_count)
    size = radix_count * rows_per
    tables = []
    for table in (np.cos(angle).astype(np.float32), np.sin(angle).astype(np.float32)):
        full = np.zeros((size, size), np.float32)
        for d in range(radix_count):
            for b in range(radix_count):
                for k in range(rows_per):
                    full[d * rows_per + k, k * radix_count + b] = table[b, d]
        tables.append(full)
    cos_full, sin_full = tables
    both = np.block([[cos_full, sin_full], [-sin_full, cos_full]])
    return jnp.asarray(both).astype(jnp.bfloat16)[None]


def spectrum_kernel(
    dest_ref, prod_ref, cos_ref, sin_ref, twc_ref, tws_ref, mix_ref, zero_ref, spec_ref, out_ref,
    feat_scratch, sems,
):
    del zero_ref
    f32 = jnp.float32
    block = pl.program_id(0)
    rows_per = feat_scratch.shape[1]
    sub_n = feat_scratch.shape[2]
    rows_all = prod_ref.shape[2]
    both = jnp.concatenate([prod_ref[0, 0], prod_ref[1, 0]], axis=0)
    by_cos = jnp.dot(both, cos_ref[...], preferred_element_type=f32)
    by_sin = jnp.dot(both, sin_ref[...], preferred_element_type=f32)
    first_real = by_cos[:rows_all] + by_sin[rows_all:]
    first_imag = by_cos[rows_all:] - by_sin[:rows_all]
    twist_cos = twc_ref[...]
    twist_sin = tws_ref[...]
    twist_real = first_real * twist_cos + first_imag * twist_sin
    twist_imag = first_imag * twist_cos - first_real * twist_sin

    twist = jnp.concatenate([twist_real, twist_imag], axis=0)
    high = twist.astype(jnp.bfloat16)
    low = (twist - high.astype(f32)).astype(jnp.bfloat16)
    mixed = jnp.dot(mix_ref[0], high, preferred_element_type=f32) + jnp.dot(
        mix_ref[0], low, preferred_element_type=f32
    )
    out_real = mixed[:rows_all]
    out_imag = mixed[rows_all:]
    feature = jnp.log1p(out_real * out_real + out_imag * out_imag).astype(feat_scratch.dtype)
    for d in range(RADIX):
        rows = slice(d * rows_per, (d + 1) * rows_per)
        lanes = slice(d * sub_n, (d + 1) * sub_n)
        spec_ref[0, 0, 0, :, lanes] = out_real[rows].astype(spec_ref.dtype)
        spec_ref[1, 0, 0, :, lanes] = out_imag[rows].astype(spec_ref.dtype)

    def tile_copy(step, d):
        return pltpu.make_async_copy(
            feat_scratch.at[d], out_ref.at[dest_ref[step * RADIX + d]], sems.at[d]
        )

    @pl.when(block > 0)
    def _():
        for d in range(RADIX):
            tile_copy(block - 1, d).wait()

    for d in range(RADIX):
        feat_scratch[d] = feature[d * rows_per : (d + 1) * rows_per]
    for d in range(RADIX):
        tile_copy(block, d).start()

    @pl.when(block == pl.num_programs(0) - 1)
    def _():
        for d in range(RADIX):
            tile_copy(block, d).wait()


def spectrum_call(products, table_sub, hops_total, dest, slots):
    _, sensors, combos, rows, sub_n = products.shape
    per_device = rows // RADIX
    blocks = sensors * combos
    flat = products.reshape(2, blocks, rows, sub_n)
    index_b = jnp.arange(RADIX, dtype=jnp.int32)[:, None]
    index_p = jnp.arange(sub_n, dtype=jnp.int32)[None, :]
    twist_angle = 2.0 * math.pi / hops_total * (index_b * index_p % hops_total).astype(jnp.float32)
    norm_factor = 1.0 / math.sqrt(hops_total)
    twist_cos = jnp.tile(norm_factor * jnp.cos(twist_angle), (per_device, 1))
    twist_sin = jnp.tile(norm_factor * jnp.sin(twist_angle), (per_device, 1))
    mixers = section_mixers(RADIX, per_device)
    zeros = jnp.zeros((slots, per_device, sub_n), jnp.bfloat16)
    grid_spec = pltpu.PrefetchScalarGridSpec(
        num_scalar_prefetch=1,
        grid=(blocks,),
        in_specs=[
            pl.BlockSpec((2, 1, rows, sub_n), lambda i, dest: (0, i, 0, 0)),
            pl.BlockSpec((sub_n, sub_n), lambda i, dest: (0, 0)),
            pl.BlockSpec((sub_n, sub_n), lambda i, dest: (0, 1)),
            pl.BlockSpec((rows, sub_n), lambda i, dest: (0, 0)),
            pl.BlockSpec((rows, sub_n), lambda i, dest: (0, 0)),
            pl.BlockSpec((1, 2 * rows, 2 * rows), lambda i, dest: (0, 0, 0)),
            pl.BlockSpec(memory_space=pl.ANY),
        ],
        out_specs=[
            pl.BlockSpec(
                (2, 1, 1, per_device, RADIX * sub_n),
                lambda i, dest: (0, i // combos, i % combos, 0, 0),
            ),
            pl.BlockSpec(memory_space=pl.ANY),
        ],
        scratch_shapes=[
            pltpu.VMEM((RADIX, per_device, sub_n), jnp.bfloat16),
            pltpu.SemaphoreType.DMA((RADIX,)),
        ],
    )
    spectrum, outgoing = pl.pallas_call(
        spectrum_kernel,
        grid_spec=grid_spec,
        out_shape=[
            jax.ShapeDtypeStruct((2, sensors, combos, per_device, RADIX * sub_n), jnp.bfloat16),
            jax.ShapeDtypeStruct((slots, per_device, sub_n), jnp.bfloat16),
        ],
        input_output_aliases={7: 1},
        compiler_params=pltpu.CompilerParams(
            vmem_limit_bytes=48 * 1024 * 1024,
            dimension_semantics=("arbitrary",),
        ),
        cost_estimate=pl.CostEstimate(
            flops=blocks * (8 * rows * sub_n * sub_n + 16 * rows * rows * sub_n),
            transcendentals=blocks * rows * sub_n,
            bytes_accessed=blocks * rows * sub_n * 2 * 5 + 4 * sub_n * sub_n,
        ),
    )(dest, flat, table_sub, table_sub, twist_cos, twist_sin, mixers, zeros)
    return spectrum, outgoing


def shards(frames, orders, owners, templates):
    rows_count = lax.axis_size("row")
    cols_count = lax.axis_size("col")
    devices_n = rows_count * cols_count
    sensors = frames.shape[0]
    hop_dev = frames.shape[1]
    frame_len = frames.shape[2]
    channels_n = 4 * frame_len
    hops_n = hop_dev * rows_count
    sub_n = hops_n // RADIX
    per_device = channels_n // devices_n
    local_channels = channels_n // cols_count
    combos = orders.shape[0] * orders.shape[1]
    feat_n = templates.shape[2]
    row_at = lax.axis_index("row")
    col_at = lax.axis_index("col")
    tail_frames = from_behind(frames[:, :3], "row", -1)
    padded = jnp.concatenate([frames, tail_frames], axis=1)
    column = jnp.arange(local_channels, dtype=jnp.int32)
    channel_ids = (column // per_device * cols_count + col_at) * per_device + column % per_device
    coefficients = channel_coefficients(channels_n, channel_ids)
    summed = jnp.zeros((sensors, 2 * local_channels, hop_dev), jnp.float32)
    for quarter in range(4):
        summed = summed + jnp.einsum(
            "shf,kf->skh",
            padded[:, quarter : quarter + hop_dev],
            coefficients[:, quarter * frame_len : (quarter + 1) * frame_len],
            preferred_element_type=jnp.float32,
        )
    hop_ids = row_at * hop_dev + jnp.arange(hop_dev, dtype=jnp.int32)
    real_part, imag_part = quarter_turn(
        summed[:, :local_channels], summed[:, local_channels:], channel_ids, hop_ids
    )
    demod = jnp.stack([real_part, imag_part]).astype(jnp.bfloat16)
    swapped = lax.all_to_all(demod, "row", split_axis=2, concat_axis=3, tiled=True)
    halves = 4
    part = sensors // halves
    pieces = []
    for half in range(halves):
        ordered = swapped[:, half * part : (half + 1) * part]
        ordered = ordered.reshape(2, part, per_device, sub_n, RADIX).transpose(0, 1, 2, 4, 3)
        above = from_behind_2(ordered, ("row", "col"), -1)
        extended = jnp.concatenate([ordered, above], axis=2)
        own_real = ordered[0].astype(jnp.float32)
        own_imag = ordered[1].astype(jnp.float32)
        prod_real = []
        prod_imag = []
        for wheel in range(orders.shape[0]):
            for order_at in range(orders.shape[1]):
                partner = lax.dynamic_slice_in_dim(
                    extended, orders[wheel, order_at], per_device, axis=2
                )
                partner = partner.astype(jnp.float32)
                prod_real.append(own_real * partner[0] + own_imag * partner[1])
                prod_imag.append(own_imag * partner[0] - own_real * partner[1])
        pieces.append(
            jnp.stack([jnp.stack(prod_real, axis=1), jnp.stack(prod_imag, axis=1)]).astype(
                jnp.bfloat16
            )
        )
    products = jnp.concatenate(pieces, axis=1)
    tiles_dev = sensors * combos * RADIX
    capacity = max(2, 2 * tiles_dev // devices_n)
    owner_ids = owners[:, 0]
    targets = jnp.arange(devices_n, dtype=jnp.int32)
    one_hot = (owner_ids[:, None] == targets[None, :]).astype(jnp.int32)
    before = jnp.cumsum(one_hot, axis=0) - one_hot
    slot_ids = jnp.sum(before * one_hot, axis=1)
    places = owner_ids * capacity + slot_ids
    table_sub = sub_coefficients(sub_n)
    spectrum, outgoing = spectrum_call(
        products.reshape(2, sensors, combos, per_device * RADIX, sub_n),
        table_sub,
        hops_n,
        places,
        devices_n * capacity,
    )
    outgoing = outgoing.reshape(devices_n, capacity * per_device, sub_n)
    arrived = lax.all_to_all(outgoing, ("row", "col"), split_axis=0, concat_axis=0, tiled=True)
    found = jnp.dot(
        arrived.reshape(-1, sub_n), templates[0], preferred_element_type=jnp.float32
    ).astype(jnp.bfloat16)
    found = found.reshape(devices_n, capacity, per_device, feat_n)
    return (spectrum, found[None])


def solution(mesh):
    in_specs = (P(None, "row", None), P(), P(("row", "col"), None), P(("row", "col"), None, None))
    out_specs = (
        P(None, None, None, ("row", "col"), None),
        P(("row", "col"), None, None, None, None),
    )
    return jax.shard_map(shards, mesh=mesh, in_specs=in_specs, out_specs=out_specs, check_vma=False)
```

```python
import math

import jax
import jax.numpy as jnp
from jax import lax
from jax.experimental import pallas as pl
from jax.experimental.pallas import tpu as pltpu
from jax.sharding import PartitionSpec as P
import numpy as np

RADIX = 8


def from_behind(block, axis, distance):
    devices = range(lax.axis_size(axis))
    route = [(i - distance, i) for i in devices if i - distance in devices]
    return lax.ppermute(block, axis, route)


def from_behind_2(value, axis, steps):
    count = lax.axis_size(axis)
    pairs = [(source, (source + steps) % count) for source in range(count)]
    return lax.ppermute(value, axis, pairs)


def channel_coefficients(n_total, channel_ids):
    lanes = 128
    position = jnp.arange(n_total, dtype=jnp.int32)
    high = jnp.arange(n_total // lanes, dtype=jnp.int32) * lanes
    low = jnp.arange(lanes, dtype=jnp.int32)
    step = 2.0 * math.pi / n_total
    high_angle = step * (channel_ids[:, None] * high[None, :] % n_total).astype(jnp.float32)
    low_angle = step * (channel_ids[:, None] * low[None, :] % n_total).astype(jnp.float32)
    high_cos, high_sin = jnp.cos(high_angle)[:, :, None], jnp.sin(high_angle)[:, :, None]
    low_cos, low_sin = jnp.cos(low_angle)[:, None], jnp.sin(low_angle)[:, None]
    cos_part = (high_cos * low_cos - high_sin * low_sin).reshape(-1, n_total)
    sin_part = (high_sin * low_cos + high_cos * low_sin).reshape(-1, n_total)
    window = 0.5 - 0.5 * jnp.cos(step * position.astype(jnp.float32))
    gain_factor = math.sqrt(8.0 / (3.0 * n_total))
    weighted = gain_factor * window[None, :]
    both = jnp.concatenate([weighted * cos_part, weighted * sin_part], axis=0)
    return both.astype(jnp.bfloat16)


def sub_coefficients(sub_total):
    index_a = jnp.arange(sub_total, dtype=jnp.int32)
    turns = index_a[:, None] * index_a[None, :] % sub_total
    phase_angle = 2.0 * math.pi / sub_total * turns.astype(jnp.float32)
    return jnp.concatenate([jnp.cos(phase_angle), jnp.sin(phase_angle)], axis=1).astype(
        jnp.bfloat16
    )


def quarter_turn(a_cos, a_sin, channel_ids, hop_ids):
    phase_step = channel_ids[:, None] % 4 * (hop_ids[None, :] % 4) % 4
    cos_quarter = (phase_step == 0).astype(jnp.float32) - (phase_step == 2).astype(jnp.float32)
    sin_quarter = (phase_step == 1).astype(jnp.float32) - (phase_step == 3).astype(jnp.float32)
    real_part = a_cos * cos_quarter - a_sin * sin_quarter
    imag_part = -a_sin * cos_quarter - a_cos * sin_quarter
    return (real_part, imag_part)


def finish_transform(first_real, first_imag, hops_total):
    radix_count = first_real.shape[-2]
    sub_total = first_real.shape[-1]
    index_b = jnp.arange(radix_count, dtype=jnp.int32)[:, None]
    index_p = jnp.arange(sub_total, dtype=jnp.int32)[None, :]
    twist_angle = 2.0 * math.pi / hops_total * (index_b * index_p % hops_total).astype(jnp.float32)
    twist_cos = jnp.cos(twist_angle)
    twist_sin = jnp.sin(twist_angle)
    twist_real = first_real * twist_cos + first_imag * twist_sin
    twist_imag = first_imag * twist_cos - first_real * twist_sin
    index_d = jnp.arange(radix_count, dtype=jnp.int32)[None, :]
    section_angle = (
        2.0 * math.pi / radix_count * (index_b * index_d % radix_count).astype(jnp.float32)
    )
    section_cos = jnp.cos(section_angle)
    section_sin = jnp.sin(section_angle)
    highest = lax.Precision.HIGHEST
    norm_factor = 1.0 / math.sqrt(hops_total)
    out_real = norm_factor * (
        jnp.einsum("...bq,bd->...dq", twist_real, section_cos, precision=highest)
        + jnp.einsum("...bq,bd->...dq", twist_imag, section_sin, precision=highest)
    )
    out_imag = norm_factor * (
        jnp.einsum("...bq,bd->...dq", twist_imag, section_cos, precision=highest)
        - jnp.einsum("...bq,bd->...dq", twist_real, section_sin, precision=highest)
    )
    return (out_real, out_imag)


def section_mixers(radix_count, rows_per):
    index_b = np.arange(radix_count)
    angle = 2.0 * np.pi / radix_count * ((index_b[:, None] * index_b[None, :]) % radix_count)
    size = radix_count * rows_per
    tables = []
    for table in (np.cos(angle).astype(np.float32), np.sin(angle).astype(np.float32)):
        full = np.zeros((size, size), np.float32)
        for d in range(radix_count):
            for b in range(radix_count):
                for k in range(rows_per):
                    full[d * rows_per + k, k * radix_count + b] = table[b, d]
        tables.append(full)
    cos_full, sin_full = tables
    both = np.block([[cos_full, sin_full], [-sin_full, cos_full]])
    return jnp.asarray(both).astype(jnp.bfloat16)[None]


def spectrum_kernel(dest_ref, prod_ref, cos_ref, sin_ref, twc_ref, tws_ref, mix_ref, *refs):
    spec_ref, out_ref, feat_scratch, sems = refs[-4:]
    f32 = jnp.float32
    block = pl.program_id(0)
    rows_per = feat_scratch.shape[1]
    sub_n = feat_scratch.shape[2]
    rows_all = prod_ref.shape[2]
    both = jnp.concatenate([prod_ref[0, 0], prod_ref[1, 0]], axis=0)
    by_cos = jnp.dot(both, cos_ref[...], preferred_element_type=f32)
    by_sin = jnp.dot(both, sin_ref[...], preferred_element_type=f32)
    first_real = by_cos[:rows_all] + by_sin[rows_all:]
    first_imag = by_cos[rows_all:] - by_sin[:rows_all]
    twist_cos = twc_ref[...]
    twist_sin = tws_ref[...]
    twist_real = first_real * twist_cos + first_imag * twist_sin
    twist_imag = first_imag * twist_cos - first_real * twist_sin

    twist = jnp.concatenate([twist_real, twist_imag], axis=0)
    high = twist.astype(jnp.bfloat16)
    low = (twist - high.astype(f32)).astype(jnp.bfloat16)
    mixed = jnp.dot(mix_ref[0], high, preferred_element_type=f32) + jnp.dot(
        mix_ref[0], low, preferred_element_type=f32
    )
    out_real = mixed[:rows_all]
    out_imag = mixed[rows_all:]
    feature = jnp.log1p(out_real * out_real + out_imag * out_imag).astype(feat_scratch.dtype)
    for d in range(RADIX):
        rows = slice(d * rows_per, (d + 1) * rows_per)
        lanes = slice(d * sub_n, (d + 1) * sub_n)
        spec_ref[0, 0, 0, :, lanes] = out_real[rows].astype(spec_ref.dtype)
        spec_ref[1, 0, 0, :, lanes] = out_imag[rows].astype(spec_ref.dtype)

    def tile_copy(step, d):
        return pltpu.make_async_copy(
            feat_scratch.at[d], out_ref.at[dest_ref[step * RADIX + d]], sems.at[d]
        )

    @pl.when(block > 0)
    def _():
        for d in range(RADIX):
            tile_copy(block - 1, d).wait()

    for d in range(RADIX):
        feat_scratch[d] = feature[d * rows_per : (d + 1) * rows_per]
    for d in range(RADIX):
        tile_copy(block, d).start()

    @pl.when(block == pl.num_programs(0) - 1)
    def _():
        for d in range(RADIX):
            tile_copy(block, d).wait()


def spectrum_call(products, table_sub, hops_total, dest, outgoing, spectrum, first_block, sensors):
    _, _, combos, rows, sub_n = products.shape
    per_device = rows // RADIX
    blocks = products.shape[1] * combos
    flat = products.reshape(2, blocks, rows, sub_n)
    index_b = jnp.arange(RADIX, dtype=jnp.int32)[:, None]
    index_p = jnp.arange(sub_n, dtype=jnp.int32)[None, :]
    twist_angle = 2.0 * math.pi / hops_total * (index_b * index_p % hops_total).astype(jnp.float32)
    norm_factor = 1.0 / math.sqrt(hops_total)
    twist_cos = jnp.tile(norm_factor * jnp.cos(twist_angle), (per_device, 1))
    twist_sin = jnp.tile(norm_factor * jnp.sin(twist_angle), (per_device, 1))
    mixers = section_mixers(RADIX, per_device)
    operands = [dest, flat, table_sub, table_sub, twist_cos, twist_sin, mixers, outgoing]
    in_specs = [
        pl.BlockSpec((2, 1, rows, sub_n), lambda i, dest: (0, i, 0, 0)),
        pl.BlockSpec((sub_n, sub_n), lambda i, dest: (0, 0)),
        pl.BlockSpec((sub_n, sub_n), lambda i, dest: (0, 1)),
        pl.BlockSpec((rows, sub_n), lambda i, dest: (0, 0)),
        pl.BlockSpec((rows, sub_n), lambda i, dest: (0, 0)),
        pl.BlockSpec((1, 2 * rows, 2 * rows), lambda i, dest: (0, 0, 0)),
        pl.BlockSpec(memory_space=pl.ANY),
    ]
    aliases = {7: 1}
    if spectrum is not None:
        operands.append(spectrum)
        in_specs.append(pl.BlockSpec(memory_space=pl.ANY))
        aliases[8] = 0
    spec_shape = (2, sensors, combos, per_device, RADIX * sub_n)
    grid_spec = pltpu.PrefetchScalarGridSpec(
        num_scalar_prefetch=1,
        grid=(blocks,),
        in_specs=in_specs,
        out_specs=[
            pl.BlockSpec(
                (2, 1, 1, per_device, RADIX * sub_n),
                lambda i, dest: (0, (i + first_block) // combos, (i + first_block) % combos, 0, 0),
            ),
            pl.BlockSpec(memory_space=pl.ANY),
        ],
        scratch_shapes=[
            pltpu.VMEM((RADIX, per_device, sub_n), jnp.bfloat16),
            pltpu.SemaphoreType.DMA((RADIX,)),
        ],
    )
    return pl.pallas_call(
        spectrum_kernel,
        grid_spec=grid_spec,
        out_shape=[
            jax.ShapeDtypeStruct(spec_shape, jnp.bfloat16),
            jax.ShapeDtypeStruct(outgoing.shape, jnp.bfloat16),
        ],
        input_output_aliases=aliases,
        compiler_params=pltpu.CompilerParams(
            vmem_limit_bytes=48 * 1024 * 1024,
            dimension_semantics=("arbitrary",),
        ),
        cost_estimate=pl.CostEstimate(
            flops=blocks * (8 * rows * sub_n * sub_n + 16 * rows * rows * sub_n),
            transcendentals=blocks * rows * sub_n,
            bytes_accessed=blocks * rows * sub_n * 2 * 5 + 4 * sub_n * sub_n,
        ),
    )(*operands)


def shards(frames, orders, owners, templates):
    rows_count = lax.axis_size("row")
    cols_count = lax.axis_size("col")
    devices_n = rows_count * cols_count
    sensors = frames.shape[0]
    hop_dev = frames.shape[1]
    frame_len = frames.shape[2]
    channels_n = 4 * frame_len
    hops_n = hop_dev * rows_count
    sub_n = hops_n // RADIX
    per_device = channels_n // devices_n
    local_channels = channels_n // cols_count
    combos = orders.shape[0] * orders.shape[1]
    feat_n = templates.shape[2]
    row_at = lax.axis_index("row")
    col_at = lax.axis_index("col")
    tail_frames = from_behind(frames[:, :3], "row", -1)
    padded = jnp.concatenate([frames, tail_frames], axis=1)
    column = jnp.arange(local_channels, dtype=jnp.int32)
    channel_ids = (column // per_device * cols_count + col_at) * per_device + column % per_device
    coefficients = channel_coefficients(channels_n, channel_ids)
    summed = jnp.zeros((sensors, 2 * local_channels, hop_dev), jnp.float32)
    for quarter in range(4):
        summed = summed + jnp.einsum(
            "shf,kf->skh",
            padded[:, quarter : quarter + hop_dev],
            coefficients[:, quarter * frame_len : (quarter + 1) * frame_len],
            preferred_element_type=jnp.float32,
        )
    hop_ids = row_at * hop_dev + jnp.arange(hop_dev, dtype=jnp.int32)
    real_part, imag_part = quarter_turn(
        summed[:, :local_channels], summed[:, local_channels:], channel_ids, hop_ids
    )
    demod = jnp.stack([real_part, imag_part]).astype(jnp.bfloat16)
    swapped = lax.all_to_all(demod, "row", split_axis=2, concat_axis=3, tiled=True)
    halves = 2
    part = sensors // halves
    pieces = []
    for half in range(halves):
        ordered = swapped[:, half * part : (half + 1) * part]
        ordered = ordered.reshape(2, part, per_device, sub_n, RADIX).transpose(0, 1, 2, 4, 3)
        above = from_behind_2(ordered, ("row", "col"), -1)
        extended = jnp.concatenate([ordered, above], axis=2)
        own_real = ordered[0].astype(jnp.float32)
        own_imag = ordered[1].astype(jnp.float32)
        prod_real = []
        prod_imag = []
        for wheel in range(orders.shape[0]):
            for order_at in range(orders.shape[1]):
                partner = lax.dynamic_slice_in_dim(
                    extended, orders[wheel, order_at], per_device, axis=2
                )
                partner = partner.astype(jnp.float32)
                prod_real.append(own_real * partner[0] + own_imag * partner[1])
                prod_imag.append(own_imag * partner[0] - own_real * partner[1])
        pieces.append(
            jnp.stack([jnp.stack(prod_real, axis=1), jnp.stack(prod_imag, axis=1)]).astype(
                jnp.bfloat16
            ).reshape(2, part, combos, per_device * RADIX, sub_n)
        )
    tiles_dev = sensors * combos * RADIX
    capacity = max(2, 2 * tiles_dev // devices_n)
    owner_ids = owners[:, 0]
    targets = jnp.arange(devices_n, dtype=jnp.int32)
    one_hot = (owner_ids[:, None] == targets[None, :]).astype(jnp.int32)
    before = jnp.cumsum(one_hot, axis=0) - one_hot
    slot_ids = jnp.sum(before * one_hot, axis=1)
    places = owner_ids * capacity + slot_ids
    table_sub = sub_coefficients(sub_n)
    tiles_part = tiles_dev // halves
    outgoing = jnp.zeros((devices_n * capacity, per_device, sub_n), jnp.bfloat16)
    spectrum = None
    for half in range(halves):
        spectrum, outgoing = spectrum_call(
            pieces[half],
            table_sub,
            hops_n,
            places[half * tiles_part : (half + 1) * tiles_part],
            outgoing,
            spectrum,
            half * part * combos,
            sensors,
        )
    outgoing = outgoing.reshape(devices_n, capacity * per_device, sub_n)
    arrived = lax.all_to_all(outgoing, ("row", "col"), split_axis=0, concat_axis=0, tiled=True)
    found = jnp.dot(
        arrived.reshape(-1, sub_n), templates[0], preferred_element_type=jnp.float32
    ).astype(jnp.bfloat16)
    found = found.reshape(devices_n, capacity, per_device, feat_n)
    return (spectrum, found[None])


def solution(mesh):
    in_specs = (P(None, "row", None), P(), P(("row", "col"), None), P(("row", "col"), None, None))
    out_specs = (
        P(None, None, None, ("row", "col"), None),
        P(("row", "col"), None, None, None, None),
    )
    return jax.shard_map(shards, mesh=mesh, in_specs=in_specs, out_specs=out_specs, check_vma=False)
```

```python
import math

import jax
import jax.numpy as jnp
from jax import lax
from jax.experimental import pallas as pl
from jax.experimental.pallas import tpu as pltpu
from jax.sharding import PartitionSpec as P
import numpy as np

RADIX = 8


def from_behind(block, axis, distance):
    devices = range(lax.axis_size(axis))
    route = [(i - distance, i) for i in devices if i - distance in devices]
    return lax.ppermute(block, axis, route)


def from_behind_2(value, axis, steps):
    count = lax.axis_size(axis)
    pairs = [(source, (source + steps) % count) for source in range(count)]
    return lax.ppermute(value, axis, pairs)


def channel_coefficients(n_total, channel_ids):
    lanes = 128
    position = jnp.arange(n_total, dtype=jnp.int32)
    high = jnp.arange(n_total // lanes, dtype=jnp.int32) * lanes
    low = jnp.arange(lanes, dtype=jnp.int32)
    step = 2.0 * math.pi / n_total
    high_angle = step * (channel_ids[:, None] * high[None, :] % n_total).astype(jnp.float32)
    low_angle = step * (channel_ids[:, None] * low[None, :] % n_total).astype(jnp.float32)
    high_cos, high_sin = jnp.cos(high_angle)[:, :, None], jnp.sin(high_angle)[:, :, None]
    low_cos, low_sin = jnp.cos(low_angle)[:, None], jnp.sin(low_angle)[:, None]
    cos_part = (high_cos * low_cos - high_sin * low_sin).reshape(-1, n_total)
    sin_part = (high_sin * low_cos + high_cos * low_sin).reshape(-1, n_total)
    window = 0.5 - 0.5 * jnp.cos(step * position.astype(jnp.float32))
    gain_factor = math.sqrt(8.0 / (3.0 * n_total))
    weighted = gain_factor * window[None, :]
    both = jnp.concatenate([weighted * cos_part, weighted * sin_part], axis=0)
    return both.astype(jnp.bfloat16)


def sub_coefficients(sub_total):
    index_a = jnp.arange(sub_total, dtype=jnp.int32)
    turns = index_a[:, None] * index_a[None, :] % sub_total
    phase_angle = 2.0 * math.pi / sub_total * turns.astype(jnp.float32)
    return jnp.concatenate([jnp.cos(phase_angle), jnp.sin(phase_angle)], axis=1).astype(
        jnp.bfloat16
    )


def quarter_turn(a_cos, a_sin, channel_ids, hop_ids):
    phase_step = channel_ids[:, None] % 4 * (hop_ids[None, :] % 4) % 4
    cos_quarter = (phase_step == 0).astype(jnp.float32) - (phase_step == 2).astype(jnp.float32)
    sin_quarter = (phase_step == 1).astype(jnp.float32) - (phase_step == 3).astype(jnp.float32)
    real_part = a_cos * cos_quarter - a_sin * sin_quarter
    imag_part = -a_sin * cos_quarter - a_cos * sin_quarter
    return (real_part, imag_part)


def section_mixers(radix_count, rows_per):
    index_b = np.arange(radix_count)
    angle = 2.0 * np.pi / radix_count * ((index_b[:, None] * index_b[None, :]) % radix_count)
    size = radix_count * rows_per
    tables = []
    for table in (np.cos(angle).astype(np.float32), np.sin(angle).astype(np.float32)):
        full = np.zeros((size, size), np.float32)
        for d in range(radix_count):
            for b in range(radix_count):
                for k in range(rows_per):
                    full[d * rows_per + k, k * radix_count + b] = table[b, d]
        tables.append(full)
    cos_full, sin_full = tables
    both = np.block([[cos_full, sin_full], [-sin_full, cos_full]])
    return jnp.asarray(both).astype(jnp.bfloat16)[None]


def spectrum_kernel(dest_ref, prod_ref, cos_ref, sin_ref, twc_ref, tws_ref, mix_ref, *refs):
    spec_ref, out_ref, feat_scratch, sems = refs[-4:]
    f32 = jnp.float32
    block = pl.program_id(0)
    rows_per = feat_scratch.shape[1]
    sub_n = feat_scratch.shape[2]
    rows_all = prod_ref.shape[2]
    both = jnp.concatenate([prod_ref[0, 0], prod_ref[1, 0]], axis=0)
    by_cos = jnp.dot(both, cos_ref[...], preferred_element_type=f32)
    by_sin = jnp.dot(both, sin_ref[...], preferred_element_type=f32)
    first_real = by_cos[:rows_all] + by_sin[rows_all:]
    first_imag = by_cos[rows_all:] - by_sin[:rows_all]
    twist_cos = twc_ref[...]
    twist_sin = tws_ref[...]
    twist_real = first_real * twist_cos + first_imag * twist_sin
    twist_imag = first_imag * twist_cos - first_real * twist_sin

    twist = jnp.concatenate([twist_real, twist_imag], axis=0)
    high = twist.astype(jnp.bfloat16)
    low = (twist - high.astype(f32)).astype(jnp.bfloat16)
    mixed = jnp.dot(mix_ref[0], high, preferred_element_type=f32) + jnp.dot(
        mix_ref[0], low, preferred_element_type=f32
    )
    out_real = mixed[:rows_all]
    out_imag = mixed[rows_all:]
    feature = jnp.log1p(out_real * out_real + out_imag * out_imag).astype(feat_scratch.dtype)
    for d in range(RADIX):
        rows = slice(d * rows_per, (d + 1) * rows_per)
        lanes = slice(d * sub_n, (d + 1) * sub_n)
        spec_ref[0, 0, 0, :, lanes] = out_real[rows].astype(spec_ref.dtype)
        spec_ref[1, 0, 0, :, lanes] = out_imag[rows].astype(spec_ref.dtype)

    def tile_copy(step, d):
        return pltpu.make_async_copy(
            feat_scratch.at[d], out_ref.at[dest_ref[step * RADIX + d]], sems.at[d]
        )

    @pl.when(block > 0)
    def _():
        for d in range(RADIX):
            tile_copy(block - 1, d).wait()

    for d in range(RADIX):
        feat_scratch[d] = feature[d * rows_per : (d + 1) * rows_per]
    for d in range(RADIX):
        tile_copy(block, d).start()

    @pl.when(block == pl.num_programs(0) - 1)
    def _():
        for d in range(RADIX):
            tile_copy(block, d).wait()


def spectrum_call(products, table_sub, hops_total, dest, outgoing, spectrum, first_block, sensors):
    _, _, combos, rows, sub_n = products.shape
    per_device = rows // RADIX
    blocks = products.shape[1] * combos
    flat = products.reshape(2, blocks, rows, sub_n)
    index_b = jnp.arange(RADIX, dtype=jnp.int32)[:, None]
    index_p = jnp.arange(sub_n, dtype=jnp.int32)[None, :]
    twist_angle = 2.0 * math.pi / hops_total * (index_b * index_p % hops_total).astype(jnp.float32)
    norm_factor = 1.0 / math.sqrt(hops_total)
    twist_cos = jnp.tile(norm_factor * jnp.cos(twist_angle), (per_device, 1))
    twist_sin = jnp.tile(norm_factor * jnp.sin(twist_angle), (per_device, 1))
    mixers = section_mixers(RADIX, per_device)
    operands = [dest, flat, table_sub, table_sub, twist_cos, twist_sin, mixers, outgoing]
    in_specs = [
        pl.BlockSpec((2, 1, rows, sub_n), lambda i, dest: (0, i, 0, 0)),
        pl.BlockSpec((sub_n, sub_n), lambda i, dest: (0, 0)),
        pl.BlockSpec((sub_n, sub_n), lambda i, dest: (0, 1)),
        pl.BlockSpec((rows, sub_n), lambda i, dest: (0, 0)),
        pl.BlockSpec((rows, sub_n), lambda i, dest: (0, 0)),
        pl.BlockSpec((1, 2 * rows, 2 * rows), lambda i, dest: (0, 0, 0)),
        pl.BlockSpec(memory_space=pl.ANY),
    ]
    aliases = {7: 1}
    if spectrum is not None:
        operands.append(spectrum)
        in_specs.append(pl.BlockSpec(memory_space=pl.ANY))
        aliases[8] = 0
    spec_shape = (2, sensors, combos, per_device, RADIX * sub_n)
    grid_spec = pltpu.PrefetchScalarGridSpec(
        num_scalar_prefetch=1,
        grid=(blocks,),
        in_specs=in_specs,
        out_specs=[
            pl.BlockSpec(
                (2, 1, 1, per_device, RADIX * sub_n),
                lambda i, dest: (0, (i + first_block) // combos, (i + first_block) % combos, 0, 0),
            ),
            pl.BlockSpec(memory_space=pl.ANY),
        ],
        scratch_shapes=[
            pltpu.VMEM((RADIX, per_device, sub_n), jnp.bfloat16),
            pltpu.SemaphoreType.DMA((RADIX,)),
        ],
    )
    return pl.pallas_call(
        spectrum_kernel,
        grid_spec=grid_spec,
        out_shape=[
            jax.ShapeDtypeStruct(spec_shape, jnp.bfloat16),
            jax.ShapeDtypeStruct(outgoing.shape, jnp.bfloat16),
        ],
        input_output_aliases=aliases,
        compiler_params=pltpu.CompilerParams(
            vmem_limit_bytes=48 * 1024 * 1024,
            dimension_semantics=("arbitrary",),
        ),
        cost_estimate=pl.CostEstimate(
            flops=blocks * (8 * rows * sub_n * sub_n + 16 * rows * rows * sub_n),
            transcendentals=blocks * rows * sub_n,
            bytes_accessed=blocks * rows * sub_n * 2 * 5 + 4 * sub_n * sub_n,
        ),
    )(*operands)


def shards_body(frames, orders, owners, templates):
    rows_count = lax.axis_size("row")
    cols_count = lax.axis_size("col")
    devices_n = rows_count * cols_count
    sensors = frames.shape[0]
    hop_dev = frames.shape[1]
    frame_len = frames.shape[2]
    channels_n = 4 * frame_len
    hops_n = hop_dev * rows_count
    sub_n = hops_n // RADIX
    per_device = channels_n // devices_n
    local_channels = channels_n // cols_count
    combos = orders.shape[0] * orders.shape[1]
    feat_n = templates.shape[2]
    row_at = lax.axis_index("row")
    col_at = lax.axis_index("col")
    tail_frames = from_behind(frames[:, :3], "row", -1)
    padded = jnp.concatenate([frames, tail_frames], axis=1)
    column = jnp.arange(local_channels, dtype=jnp.int32)
    channel_ids = (column // per_device * cols_count + col_at) * per_device + column % per_device
    coefficients = channel_coefficients(channels_n, channel_ids)
    summed = jnp.zeros((sensors, 2 * local_channels, hop_dev), jnp.float32)
    for quarter in range(4):
        summed = summed + jnp.einsum(
            "shf,kf->skh",
            padded[:, quarter : quarter + hop_dev],
            coefficients[:, quarter * frame_len : (quarter + 1) * frame_len],
            preferred_element_type=jnp.float32,
        )
    hop_ids = row_at * hop_dev + jnp.arange(hop_dev, dtype=jnp.int32)
    real_part, imag_part = quarter_turn(
        summed[:, :local_channels], summed[:, local_channels:], channel_ids, hop_ids
    )
    demod = jnp.stack([real_part, imag_part]).astype(jnp.bfloat16)
    swapped = lax.all_to_all(demod, "row", split_axis=2, concat_axis=3, tiled=True)
    halves = 2
    part = sensors // halves
    pieces = []
    for half in range(halves):
        ordered = swapped[:, half * part : (half + 1) * part]
        ordered = ordered.reshape(2, part, per_device, sub_n, RADIX).transpose(0, 1, 2, 4, 3)
        above = from_behind_2(ordered, ("row", "col"), -1)
        extended = jnp.concatenate([ordered, above], axis=2)
        own_real = ordered[0].astype(jnp.float32)
        own_imag = ordered[1].astype(jnp.float32)
        prod_real = []
        prod_imag = []
        for wheel in range(orders.shape[0]):
            for order_at in range(orders.shape[1]):
                partner = lax.dynamic_slice_in_dim(
                    extended, orders[wheel, order_at], per_device, axis=2
                )
                partner = partner.astype(jnp.float32)
                prod_real.append(own_real * partner[0] + own_imag * partner[1])
                prod_imag.append(own_imag * partner[0] - own_real * partner[1])
        pieces.append(
            jnp.stack([jnp.stack(prod_real, axis=1), jnp.stack(prod_imag, axis=1)]).astype(
                jnp.bfloat16
            ).reshape(2, part, combos, per_device * RADIX, sub_n)
        )
    tiles_dev = sensors * combos * RADIX
    capacity = max(2, 2 * tiles_dev // devices_n)
    owner_ids = owners[:, 0]
    targets = jnp.arange(devices_n, dtype=jnp.int32)
    one_hot = (owner_ids[:, None] == targets[None, :]).astype(jnp.int32)
    before = jnp.cumsum(one_hot, axis=0) - one_hot
    slot_ids = jnp.sum(before * one_hot, axis=1)
    places = owner_ids * capacity + slot_ids
    table_sub = sub_coefficients(sub_n)
    tiles_part = tiles_dev // halves
    outgoing = jnp.zeros((devices_n * capacity, per_device, sub_n), jnp.bfloat16)
    spectrum = None
    for half in range(halves):
        spectrum, outgoing = spectrum_call(
            pieces[half],
            table_sub,
            hops_n,
            places[half * tiles_part : (half + 1) * tiles_part],
            outgoing,
            spectrum,
            half * part * combos,
            sensors,
        )
    outgoing = outgoing.reshape(devices_n, capacity * per_device, sub_n)
    arrived = lax.all_to_all(outgoing, ("row", "col"), split_axis=0, concat_axis=0, tiled=True)
    found = jnp.dot(
        arrived.reshape(-1, sub_n), templates[0], preferred_element_type=jnp.float32
    ).astype(jnp.bfloat16)
    found = found.reshape(devices_n, capacity, per_device, feat_n)
    return (spectrum, found[None])


def solution(mesh):
    in_specs = (P(None, "row", None), P(), P(("row", "col"), None), P(("row", "col"), None, None))
    out_specs = (
        P(None, None, None, ("row", "col"), None),
        P(("row", "col"), None, None, None, None),
    )
    return jax.shard_map(shards_body, mesh=mesh, in_specs=in_specs, out_specs=out_specs, check_vma=False)
```

```python
import math

import jax
import jax.numpy as jnp
from jax import lax
from jax.experimental import pallas as pl
from jax.experimental.pallas import tpu as pltpu
from jax.sharding import PartitionSpec as P
import numpy as np

RADIX = 8


def from_behind(block, axis, distance):
    devices = range(lax.axis_size(axis))
    route = [(i - distance, i) for i in devices if i - distance in devices]
    return lax.ppermute(block, axis, route)


def from_behind_2(value, axis, steps):
    count = lax.axis_size(axis)
    pairs = [(source, (source + steps) % count) for source in range(count)]
    return lax.ppermute(value, axis, pairs)


def channel_coefficients(n_total, channel_ids):
    lanes = 128
    position = jnp.arange(n_total, dtype=jnp.int32)
    high = jnp.arange(n_total // lanes, dtype=jnp.int32) * lanes
    low = jnp.arange(lanes, dtype=jnp.int32)
    step = 2.0 * math.pi / n_total
    high_angle = step * (channel_ids[:, None] * high[None, :] % n_total).astype(jnp.float32)
    low_angle = step * (channel_ids[:, None] * low[None, :] % n_total).astype(jnp.float32)
    high_cos, high_sin = jnp.cos(high_angle)[:, :, None], jnp.sin(high_angle)[:, :, None]
    low_cos, low_sin = jnp.cos(low_angle)[:, None], jnp.sin(low_angle)[:, None]
    cos_part = (high_cos * low_cos - high_sin * low_sin).reshape(-1, n_total)
    sin_part = (high_sin * low_cos + high_cos * low_sin).reshape(-1, n_total)
    window = 0.5 - 0.5 * jnp.cos(step * position.astype(jnp.float32))
    gain_factor = math.sqrt(8.0 / (3.0 * n_total))
    weighted = gain_factor * window[None, :]
    both = jnp.concatenate([weighted * cos_part, weighted * sin_part], axis=0)
    return both.astype(jnp.bfloat16)


def sub_coefficients(sub_total):
    index_a = jnp.arange(sub_total, dtype=jnp.int32)
    turns = index_a[:, None] * index_a[None, :] % sub_total
    phase_angle = 2.0 * math.pi / sub_total * turns.astype(jnp.float32)
    return jnp.concatenate([jnp.cos(phase_angle), jnp.sin(phase_angle)], axis=1).astype(
        jnp.bfloat16
    )


def quarter_turn(a_cos, a_sin, channel_ids, hop_ids):
    phase_step = channel_ids[:, None] % 4 * (hop_ids[None, :] % 4) % 4
    cos_quarter = (phase_step == 0).astype(jnp.float32) - (phase_step == 2).astype(jnp.float32)
    sin_quarter = (phase_step == 1).astype(jnp.float32) - (phase_step == 3).astype(jnp.float32)
    real_part = a_cos * cos_quarter - a_sin * sin_quarter
    imag_part = -a_sin * cos_quarter - a_cos * sin_quarter
    return (real_part, imag_part)


def section_mixers(radix_count, rows_per):
    index_b = np.arange(radix_count)
    angle = 2.0 * np.pi / radix_count * ((index_b[:, None] * index_b[None, :]) % radix_count)
    size = radix_count * rows_per
    tables = []
    for table in (np.cos(angle).astype(np.float32), np.sin(angle).astype(np.float32)):
        full = np.zeros((size, size), np.float32)
        for d in range(radix_count):
            for b in range(radix_count):
                for k in range(rows_per):
                    full[d * rows_per + k, k * radix_count + b] = table[b, d]
        tables.append(full)
    cos_full, sin_full = tables
    both = np.block([[cos_full, sin_full], [-sin_full, cos_full]])
    return jnp.asarray(both).astype(jnp.bfloat16)[None]


def spectrum_kernel(dest_ref, prod_ref, cos_ref, sin_ref, twc_ref, tws_ref, mix_ref, *refs):
    spec_ref, out_ref, feat_scratch, sems = refs[-4:]
    f32 = jnp.float32
    block = pl.program_id(0)
    rows_per = feat_scratch.shape[1]
    sub_n = feat_scratch.shape[2]
    rows_all = prod_ref.shape[2]
    both = jnp.concatenate([prod_ref[0, 0], prod_ref[1, 0]], axis=0)
    by_cos = jnp.dot(both, cos_ref[...], preferred_element_type=f32)
    by_sin = jnp.dot(both, sin_ref[...], preferred_element_type=f32)
    first_real = by_cos[:rows_all] + by_sin[rows_all:]
    first_imag = by_cos[rows_all:] - by_sin[:rows_all]
    twist_cos = twc_ref[...]
    twist_sin = tws_ref[...]
    twist_real = first_real * twist_cos + first_imag * twist_sin
    twist_imag = first_imag * twist_cos - first_real * twist_sin

    twist = jnp.concatenate([twist_real, twist_imag], axis=0)
    high = twist.astype(jnp.bfloat16)
    low = (twist - high.astype(f32)).astype(jnp.bfloat16)
    mixed = jnp.dot(mix_ref[0], high, preferred_element_type=f32) + jnp.dot(
        mix_ref[0], low, preferred_element_type=f32
    )
    out_real = mixed[:rows_all]
    out_imag = mixed[rows_all:]
    feature = jnp.log1p(out_real * out_real + out_imag * out_imag).astype(feat_scratch.dtype)
    for d in range(RADIX):
        rows = slice(d * rows_per, (d + 1) * rows_per)
        lanes = slice(d * sub_n, (d + 1) * sub_n)
        spec_ref[0, 0, 0, :, lanes] = out_real[rows].astype(spec_ref.dtype)
        spec_ref[1, 0, 0, :, lanes] = out_imag[rows].astype(spec_ref.dtype)

    def tile_copy(step, d):
        return pltpu.make_async_copy(
            feat_scratch.at[d], out_ref.at[dest_ref[step * RADIX + d]], sems.at[d]
        )

    @pl.when(block > 0)
    def _():
        for d in range(RADIX):
            tile_copy(block - 1, d).wait()

    for d in range(RADIX):
        feat_scratch[d] = feature[d * rows_per : (d + 1) * rows_per]
    for d in range(RADIX):
        tile_copy(block, d).start()

    @pl.when(block == pl.num_programs(0) - 1)
    def _():
        for d in range(RADIX):
            tile_copy(block, d).wait()


def spectrum_call(products, table_sub, hops_total, dest, outgoing, spectrum, first_block, sensors):
    _, _, combos, rows, sub_n = products.shape
    per_device = rows // RADIX
    blocks = products.shape[1] * combos
    flat = products.reshape(2, blocks, rows, sub_n)
    index_b = jnp.arange(RADIX, dtype=jnp.int32)[:, None]
    index_p = jnp.arange(sub_n, dtype=jnp.int32)[None, :]
    twist_angle = 2.0 * math.pi / hops_total * (index_b * index_p % hops_total).astype(jnp.float32)
    norm_factor = 1.0 / math.sqrt(hops_total)
    twist_cos = jnp.tile(norm_factor * jnp.cos(twist_angle), (per_device, 1))
    twist_sin = jnp.tile(norm_factor * jnp.sin(twist_angle), (per_device, 1))
    mixers = section_mixers(RADIX, per_device)
    operands = [dest, flat, table_sub, table_sub, twist_cos, twist_sin, mixers, outgoing]
    in_specs = [
        pl.BlockSpec((2, 1, rows, sub_n), lambda i, dest: (0, i, 0, 0)),
        pl.BlockSpec((sub_n, sub_n), lambda i, dest: (0, 0)),
        pl.BlockSpec((sub_n, sub_n), lambda i, dest: (0, 1)),
        pl.BlockSpec((rows, sub_n), lambda i, dest: (0, 0)),
        pl.BlockSpec((rows, sub_n), lambda i, dest: (0, 0)),
        pl.BlockSpec((1, 2 * rows, 2 * rows), lambda i, dest: (0, 0, 0)),
        pl.BlockSpec(memory_space=pl.ANY),
    ]
    aliases = {7: 1}
    if spectrum is not None:
        operands.append(spectrum)
        in_specs.append(pl.BlockSpec(memory_space=pl.ANY))
        aliases[8] = 0
    spec_shape = (2, sensors, combos, per_device, RADIX * sub_n)
    grid_spec = pltpu.PrefetchScalarGridSpec(
        num_scalar_prefetch=1,
        grid=(blocks,),
        in_specs=in_specs,
        out_specs=[
            pl.BlockSpec(
                (2, 1, 1, per_device, RADIX * sub_n),
                lambda i, dest: (0, (i + first_block) // combos, (i + first_block) % combos, 0, 0),
            ),
            pl.BlockSpec(memory_space=pl.ANY),
        ],
        scratch_shapes=[
            pltpu.VMEM((RADIX, per_device, sub_n), jnp.bfloat16),
            pltpu.SemaphoreType.DMA((RADIX,)),
        ],
    )
    return pl.pallas_call(
        spectrum_kernel,
        grid_spec=grid_spec,
        out_shape=[
            jax.ShapeDtypeStruct(spec_shape, jnp.bfloat16),
            jax.ShapeDtypeStruct(outgoing.shape, jnp.bfloat16),
        ],
        input_output_aliases=aliases,
        compiler_params=pltpu.CompilerParams(
            vmem_limit_bytes=48 * 1024 * 1024,
            dimension_semantics=("arbitrary",),
        ),
        cost_estimate=pl.CostEstimate(
            flops=blocks * (8 * rows * sub_n * sub_n + 16 * rows * rows * sub_n),
            transcendentals=blocks * rows * sub_n,
            bytes_accessed=blocks * rows * sub_n * 2 * 5 + 4 * sub_n * sub_n,
        ),
    )(*operands)


def shards_body(frames, orders, owners, templates):
    rows_count = lax.axis_size("row")
    cols_count = lax.axis_size("col")
    devices_n = rows_count * cols_count
    sensors = frames.shape[0]
    hop_dev = frames.shape[1]
    frame_len = frames.shape[2]
    channels_n = 4 * frame_len
    hops_n = hop_dev * rows_count
    sub_n = hops_n // RADIX
    per_device = channels_n // devices_n
    local_channels = channels_n // cols_count
    combos = orders.shape[0] * orders.shape[1]
    feat_n = templates.shape[2]
    row_at = lax.axis_index("row")
    col_at = lax.axis_index("col")
    tail_frames = from_behind(frames[:, :3], "row", -1)
    padded = jnp.concatenate([frames, tail_frames], axis=1)
    column = jnp.arange(local_channels, dtype=jnp.int32)
    channel_ids = (column // per_device * cols_count + col_at) * per_device + column % per_device
    coefficients = channel_coefficients(channels_n, channel_ids)
    summed = jnp.zeros((sensors, 2 * local_channels, hop_dev), jnp.float32)
    for quarter in range(4):
        summed = summed + jnp.einsum(
            "shf,kf->skh",
            padded[:, quarter : quarter + hop_dev],
            coefficients[:, quarter * frame_len : (quarter + 1) * frame_len],
            preferred_element_type=jnp.float32,
        )
    hop_ids = row_at * hop_dev + jnp.arange(hop_dev, dtype=jnp.int32)
    real_part, imag_part = quarter_turn(
        summed[:, :local_channels], summed[:, local_channels:], channel_ids, hop_ids
    )
    demod = jnp.stack([real_part, imag_part]).astype(jnp.bfloat16)
    split_parts = []
    for half in range(2):
        piece = demod[:, half * (sensors // 2) : (half + 1) * (sensors // 2)]
        split_parts.append(lax.all_to_all(piece, "row", split_axis=2, concat_axis=3, tiled=True))
    halves = 2
    part = sensors // halves
    pieces = []
    for half in range(halves):
        ordered = split_parts[half]
        ordered = ordered.reshape(2, part, per_device, sub_n, RADIX).transpose(0, 1, 2, 4, 3)
        above = from_behind_2(ordered, ("row", "col"), -1)
        extended = jnp.concatenate([ordered, above], axis=2)
        own_real = ordered[0].astype(jnp.float32)
        own_imag = ordered[1].astype(jnp.float32)
        prod_real = []
        prod_imag = []
        for wheel in range(orders.shape[0]):
            for order_at in range(orders.shape[1]):
                partner = lax.dynamic_slice_in_dim(
                    extended, orders[wheel, order_at], per_device, axis=2
                )
                partner = partner.astype(jnp.float32)
                prod_real.append(own_real * partner[0] + own_imag * partner[1])
                prod_imag.append(own_imag * partner[0] - own_real * partner[1])
        pieces.append(
            jnp.stack([jnp.stack(prod_real, axis=1), jnp.stack(prod_imag, axis=1)]).astype(
                jnp.bfloat16
            ).reshape(2, part, combos, per_device * RADIX, sub_n)
        )
    tiles_dev = sensors * combos * RADIX
    capacity = max(2, 2 * tiles_dev // devices_n)
    owner_ids = owners[:, 0]
    targets = jnp.arange(devices_n, dtype=jnp.int32)
    one_hot = (owner_ids[:, None] == targets[None, :]).astype(jnp.int32)
    before = jnp.cumsum(one_hot, axis=0) - one_hot
    slot_ids = jnp.sum(before * one_hot, axis=1)
    places = owner_ids * capacity + slot_ids
    table_sub = sub_coefficients(sub_n)
    tiles_part = tiles_dev // halves
    outgoing = jnp.zeros((devices_n * capacity, per_device, sub_n), jnp.bfloat16)
    spectrum = None
    for half in range(halves):
        spectrum, outgoing = spectrum_call(
            pieces[half],
            table_sub,
            hops_n,
            places[half * tiles_part : (half + 1) * tiles_part],
            outgoing,
            spectrum,
            half * part * combos,
            sensors,
        )
    outgoing = outgoing.reshape(devices_n, capacity * per_device, sub_n)
    arrived = lax.all_to_all(outgoing, ("row", "col"), split_axis=0, concat_axis=0, tiled=True)
    found = jnp.dot(
        arrived.reshape(-1, sub_n), templates[0], preferred_element_type=jnp.float32
    ).astype(jnp.bfloat16)
    found = found.reshape(devices_n, capacity, per_device, feat_n)
    return (spectrum, found[None])


def solution(mesh):
    in_specs = (P(None, "row", None), P(), P(("row", "col"), None), P(("row", "col"), None, None))
    out_specs = (
        P(None, None, None, ("row", "col"), None),
        P(("row", "col"), None, None, None, None),
    )
    return jax.shard_map(shards_body, mesh=mesh, in_specs=in_specs, out_specs=out_specs, check_vma=False)
```

```python
import math

import jax
import jax.numpy as jnp
from jax import lax
from jax.experimental import pallas as pl
from jax.experimental.pallas import tpu as pltpu
from jax.sharding import PartitionSpec as P
import numpy as np

RADIX = 8


def from_behind(block, axis, distance):
    devices = range(lax.axis_size(axis))
    route = [(i - distance, i) for i in devices if i - distance in devices]
    return lax.ppermute(block, axis, route)


def from_behind_2(value, axis, steps):
    count = lax.axis_size(axis)
    pairs = [(source, (source + steps) % count) for source in range(count)]
    return lax.ppermute(value, axis, pairs)


def channel_coefficients(n_total, channel_ids):
    lanes = 128
    position = jnp.arange(n_total, dtype=jnp.int32)
    high = jnp.arange(n_total // lanes, dtype=jnp.int32) * lanes
    low = jnp.arange(lanes, dtype=jnp.int32)
    step = 2.0 * math.pi / n_total
    high_angle = step * (channel_ids[:, None] * high[None, :] % n_total).astype(jnp.float32)
    low_angle = step * (channel_ids[:, None] * low[None, :] % n_total).astype(jnp.float32)
    high_cos, high_sin = jnp.cos(high_angle)[:, :, None], jnp.sin(high_angle)[:, :, None]
    low_cos, low_sin = jnp.cos(low_angle)[:, None], jnp.sin(low_angle)[:, None]
    cos_part = (high_cos * low_cos - high_sin * low_sin).reshape(-1, n_total)
    sin_part = (high_sin * low_cos + high_cos * low_sin).reshape(-1, n_total)
    window = 0.5 - 0.5 * jnp.cos(step * position.astype(jnp.float32))
    gain_factor = math.sqrt(8.0 / (3.0 * n_total))
    weighted = gain_factor * window[None, :]
    both = jnp.concatenate([weighted * cos_part, weighted * sin_part], axis=0)
    return both.astype(jnp.bfloat16)


def sub_coefficients(sub_total):
    index_a = jnp.arange(sub_total, dtype=jnp.int32)
    turns = index_a[:, None] * index_a[None, :] % sub_total
    phase_angle = 2.0 * math.pi / sub_total * turns.astype(jnp.float32)
    return jnp.concatenate([jnp.cos(phase_angle), jnp.sin(phase_angle)], axis=1).astype(
        jnp.bfloat16
    )


def quarter_turn(a_cos, a_sin, channel_ids, hop_ids):
    phase_step = channel_ids[:, None] % 4 * (hop_ids[None, :] % 4) % 4
    cos_quarter = (phase_step == 0).astype(jnp.float32) - (phase_step == 2).astype(jnp.float32)
    sin_quarter = (phase_step == 1).astype(jnp.float32) - (phase_step == 3).astype(jnp.float32)
    real_part = a_cos * cos_quarter - a_sin * sin_quarter
    imag_part = -a_sin * cos_quarter - a_cos * sin_quarter
    return (real_part, imag_part)


def section_mixers(radix_count, rows_per):
    index_b = np.arange(radix_count)
    angle = 2.0 * np.pi / radix_count * ((index_b[:, None] * index_b[None, :]) % radix_count)
    size = radix_count * rows_per
    tables = []
    for table in (np.cos(angle).astype(np.float32), np.sin(angle).astype(np.float32)):
        full = np.zeros((size, size), np.float32)
        for d in range(radix_count):
            for b in range(radix_count):
                for k in range(rows_per):
                    full[d * rows_per + k, k * radix_count + b] = table[b, d]
        tables.append(full)
    cos_full, sin_full = tables
    both = np.block([[cos_full, sin_full], [-sin_full, cos_full]])
    return jnp.asarray(both).astype(jnp.bfloat16)[None]


def spectrum_kernel(dest_ref, prod_ref, cos_ref, sin_ref, twc_ref, tws_ref, mix_ref, *refs):
    spec_ref, out_ref, feat_scratch, sems = refs[-4:]
    f32 = jnp.float32
    block = pl.program_id(0)
    rows_per = feat_scratch.shape[1]
    sub_n = feat_scratch.shape[2]
    rows_all = prod_ref.shape[2]
    both = jnp.concatenate([prod_ref[0, 0], prod_ref[1, 0]], axis=0)
    by_cos = jnp.dot(both, cos_ref[...], preferred_element_type=f32)
    by_sin = jnp.dot(both, sin_ref[...], preferred_element_type=f32)
    first_real = by_cos[:rows_all] + by_sin[rows_all:]
    first_imag = by_cos[rows_all:] - by_sin[:rows_all]
    twist_cos = twc_ref[...]
    twist_sin = tws_ref[...]
    twist_real = first_real * twist_cos + first_imag * twist_sin
    twist_imag = first_imag * twist_cos - first_real * twist_sin

    twist = jnp.concatenate([twist_real, twist_imag], axis=0)
    mixed = jnp.dot(mix_ref[0], twist.astype(jnp.bfloat16), preferred_element_type=f32)
    out_real = mixed[:rows_all]
    out_imag = mixed[rows_all:]
    feature = jnp.log1p(out_real * out_real + out_imag * out_imag).astype(feat_scratch.dtype)
    for d in range(RADIX):
        rows = slice(d * rows_per, (d + 1) * rows_per)
        lanes = slice(d * sub_n, (d + 1) * sub_n)
        spec_ref[0, 0, 0, :, lanes] = out_real[rows].astype(spec_ref.dtype)
        spec_ref[1, 0, 0, :, lanes] = out_imag[rows].astype(spec_ref.dtype)

    def tile_copy(step, d):
        return pltpu.make_async_copy(
            feat_scratch.at[d], out_ref.at[dest_ref[step * RADIX + d]], sems.at[d]
        )

    @pl.when(block > 0)
    def _():
        for d in range(RADIX):
            tile_copy(block - 1, d).wait()

    for d in range(RADIX):
        feat_scratch[d] = feature[d * rows_per : (d + 1) * rows_per]
    for d in range(RADIX):
        tile_copy(block, d).start()

    @pl.when(block == pl.num_programs(0) - 1)
    def _():
        for d in range(RADIX):
            tile_copy(block, d).wait()


def spectrum_call(products, table_sub, hops_total, dest, outgoing, spectrum, first_block, sensors):
    _, _, combos, rows, sub_n = products.shape
    per_device = rows // RADIX
    blocks = products.shape[1] * combos
    flat = products.reshape(2, blocks, rows, sub_n)
    index_b = jnp.arange(RADIX, dtype=jnp.int32)[:, None]
    index_p = jnp.arange(sub_n, dtype=jnp.int32)[None, :]
    twist_angle = 2.0 * math.pi / hops_total * (index_b * index_p % hops_total).astype(jnp.float32)
    norm_factor = 1.0 / math.sqrt(hops_total)
    twist_cos = jnp.tile(norm_factor * jnp.cos(twist_angle), (per_device, 1))
    twist_sin = jnp.tile(norm_factor * jnp.sin(twist_angle), (per_device, 1))
    mixers = section_mixers(RADIX, per_device)
    operands = [dest, flat, table_sub, table_sub, twist_cos, twist_sin, mixers, outgoing]
    in_specs = [
        pl.BlockSpec((2, 1, rows, sub_n), lambda i, dest: (0, i, 0, 0)),
        pl.BlockSpec((sub_n, sub_n), lambda i, dest: (0, 0)),
        pl.BlockSpec((sub_n, sub_n), lambda i, dest: (0, 1)),
        pl.BlockSpec((rows, sub_n), lambda i, dest: (0, 0)),
        pl.BlockSpec((rows, sub_n), lambda i, dest: (0, 0)),
        pl.BlockSpec((1, 2 * rows, 2 * rows), lambda i, dest: (0, 0, 0)),
        pl.BlockSpec(memory_space=pl.ANY),
    ]
    aliases = {7: 1}
    if spectrum is not None:
        operands.append(spectrum)
        in_specs.append(pl.BlockSpec(memory_space=pl.ANY))
        aliases[8] = 0
    spec_shape = (2, sensors, combos, per_device, RADIX * sub_n)
    grid_spec = pltpu.PrefetchScalarGridSpec(
        num_scalar_prefetch=1,
        grid=(blocks,),
        in_specs=in_specs,
        out_specs=[
            pl.BlockSpec(
                (2, 1, 1, per_device, RADIX * sub_n),
                lambda i, dest: (0, (i + first_block) // combos, (i + first_block) % combos, 0, 0),
            ),
            pl.BlockSpec(memory_space=pl.ANY),
        ],
        scratch_shapes=[
            pltpu.VMEM((RADIX, per_device, sub_n), jnp.bfloat16),
            pltpu.SemaphoreType.DMA((RADIX,)),
        ],
    )
    return pl.pallas_call(
        spectrum_kernel,
        grid_spec=grid_spec,
        out_shape=[
            jax.ShapeDtypeStruct(spec_shape, jnp.bfloat16),
            jax.ShapeDtypeStruct(outgoing.shape, jnp.bfloat16),
        ],
        input_output_aliases=aliases,
        compiler_params=pltpu.CompilerParams(
            vmem_limit_bytes=48 * 1024 * 1024,
            dimension_semantics=("arbitrary",),
            allow_input_fusion=[index == 1 for index in range(len(operands))],
        ),
        cost_estimate=pl.CostEstimate(
            flops=blocks * (8 * rows * sub_n * sub_n + 8 * rows * rows * sub_n),
            transcendentals=blocks * rows * sub_n,
            bytes_accessed=blocks * rows * sub_n * 2 * 5 + 4 * sub_n * sub_n,
        ),
    )(*operands)


def shards_body(frames, orders, owners, templates):
    rows_count = lax.axis_size("row")
    cols_count = lax.axis_size("col")
    devices_n = rows_count * cols_count
    sensors = frames.shape[0]
    hop_dev = frames.shape[1]
    frame_len = frames.shape[2]
    channels_n = 4 * frame_len
    hops_n = hop_dev * rows_count
    sub_n = hops_n // RADIX
    per_device = channels_n // devices_n
    local_channels = channels_n // cols_count
    combos = orders.shape[0] * orders.shape[1]
    feat_n = templates.shape[2]
    row_at = lax.axis_index("row")
    col_at = lax.axis_index("col")
    tail_frames = from_behind(frames[:, :3], "row", -1)
    padded = jnp.concatenate([frames, tail_frames], axis=1)
    column = jnp.arange(local_channels, dtype=jnp.int32)
    channel_ids = (column // per_device * cols_count + col_at) * per_device + column % per_device
    coefficients = channel_coefficients(channels_n, channel_ids)
    summed = jnp.zeros((sensors, 2 * local_channels, hop_dev), jnp.float32)
    for quarter in range(4):
        summed = summed + jnp.einsum(
            "shf,kf->skh",
            padded[:, quarter : quarter + hop_dev],
            coefficients[:, quarter * frame_len : (quarter + 1) * frame_len],
            preferred_element_type=jnp.float32,
        )
    hop_ids = row_at * hop_dev + jnp.arange(hop_dev, dtype=jnp.int32)
    real_part, imag_part = quarter_turn(
        summed[:, :local_channels], summed[:, local_channels:], channel_ids, hop_ids
    )
    demod = jnp.stack([real_part, imag_part]).astype(jnp.bfloat16)
    swapped = lax.all_to_all(demod, "row", split_axis=2, concat_axis=3, tiled=True)
    halves = 2
    part = sensors // halves
    pieces = []
    for half in range(halves):
        ordered = swapped[:, half * part : (half + 1) * part]
        ordered = ordered.reshape(2, part, per_device, sub_n, RADIX).transpose(0, 1, 2, 4, 3)
        above = from_behind_2(ordered, ("row", "col"), -1)
        extended = jnp.concatenate([ordered, above], axis=2)
        own_real = ordered[0].astype(jnp.float32)
        own_imag = ordered[1].astype(jnp.float32)
        prod_real = []
        prod_imag = []
        for wheel in range(orders.shape[0]):
            for order_at in range(orders.shape[1]):
                partner = lax.dynamic_slice_in_dim(
                    extended, orders[wheel, order_at], per_device, axis=2
                )
                partner = partner.astype(jnp.float32)
                prod_real.append(own_real * partner[0] + own_imag * partner[1])
                prod_imag.append(own_imag * partner[0] - own_real * partner[1])
        pieces.append(
            jnp.stack([jnp.stack(prod_real, axis=1), jnp.stack(prod_imag, axis=1)]).astype(
                jnp.bfloat16
            ).reshape(2, part, combos, per_device * RADIX, sub_n)
        )
    tiles_dev = sensors * combos * RADIX
    capacity = max(2, 2 * tiles_dev // devices_n)
    owner_ids = owners[:, 0]
    targets = jnp.arange(devices_n, dtype=jnp.int32)
    one_hot = (owner_ids[:, None] == targets[None, :]).astype(jnp.int32)
    before = jnp.cumsum(one_hot, axis=0) - one_hot
    slot_ids = jnp.sum(before * one_hot, axis=1)
    places = owner_ids * capacity + slot_ids
    table_sub = sub_coefficients(sub_n)
    tiles_part = tiles_dev // halves
    outgoing = jnp.zeros((devices_n * capacity, per_device, sub_n), jnp.bfloat16)
    spectrum = None
    for half in range(halves):
        spectrum, outgoing = spectrum_call(
            pieces[half],
            table_sub,
            hops_n,
            places[half * tiles_part : (half + 1) * tiles_part],
            outgoing,
            spectrum,
            half * part * combos,
            sensors,
        )
    outgoing = outgoing.reshape(devices_n, capacity * per_device, sub_n)
    arrived = lax.all_to_all(outgoing, ("row", "col"), split_axis=0, concat_axis=0, tiled=True)
    found = jnp.dot(
        arrived.reshape(-1, sub_n), templates[0], preferred_element_type=jnp.float32
    ).astype(jnp.bfloat16)
    found = found.reshape(devices_n, capacity, per_device, feat_n)
    return (spectrum, found[None])


def solution(mesh):
    in_specs = (P(None, "row", None), P(), P(("row", "col"), None), P(("row", "col"), None, None))
    out_specs = (
        P(None, None, None, ("row", "col"), None),
        P(("row", "col"), None, None, None, None),
    )
    return jax.shard_map(shards_body, mesh=mesh, in_specs=in_specs, out_specs=out_specs, check_vma=False)
```

```python
import math

import jax
import jax.numpy as jnp
from jax import lax
from jax.experimental import pallas as pl
from jax.experimental.pallas import tpu as pltpu
from jax.sharding import PartitionSpec as P
import numpy as np

RADIX = 8


def from_behind(block, axis, distance):
    devices = range(lax.axis_size(axis))
    route = [(i - distance, i) for i in devices if i - distance in devices]
    return lax.ppermute(block, axis, route)


def from_behind_2(value, axis, steps):
    count = lax.axis_size(axis)
    pairs = [(source, (source + steps) % count) for source in range(count)]
    return lax.ppermute(value, axis, pairs)


def channel_coefficients(n_total, channel_ids):
    lanes = 128
    position = jnp.arange(n_total, dtype=jnp.int32)
    high = jnp.arange(n_total // lanes, dtype=jnp.int32) * lanes
    low = jnp.arange(lanes, dtype=jnp.int32)
    step = 2.0 * math.pi / n_total
    high_angle = step * (channel_ids[:, None] * high[None, :] % n_total).astype(jnp.float32)
    low_angle = step * (channel_ids[:, None] * low[None, :] % n_total).astype(jnp.float32)
    high_cos, high_sin = jnp.cos(high_angle)[:, :, None], jnp.sin(high_angle)[:, :, None]
    low_cos, low_sin = jnp.cos(low_angle)[:, None], jnp.sin(low_angle)[:, None]
    cos_part = (high_cos * low_cos - high_sin * low_sin).reshape(-1, n_total)
    sin_part = (high_sin * low_cos + high_cos * low_sin).reshape(-1, n_total)
    window = 0.5 - 0.5 * jnp.cos(step * position.astype(jnp.float32))
    gain_factor = math.sqrt(8.0 / (3.0 * n_total))
    weighted = gain_factor * window[None, :]
    both = jnp.concatenate([weighted * cos_part, weighted * sin_part], axis=0)
    return both.astype(jnp.bfloat16)


def sub_coefficients(sub_total):
    index_a = jnp.arange(sub_total, dtype=jnp.int32)
    turns = index_a[:, None] * index_a[None, :] % sub_total
    phase_angle = 2.0 * math.pi / sub_total * turns.astype(jnp.float32)
    return jnp.concatenate([jnp.cos(phase_angle), jnp.sin(phase_angle)], axis=1).astype(
        jnp.bfloat16
    )


def quarter_turn(a_cos, a_sin, channel_ids, hop_ids):
    phase_step = channel_ids[:, None] % 4 * (hop_ids[None, :] % 4) % 4
    cos_quarter = (phase_step == 0).astype(jnp.float32) - (phase_step == 2).astype(jnp.float32)
    sin_quarter = (phase_step == 1).astype(jnp.float32) - (phase_step == 3).astype(jnp.float32)
    real_part = a_cos * cos_quarter - a_sin * sin_quarter
    imag_part = -a_sin * cos_quarter - a_cos * sin_quarter
    return (real_part, imag_part)


def section_mixers(radix_count, rows_per):
    index_b = np.arange(radix_count)
    angle = 2.0 * np.pi / radix_count * ((index_b[:, None] * index_b[None, :]) % radix_count)
    size = radix_count * rows_per
    tables = []
    for table in (np.cos(angle).astype(np.float32), np.sin(angle).astype(np.float32)):
        full = np.zeros((size, size), np.float32)
        for d in range(radix_count):
            for b in range(radix_count):
                for k in range(rows_per):
                    full[d * rows_per + k, k * radix_count + b] = table[b, d]
        tables.append(full)
    cos_full, sin_full = tables
    both = np.block([[cos_full, sin_full], [-sin_full, cos_full]])
    return jnp.asarray(both).astype(jnp.bfloat16)[None]


def spectrum_kernel(dest_ref, prod_ref, cos_ref, sin_ref, twc_ref, tws_ref, mix_ref, *refs):
    spec_ref, out_ref, feat_scratch, sems = refs[-4:]
    f32 = jnp.float32
    block = pl.program_id(0)
    rows_per = feat_scratch.shape[1]
    sub_n = feat_scratch.shape[2]
    rows_all = prod_ref.shape[2]
    both = jnp.concatenate([prod_ref[0, 0], prod_ref[1, 0]], axis=0)
    by_cos = jnp.dot(both, cos_ref[...], preferred_element_type=f32)
    by_sin = jnp.dot(both, sin_ref[...], preferred_element_type=f32)
    first_real = by_cos[:rows_all] + by_sin[rows_all:]
    first_imag = by_cos[rows_all:] - by_sin[:rows_all]
    twist_cos = twc_ref[...]
    twist_sin = tws_ref[...]
    twist_real = first_real * twist_cos + first_imag * twist_sin
    twist_imag = first_imag * twist_cos - first_real * twist_sin

    twist = jnp.concatenate([twist_real, twist_imag], axis=0)
    mixed = jnp.dot(mix_ref[0], twist.astype(jnp.bfloat16), preferred_element_type=f32)
    out_real = mixed[:rows_all]
    out_imag = mixed[rows_all:]
    feature = jnp.log1p(out_real * out_real + out_imag * out_imag).astype(feat_scratch.dtype)
    for d in range(RADIX):
        rows = slice(d * rows_per, (d + 1) * rows_per)
        lanes = slice(d * sub_n, (d + 1) * sub_n)
        spec_ref[0, 0, 0, :, lanes] = out_real[rows].astype(spec_ref.dtype)
        spec_ref[1, 0, 0, :, lanes] = out_imag[rows].astype(spec_ref.dtype)

    def tile_copy(step, d):
        return pltpu.make_async_copy(
            feat_scratch.at[d], out_ref.at[dest_ref[step * RADIX + d]], sems.at[d]
        )

    @pl.when(block > 0)
    def _():
        for d in range(RADIX):
            tile_copy(block - 1, d).wait()

    for d in range(RADIX):
        feat_scratch[d] = feature[d * rows_per : (d + 1) * rows_per]
    for d in range(RADIX):
        tile_copy(block, d).start()

    @pl.when(block == pl.num_programs(0) - 1)
    def _():
        for d in range(RADIX):
            tile_copy(block, d).wait()


def spectrum_call(products, table_sub, hops_total, dest, outgoing, spectrum, first_block, sensors):
    _, _, combos, rows, sub_n = products.shape
    per_device = rows // RADIX
    blocks = products.shape[1] * combos
    flat = products.reshape(2, blocks, rows, sub_n)
    index_b = jnp.arange(RADIX, dtype=jnp.int32)[:, None]
    index_p = jnp.arange(sub_n, dtype=jnp.int32)[None, :]
    twist_angle = 2.0 * math.pi / hops_total * (index_b * index_p % hops_total).astype(jnp.float32)
    norm_factor = 1.0 / math.sqrt(hops_total)
    twist_cos = jnp.tile(norm_factor * jnp.cos(twist_angle), (per_device, 1))
    twist_sin = jnp.tile(norm_factor * jnp.sin(twist_angle), (per_device, 1))
    mixers = section_mixers(RADIX, per_device)
    operands = [dest, flat, table_sub, table_sub, twist_cos, twist_sin, mixers, outgoing]
    in_specs = [
        pl.BlockSpec((2, 1, rows, sub_n), lambda i, dest: (0, i, 0, 0)),
        pl.BlockSpec((sub_n, sub_n), lambda i, dest: (0, 0)),
        pl.BlockSpec((sub_n, sub_n), lambda i, dest: (0, 1)),
        pl.BlockSpec((rows, sub_n), lambda i, dest: (0, 0)),
        pl.BlockSpec((rows, sub_n), lambda i, dest: (0, 0)),
        pl.BlockSpec((1, 2 * rows, 2 * rows), lambda i, dest: (0, 0, 0)),
        pl.BlockSpec(memory_space=pl.ANY),
    ]
    aliases = {7: 1}
    if spectrum is not None:
        operands.append(spectrum)
        in_specs.append(pl.BlockSpec(memory_space=pl.ANY))
        aliases[8] = 0
    spec_shape = (2, sensors, combos, per_device, RADIX * sub_n)
    grid_spec = pltpu.PrefetchScalarGridSpec(
        num_scalar_prefetch=1,
        grid=(blocks,),
        in_specs=in_specs,
        out_specs=[
            pl.BlockSpec(
                (2, 1, 1, per_device, RADIX * sub_n),
                lambda i, dest: (0, (i + first_block) // combos, (i + first_block) % combos, 0, 0),
            ),
            pl.BlockSpec(memory_space=pl.ANY),
        ],
        scratch_shapes=[
            pltpu.VMEM((RADIX, per_device, sub_n), jnp.bfloat16),
            pltpu.SemaphoreType.DMA((RADIX,)),
        ],
    )
    return pl.pallas_call(
        spectrum_kernel,
        grid_spec=grid_spec,
        out_shape=[
            jax.ShapeDtypeStruct(spec_shape, jnp.bfloat16),
            jax.ShapeDtypeStruct(outgoing.shape, jnp.bfloat16),
        ],
        input_output_aliases=aliases,
        compiler_params=pltpu.CompilerParams(
            vmem_limit_bytes=48 * 1024 * 1024,
            dimension_semantics=("arbitrary",),
            allow_input_fusion=[index == 1 for index in range(len(operands))],
        ),
        cost_estimate=pl.CostEstimate(
            flops=blocks * (8 * rows * sub_n * sub_n + 8 * rows * rows * sub_n),
            transcendentals=blocks * rows * sub_n,
            bytes_accessed=blocks * rows * sub_n * 2 * 5 + 4 * sub_n * sub_n,
        ),
    )(*operands)


def shards_body(frames, orders, owners, templates):
    rows_count = lax.axis_size("row")
    cols_count = lax.axis_size("col")
    devices_n = rows_count * cols_count
    sensors = frames.shape[0]
    hop_dev = frames.shape[1]
    frame_len = frames.shape[2]
    channels_n = 4 * frame_len
    hops_n = hop_dev * rows_count
    sub_n = hops_n // RADIX
    per_device = channels_n // devices_n
    local_channels = channels_n // cols_count
    combos = orders.shape[0] * orders.shape[1]
    feat_n = templates.shape[2]
    row_at = lax.axis_index("row")
    col_at = lax.axis_index("col")
    tail_frames = from_behind(frames[:, :3], "row", -1)
    padded = jnp.concatenate([frames, tail_frames], axis=1)
    column = jnp.arange(local_channels, dtype=jnp.int32)
    channel_ids = (column // per_device * cols_count + col_at) * per_device + column % per_device
    coefficients = channel_coefficients(channels_n, channel_ids)
    summed = jnp.zeros((sensors, 2 * local_channels, hop_dev), jnp.float32)
    for quarter in range(4):
        summed = summed + jnp.einsum(
            "shf,kf->skh",
            padded[:, quarter : quarter + hop_dev],
            coefficients[:, quarter * frame_len : (quarter + 1) * frame_len],
            preferred_element_type=jnp.float32,
        )
    hop_ids = row_at * hop_dev + jnp.arange(hop_dev, dtype=jnp.int32)
    real_part, imag_part = quarter_turn(
        summed[:, :local_channels], summed[:, local_channels:], channel_ids, hop_ids
    )
    demod = jnp.stack([real_part, imag_part]).astype(jnp.bfloat16)
    swapped = lax.all_to_all(demod, "row", split_axis=2, concat_axis=3, tiled=True)
    halves = 2
    part = sensors // halves
    pieces = []
    for half in range(halves):
        ordered = swapped[:, half * part : (half + 1) * part]
        ordered = ordered.reshape(2, part, per_device, sub_n, RADIX).transpose(0, 1, 2, 4, 3)
        above = from_behind_2(ordered, ("row", "col"), -1)
        extended = jnp.concatenate([ordered, above], axis=2)
        own = ordered.astype(jnp.float32)[:, :, None]
        partner = jnp.stack(
            [
                lax.dynamic_slice_in_dim(extended, orders[wheel, order_at], per_device, axis=2)
                for wheel in range(orders.shape[0])
                for order_at in range(orders.shape[1])
            ],
            axis=2,
        ).astype(jnp.float32)
        prod_real = own[0] * partner[0] + own[1] * partner[1]
        prod_imag = own[1] * partner[0] - own[0] * partner[1]
        pieces.append(
            jnp.stack([prod_real, prod_imag])
            .astype(jnp.bfloat16)
            .reshape(2, part, combos, per_device * RADIX, sub_n)
        )
    tiles_dev = sensors * combos * RADIX
    capacity = max(2, 2 * tiles_dev // devices_n)
    owner_ids = owners[:, 0]
    targets = jnp.arange(devices_n, dtype=jnp.int32)
    one_hot = (owner_ids[:, None] == targets[None, :]).astype(jnp.int32)
    before = jnp.cumsum(one_hot, axis=0) - one_hot
    slot_ids = jnp.sum(before * one_hot, axis=1)
    places = owner_ids * capacity + slot_ids
    table_sub = sub_coefficients(sub_n)
    tiles_part = tiles_dev // halves
    outgoing = jnp.zeros((devices_n * capacity, per_device, sub_n), jnp.bfloat16)
    spectrum = None
    for half in range(halves):
        spectrum, outgoing = spectrum_call(
            pieces[half],
            table_sub,
            hops_n,
            places[half * tiles_part : (half + 1) * tiles_part],
            outgoing,
            spectrum,
            half * part * combos,
            sensors,
        )
    outgoing = outgoing.reshape(devices_n, capacity * per_device, sub_n)
    arrived = lax.all_to_all(outgoing, ("row", "col"), split_axis=0, concat_axis=0, tiled=True)
    found = jnp.dot(
        arrived.reshape(-1, sub_n), templates[0], preferred_element_type=jnp.float32
    ).astype(jnp.bfloat16)
    found = found.reshape(devices_n, capacity, per_device, feat_n)
    return (spectrum, found[None])


def solution(mesh):
    in_specs = (P(None, "row", None), P(), P(("row", "col"), None), P(("row", "col"), None, None))
    out_specs = (
        P(None, None, None, ("row", "col"), None),
        P(("row", "col"), None, None, None, None),
    )
    return jax.shard_map(shards_body, mesh=mesh, in_specs=in_specs, out_specs=out_specs, check_vma=False)
```
